32 devices in a mesh: xy: 8 (over y, x, core), gz: 4 (over z).
Axes of the slice: x: 2, y: 2, z: 4, core: 2. Of those that a mesh axis runs over, the one named last changes fastest.
Arguments:
- sections: float32 [64, 256, 256], P('xy', None, 'gz'), may hold values from -6 to 6
Outputs:
- diffused: float32 [64, 256, 256], P('gz', 'xy')
The draws below stay inside these ranges and needn't reach their ends.
All inputs are finite; a program needn't handle non-finite values.
Results may differ from the reference program's by a relative error of at most 0.0003.
Values sent between devices are 32-bit elements; how exact they have to be, the bound alone decides.
No kernel may reach another device: no remote copies, remote signals or barrier semaphores. Data moves between devices by JAX's collectives and lax.ppermute only.
A program may use at most 128 MiB of HBM per device.

```python
import math
import jax
import jax.numpy as jnp
from jax import lax

NX = 256
GRAD_REACH = 3
TENSOR_REACH = 4
SWEEPS = 4
STEPS = 3
NZ = 64
NY = 256


def levels(rng, dims, shards, least, top_value):
    gain, own = 1.0, jax.random.fold_in(rng, 6)
    for position, shards_of in shards:
        steps = jnp.exp(jax.random.uniform(jax.random.fold_in(own, position), (shards_of,), jnp.float32, least / len(shards), top_value / len(shards)))
        gain = gain * jnp.repeat(steps, dims[position] // shards_of).reshape([-1 if axis == position else 1 for axis in range(len(dims))])
    return gain


def bell_draw(stream_key, extent, scale, most, pieces=(), held_as=jnp.bfloat16):
    loudness = levels(stream_key, extent, pieces, -0.22, 0.18) if pieces else 1.0
    values = jax.random.normal(stream_key, extent, jnp.float32) * scale * loudness
    return jnp.minimum(jnp.maximum(values, -most), most).astype(held_as)


def setup_inputs(seed: int = 0) -> dict:
    keys = jax.random.split(jax.random.key(seed), 2)
    return {
        "sections": bell_draw(keys[0], (NZ, NY, NX), 1.0, 6.0, ((0, 8), (2, 4)), jnp.float32),
    }


sigma_noise = 1.0
sigma_tensor = 1.5
alpha_floor = 0.05
contrast = 0.05
time_step = 0.5
pair_list = ((0, 0), (1, 1), (2, 2), (0, 1), (0, 2), (1, 2))

def gauss_taps(sigma, reach):
    raw = [math.exp(-(t * t) / (2.0 * sigma * sigma)) for t in range(-reach, reach + 1)]
    total = sum(raw)
    return [value / total for value in raw]

def slope_taps(sigma, reach):
    base = gauss_taps(sigma, reach)
    return [t * base[t + reach] / (sigma * sigma) for t in range(-reach, reach + 1)]

def correlate(values, taps, along):
    count = values.shape[along] - len(taps) + 1
    result = taps[0] * lax.slice_in_dim(values, 0, count, axis=along)
    for index in range(1, len(taps)):
        result = result + taps[index] * lax.slice_in_dim(values, index, index + count, axis=along)
    return result

def pad_along(values, width, along):
    widths = [(0, 0), (0, 0), (0, 0)]
    widths[along] = (width, width)
    return jnp.pad(values, widths)

def pair_index(first, second):
    low, high = (min(first, second), max(first, second))
    return pair_list.index((low, high))

def diffusion_tensor(parts):
    entry = {}
    for index in range(6):
        entry[pair_list[index]] = parts[index]
    ones = jnp.ones_like(parts[0])
    zeros = jnp.zeros_like(parts[0])
    basis = [[ones if row == col else zeros for col in range(3)] for row in range(3)]
    for sweep in range(SWEEPS):
        for first, second in ((0, 1), (0, 2), (1, 2)):
            third = 3 - first - second
            offdiag = entry[first, second]
            spread = entry[second, second] - entry[first, first]
            radius = jnp.sqrt(spread * spread + 4.0 * offdiag * offdiag + 1e-30)
            sign_part = jnp.where(spread >= 0.0, 1.0, -1.0)
            tangent = sign_part * 2.0 * offdiag / (jnp.abs(spread) + radius)
            cosine = 1.0 / jnp.sqrt(1.0 + tangent * tangent)
            sine = tangent * cosine
            entry[first, first] = entry[first, first] - tangent * offdiag
            entry[second, second] = entry[second, second] + tangent * offdiag
            entry[first, second] = zeros
            key_first = (min(third, first), max(third, first))
            key_second = (min(third, second), max(third, second))
            old_first = entry[key_first]
            old_second = entry[key_second]
            entry[key_first] = cosine * old_first - sine * old_second
            entry[key_second] = sine * old_first + cosine * old_second
            for row in range(3):
                left = basis[row][first]
                right = basis[row][second]
                basis[row][first] = cosine * left - sine * right
                basis[row][second] = sine * left + cosine * right
    eigen = [entry[0, 0], entry[1, 1], entry[2, 2]]
    top = jnp.maximum(jnp.maximum(eigen[0], eigen[1]), eigen[2])
    trace = eigen[0] + eigen[1] + eigen[2]
    gains = []
    for index in range(3):
        gap = top - eigen[index]
        gains.append(alpha_floor + (1.0 - alpha_floor) * gap * gap / (gap * gap + contrast * trace * trace + 1e-30))
    result = []
    for first, second in pair_list:
        total = gains[0] * basis[first][0] * basis[second][0]
        total = total + gains[1] * basis[first][1] * basis[second][1]
        total = total + gains[2] * basis[first][2] * basis[second][2]
        result.append(total)
    return result

def offset_view(values, along, offset):
    index = []
    for dim in range(3):
        if dim == along:
            index.append(slice(1 + offset, values.shape[dim] - 1 + offset))
        else:
            index.append(slice(1, values.shape[dim] - 1))
    return values[tuple(index)]

def divergence(field, parts):
    padded = jnp.pad(field, ((0, 0), (0, 0), (2, 2)))
    wide_parts = [jnp.pad(item, ((0, 0), (0, 0), (1, 1))) for item in parts]
    slopes = [(offset_view(padded, along, 1) - offset_view(padded, along, -1)) * 0.5 for along in range(3)]
    fluxes = []
    for along in range(3):
        flux = wide_parts[pair_index(along, 0)] * slopes[0]
        flux = flux + wide_parts[pair_index(along, 1)] * slopes[1]
        flux = flux + wide_parts[pair_index(along, 2)] * slopes[2]
        fluxes.append(flux)
    total = (offset_view(fluxes[0], 0, 1) - offset_view(fluxes[0], 0, -1)) * 0.5
    total = total + (offset_view(fluxes[1], 1, 1) - offset_view(fluxes[1], 1, -1)) * 0.5
    total = total + (offset_view(fluxes[2], 2, 1) - offset_view(fluxes[2], 2, -1)) * 0.5
    return total

def plane_tensor(plane):
    return jnp.stack(diffusion_tensor([plane[index] for index in range(6)]), 0)

def reference(sections):
    smooth = gauss_taps(sigma_noise, GRAD_REACH)
    slope = slope_taps(sigma_noise, GRAD_REACH)
    wide = gauss_taps(sigma_tensor, TENSOR_REACH)
    grads = []
    for component in range(3):
        values = sections
        for along in range(3):
            taps = slope if along == component else smooth
            values = correlate(pad_along(values, GRAD_REACH, along), taps, along)
        grads.append(values)
    tensor = []
    for first, second in pair_list:
        values = grads[first] * grads[second]
        for along in range(3):
            values = correlate(pad_along(values, TENSOR_REACH, along), wide, along)
        tensor.append(values)
    stacked = jnp.stack(tensor, axis=1)
    mapped = lax.map(plane_tensor, stacked)
    parts = [mapped[:, index] for index in range(6)]
    padded_parts = [jnp.pad(item, ((1, 1), (1, 1), (0, 0))) for item in parts]
    field = sections
    for segment in range(STEPS):
        padded = jnp.pad(field, ((2, 2), (2, 2), (0, 0)))
        field = field + time_step * divergence(padded, padded_parts)
    return field
```

```python
import math

import jax
import jax.numpy as jnp
from jax import lax
from jax.sharding import PartitionSpec as P

GRAD_REACH = 3
TENSOR_REACH = 4
SWEEPS = 4
STEPS = 3


sigma_noise = 1.0
sigma_tensor = 1.5
alpha_floor = 0.05
contrast = 0.05
time_step = 0.5
pair_list = ((0, 0), (1, 1), (2, 2), (0, 1), (0, 2), (1, 2))

VOLUME_HALO = max(GRAD_REACH + TENSOR_REACH, 2 * STEPS)
TENSOR_HALO = 2 * STEPS - 1


def extended_2(block, sides, width):
    for axis, dim in sides:
        count = lax.axis_size(axis)
        forward = [(i, i + 1) for i in range(count - 1)]
        backward = [(target, source) for source, target in forward]
        low = lax.ppermute(
            lax.slice_in_dim(block, block.shape[dim] - width, None, axis=dim), axis, forward
        )
        high = lax.ppermute(lax.slice_in_dim(block, 0, width, axis=dim), axis, backward)
        block = jnp.concatenate([low, block, high], axis=dim)
    return block


def gauss_taps(sigma, reach):
    raw = [math.exp(-(t * t) / (2.0 * sigma * sigma)) for t in range(-reach, reach + 1)]
    total = sum(raw)
    return [value / total for value in raw]


def slope_taps(sigma, reach):
    base = gauss_taps(sigma, reach)
    return [t * base[t + reach] / (sigma * sigma) for t in range(-reach, reach + 1)]


def correlate(values, taps, along):
    count = values.shape[along] - len(taps) + 1
    result = taps[0] * lax.slice_in_dim(values, 0, count, axis=along)
    for index in range(1, len(taps)):
        result = result + taps[index] * lax.slice_in_dim(values, index, index + count, axis=along)
    return result


def pad_x(values, width):
    return jnp.pad(values, ((0, 0), (0, 0), (width, width)))


def pair_index(first, second):
    low, high = (min(first, second), max(first, second))
    return pair_list.index((low, high))


def diffusion_tensor(parts):
    entry = {}
    for index in range(6):
        entry[pair_list[index]] = parts[index]
    ones = jnp.ones_like(parts[0])
    zeros = jnp.zeros_like(parts[0])
    basis = [[ones if row == col else zeros for col in range(3)] for row in range(3)]
    for sweep in range(SWEEPS):
        for first, second in ((0, 1), (0, 2), (1, 2)):
            third = 3 - first - second
            offdiag = entry[first, second]
            spread = entry[second, second] - entry[first, first]
            radius = jnp.sqrt(spread * spread + 4.0 * offdiag * offdiag + 1e-30)
            sign_part = jnp.where(spread >= 0.0, 1.0, -1.0)
            tangent = sign_part * 2.0 * offdiag / (jnp.abs(spread) + radius)
            cosine = 1.0 / jnp.sqrt(1.0 + tangent * tangent)
            sine = tangent * cosine
            entry[first, first] = entry[first, first] - tangent * offdiag
            entry[second, second] = entry[second, second] + tangent * offdiag
            entry[first, second] = zeros
            key_first = (min(third, first), max(third, first))
            key_second = (min(third, second), max(third, second))
            old_first = entry[key_first]
            old_second = entry[key_second]
            entry[key_first] = cosine * old_first - sine * old_second
            entry[key_second] = sine * old_first + cosine * old_second
            for row in range(3):
                left = basis[row][first]
                right = basis[row][second]
                basis[row][first] = cosine * left - sine * right
                basis[row][second] = sine * left + cosine * right
    eigen = [entry[0, 0], entry[1, 1], entry[2, 2]]
    top = jnp.maximum(jnp.maximum(eigen[0], eigen[1]), eigen[2])
    trace = eigen[0] + eigen[1] + eigen[2]
    gains = []
    for index in range(3):
        gap = top - eigen[index]
        gains.append(
            alpha_floor
            + (1.0 - alpha_floor) * gap * gap / (gap * gap + contrast * trace * trace + 1e-30)
        )
    result = []
    for first, second in pair_list:
        total = gains[0] * basis[first][0] * basis[second][0]
        total = total + gains[1] * basis[first][1] * basis[second][1]
        total = total + gains[2] * basis[first][2] * basis[second][2]
        result.append(total)
    return result


def inside_mask(shape, z_start, y_start, z_total, y_total):
    z = lax.broadcasted_iota(jnp.int32, shape, 0) + z_start
    y = lax.broadcasted_iota(jnp.int32, shape, 1) + y_start
    return (z >= 0) & (z < z_total) & (y >= 0) & (y < y_total)


def regroup(sections, halo):
    n_xy = lax.axis_size("xy")
    n_gz = lax.axis_size("gz")
    z_in, y_total, _ = sections.shape
    y_block = y_total // n_xy
    z_total = z_in * n_xy
    z_block = z_total // n_gz
    padded = jnp.pad(sections, ((0, 0), (halo, halo), (0, 0)))
    windows = jnp.stack(
        [lax.slice_in_dim(padded, a * y_block, a * y_block + y_block + 2 * halo, axis=1) for a in range(n_xy)]
    )
    got = lax.all_to_all(windows, "xy", split_axis=0, concat_axis=0, tiled=True)
    column = got.reshape((z_total,) + got.shape[2:])
    padded = jnp.pad(column, ((halo, halo), (0, 0), (0, 0)))
    windows = jnp.stack(
        [lax.slice_in_dim(padded, b * z_block, b * z_block + z_block + 2 * halo, axis=0) for b in range(n_gz)]
    )
    got = lax.all_to_all(windows, "gz", split_axis=0, concat_axis=0, tiled=True)
    volume = jnp.transpose(got, (1, 2, 0, 3))
    return volume.reshape(volume.shape[:2] + (-1,)), z_total, y_total, z_block, y_block


def shards(sections):
    halo = VOLUME_HALO
    volume, z_total, y_total, z_block, y_block = regroup(sections, halo)
    z0 = lax.axis_index("gz") * z_block
    y0 = lax.axis_index("xy") * y_block

    smooth = gauss_taps(sigma_noise, GRAD_REACH)
    slope = slope_taps(sigma_noise, GRAD_REACH)
    wide = gauss_taps(sigma_tensor, TENSOR_REACH)

    grads = []
    for component in range(3):
        values = volume
        for along in range(2):
            taps = slope if along == component else smooth
            values = correlate(values, taps, along)
        taps = slope if component == 2 else smooth
        values = correlate(pad_x(values, GRAD_REACH), taps, 2)
        grads.append(values)
    grad_ext = halo - GRAD_REACH
    inside = inside_mask(grads[0].shape, z0 - grad_ext, y0 - grad_ext, z_total, y_total)
    tensor = []
    for first, second in pair_list:
        values = jnp.where(inside, grads[first] * grads[second], 0.0)
        values = lax.slice_in_dim(values, grad_ext - TENSOR_REACH, values.shape[0] - grad_ext + TENSOR_REACH, axis=0)
        values = lax.slice_in_dim(values, grad_ext - TENSOR_REACH, values.shape[1] - grad_ext + TENSOR_REACH, axis=1)
        values = correlate(values, wide, 0)
        values = correlate(values, wide, 1)
        values = correlate(pad_x(values, TENSOR_REACH), wide, 2)
        tensor.append(values)
    parts = diffusion_tensor(tensor)
    stacked = jnp.stack(parts)
    stacked = extended_2(stacked, (("xy", 2), ("gz", 1)), TENSOR_HALO)

    reach = 2 * STEPS
    field = volume[halo - reach : volume.shape[0] - halo + reach, halo - reach : volume.shape[1] - halo + reach]
    for segment in range(STEPS):
        ext = reach - 2 * segment
        cut = TENSOR_HALO - (ext - 1)
        local = [
            stacked[index, cut : stacked.shape[1] - cut, cut : stacked.shape[2] - cut]
            for index in range(6)
        ]
        wide_field = pad_x(field, 1)
        slopes = [
            (wide_field[2:, 1:-1, 1:-1] - wide_field[:-2, 1:-1, 1:-1]) * 0.5,
            (wide_field[1:-1, 2:, 1:-1] - wide_field[1:-1, :-2, 1:-1]) * 0.5,
            (wide_field[1:-1, 1:-1, 2:] - wide_field[1:-1, 1:-1, :-2]) * 0.5,
        ]
        fluxes = []
        for along in range(3):
            flux = local[pair_index(along, 0)] * slopes[0]
            flux = flux + local[pair_index(along, 1)] * slopes[1]
            flux = flux + local[pair_index(along, 2)] * slopes[2]
            fluxes.append(flux)
        flux_x = pad_x(fluxes[2], 1)
        total = (fluxes[0][2:, 1:-1] - fluxes[0][:-2, 1:-1]) * 0.5
        total = total + (fluxes[1][1:-1, 2:] - fluxes[1][1:-1, :-2]) * 0.5
        total = total + (flux_x[1:-1, 1:-1, 2:] - flux_x[1:-1, 1:-1, :-2]) * 0.5
        field = field[2:-2, 2:-2] + time_step * total
        if segment < STEPS - 1:
            new_ext = ext - 2
            inside = inside_mask(field.shape, z0 - new_ext, y0 - new_ext, z_total, y_total)
            field = jnp.where(inside, field, 0.0)
    return field


def solution(mesh):
    in_specs = (P("xy", None, "gz"),)
    out_specs = P("gz", "xy", None)
    return jax.shard_map(shards, mesh=mesh, in_specs=in_specs, out_specs=out_specs, check_vma=False)
```

```python
import math

import jax
import jax.numpy as jnp
from jax import lax
from jax.sharding import PartitionSpec as P

GRAD_REACH = 3
TENSOR_REACH = 4
SWEEPS = 4
STEPS = 3


sigma_noise = 1.0
sigma_tensor = 1.5
alpha_floor = 0.05
contrast = 0.05
time_step = 0.5
pair_list = ((0, 0), (1, 1), (2, 2), (0, 1), (0, 2), (1, 2))

VOLUME_HALO = max(GRAD_REACH + TENSOR_REACH, 2 * STEPS)
TENSOR_HALO = 2 * STEPS - 1


def extended_2(block, sides, width):
    for axis, dim in sides:
        count = lax.axis_size(axis)
        forward = [(i, i + 1) for i in range(count - 1)]
        backward = [(target, source) for source, target in forward]
        low = lax.ppermute(
            lax.slice_in_dim(block, block.shape[dim] - width, None, axis=dim), axis, forward
        )
        high = lax.ppermute(lax.slice_in_dim(block, 0, width, axis=dim), axis, backward)
        block = jnp.concatenate([low, block, high], axis=dim)
    return block


def gauss_taps(sigma, reach):
    raw = [math.exp(-(t * t) / (2.0 * sigma * sigma)) for t in range(-reach, reach + 1)]
    total = sum(raw)
    return [value / total for value in raw]


def slope_taps(sigma, reach):
    base = gauss_taps(sigma, reach)
    return [t * base[t + reach] / (sigma * sigma) for t in range(-reach, reach + 1)]


def correlate(values, taps, along):
    count = values.shape[along] - len(taps) + 1
    result = taps[0] * lax.slice_in_dim(values, 0, count, axis=along)
    for index in range(1, len(taps)):
        result = result + taps[index] * lax.slice_in_dim(values, index, index + count, axis=along)
    return result


def pad_x(values, width):
    return jnp.pad(values, ((0, 0), (0, 0), (width, width)))


def pair_index(first, second):
    low, high = (min(first, second), max(first, second))
    return pair_list.index((low, high))


def diffusion_tensor(parts):
    entry = {}
    for index in range(6):
        entry[pair_list[index]] = parts[index]
    ones = jnp.ones_like(parts[0])
    zeros = jnp.zeros_like(parts[0])
    basis = [[ones if row == col else zeros for col in range(3)] for row in range(3)]
    for sweep in range(SWEEPS):
        for first, second in ((0, 1), (0, 2), (1, 2)):
            third = 3 - first - second
            offdiag = entry[first, second]
            spread = entry[second, second] - entry[first, first]
            radius = jnp.sqrt(spread * spread + 4.0 * offdiag * offdiag + 1e-30)
            sign_part = jnp.where(spread >= 0.0, 1.0, -1.0)
            tangent = sign_part * 2.0 * offdiag / (jnp.abs(spread) + radius)
            cosine = 1.0 / jnp.sqrt(1.0 + tangent * tangent)
            sine = tangent * cosine
            entry[first, first] = entry[first, first] - tangent * offdiag
            entry[second, second] = entry[second, second] + tangent * offdiag
            entry[first, second] = zeros
            key_first = (min(third, first), max(third, first))
            key_second = (min(third, second), max(third, second))
            old_first = entry[key_first]
            old_second = entry[key_second]
            entry[key_first] = cosine * old_first - sine * old_second
            entry[key_second] = sine * old_first + cosine * old_second
            for row in range(3):
                left = basis[row][first]
                right = basis[row][second]
                basis[row][first] = cosine * left - sine * right
                basis[row][second] = sine * left + cosine * right
    eigen = [entry[0, 0], entry[1, 1], entry[2, 2]]
    top = jnp.maximum(jnp.maximum(eigen[0], eigen[1]), eigen[2])
    trace = eigen[0] + eigen[1] + eigen[2]
    gains = []
    for index in range(3):
        gap = top - eigen[index]
        gains.append(
            alpha_floor
            + (1.0 - alpha_floor) * gap * gap / (gap * gap + contrast * trace * trace + 1e-30)
        )
    result = []
    for first, second in pair_list:
        total = gains[0] * basis[first][0] * basis[second][0]
        total = total + gains[1] * basis[first][1] * basis[second][1]
        total = total + gains[2] * basis[first][2] * basis[second][2]
        result.append(total)
    return result


def inside_mask(shape, y_start, x_start, y_total, x_total):
    y = lax.broadcasted_iota(jnp.int32, shape, 1) + y_start
    x = lax.broadcasted_iota(jnp.int32, shape, 2) + x_start
    return (y >= 0) & (y < y_total) & (x >= 0) & (x < x_total)


def pad_z(values, width):
    return jnp.pad(values, ((width, width), (0, 0), (0, 0)))


def regroup(sections, halo):
    n_xy = lax.axis_size("xy")
    z_in, y_total, _ = sections.shape
    y_block = y_total // n_xy
    padded = jnp.pad(sections, ((0, 0), (halo, halo), (0, 0)))
    windows = jnp.stack(
        [lax.slice_in_dim(padded, a * y_block, a * y_block + y_block + 2 * halo, axis=1) for a in range(n_xy)]
    )
    got = lax.all_to_all(windows, "xy", split_axis=0, concat_axis=0, tiled=True)
    column = got.reshape((z_in * n_xy,) + got.shape[2:])
    return extended_2(column, (("gz", 2),), halo), y_total, y_block


def shards(sections):
    halo = VOLUME_HALO
    x_block = sections.shape[2]
    x_total = x_block * lax.axis_size("gz")
    volume, y_total, y_block = regroup(sections, halo)
    y0 = lax.axis_index("xy") * y_block
    x0 = lax.axis_index("gz") * x_block

    smooth = gauss_taps(sigma_noise, GRAD_REACH)
    slope = slope_taps(sigma_noise, GRAD_REACH)
    wide = gauss_taps(sigma_tensor, TENSOR_REACH)

    grads = []
    for component in range(3):
        values = volume
        for along in range(3):
            taps = slope if along == component else smooth
            if along == 0:
                values = pad_z(values, GRAD_REACH)
            values = correlate(values, taps, along)
        grads.append(values)
    grad_ext = halo - GRAD_REACH
    inside = inside_mask(grads[0].shape, y0 - grad_ext, x0 - grad_ext, y_total, x_total)
    tensor = []
    for first, second in pair_list:
        values = jnp.where(inside, grads[first] * grads[second], 0.0)
        for along in (1, 2):
            values = lax.slice_in_dim(
                values, grad_ext - TENSOR_REACH, values.shape[along] - grad_ext + TENSOR_REACH, axis=along
            )
        values = correlate(pad_z(values, TENSOR_REACH), wide, 0)
        values = correlate(values, wide, 1)
        values = correlate(values, wide, 2)
        tensor.append(values)
    parts = diffusion_tensor(tensor)
    stacked = jnp.stack(parts)
    stacked = extended_2(stacked, (("xy", 2), ("gz", 3)), TENSOR_HALO)

    reach = 2 * STEPS
    field = volume[:, halo - reach : volume.shape[1] - halo + reach, halo - reach : volume.shape[2] - halo + reach]
    for segment in range(STEPS):
        ext = reach - 2 * segment
        cut = TENSOR_HALO - (ext - 1)
        local = [
            stacked[index, :, cut : stacked.shape[2] - cut, cut : stacked.shape[3] - cut]
            for index in range(6)
        ]
        tall = pad_z(field, 1)
        slopes = [
            (tall[2:, 1:-1, 1:-1] - tall[:-2, 1:-1, 1:-1]) * 0.5,
            (field[:, 2:, 1:-1] - field[:, :-2, 1:-1]) * 0.5,
            (field[:, 1:-1, 2:] - field[:, 1:-1, :-2]) * 0.5,
        ]
        fluxes = []
        for along in range(3):
            flux = local[pair_index(along, 0)] * slopes[0]
            flux = flux + local[pair_index(along, 1)] * slopes[1]
            flux = flux + local[pair_index(along, 2)] * slopes[2]
            fluxes.append(flux)
        flux_z = pad_z(fluxes[0], 1)
        total = (flux_z[2:, 1:-1, 1:-1] - flux_z[:-2, 1:-1, 1:-1]) * 0.5
        total = total + (fluxes[1][:, 2:, 1:-1] - fluxes[1][:, :-2, 1:-1]) * 0.5
        total = total + (fluxes[2][:, 1:-1, 2:] - fluxes[2][:, 1:-1, :-2]) * 0.5
        field = field[:, 2:-2, 2:-2] + time_step * total
        if segment < STEPS - 1:
            new_ext = ext - 2
            inside = inside_mask(field.shape, y0 - new_ext, x0 - new_ext, y_total, x_total)
            field = jnp.where(inside, field, 0.0)
    return lax.all_to_all(field, "gz", split_axis=0, concat_axis=2, tiled=True)


def solution(mesh):
    in_specs = (P("xy", None, "gz"),)
    out_specs = P("gz", "xy", None)
    return jax.shard_map(shards, mesh=mesh, in_specs=in_specs, out_specs=out_specs, check_vma=False)
```

```python
import math

import jax
import jax.numpy as jnp
from jax import lax
from jax.sharding import PartitionSpec as P

GRAD_REACH = 3
TENSOR_REACH = 4
SWEEPS = 4
STEPS = 3


sigma_noise = 1.0
sigma_tensor = 1.5
alpha_floor = 0.05
contrast = 0.05
time_step = 0.5
pair_list = ((0, 0), (1, 1), (2, 2), (0, 1), (0, 2), (1, 2))

VOLUME_HALO = max(GRAD_REACH + TENSOR_REACH, 2 * STEPS)
TENSOR_HALO = 2 * STEPS - 1


def extended_2(block, sides, width):
    for axis, dim in sides:
        count = lax.axis_size(axis)
        forward = [(i, i + 1) for i in range(count - 1)]
        backward = [(target, source) for source, target in forward]
        low = lax.ppermute(
            lax.slice_in_dim(block, block.shape[dim] - width, None, axis=dim), axis, forward
        )
        high = lax.ppermute(lax.slice_in_dim(block, 0, width, axis=dim), axis, backward)
        block = jnp.concatenate([low, block, high], axis=dim)
    return block


def gauss_taps(sigma, reach):
    raw = [math.exp(-(t * t) / (2.0 * sigma * sigma)) for t in range(-reach, reach + 1)]
    total = sum(raw)
    return [value / total for value in raw]


def slope_taps(sigma, reach):
    base = gauss_taps(sigma, reach)
    return [t * base[t + reach] / (sigma * sigma) for t in range(-reach, reach + 1)]


def correlate(values, taps, along):
    count = values.shape[along] - len(taps) + 1
    result = taps[0] * lax.slice_in_dim(values, 0, count, axis=along)
    for index in range(1, len(taps)):
        result = result + taps[index] * lax.slice_in_dim(values, index, index + count, axis=along)
    return result


def pad_x(values, width):
    return jnp.pad(values, ((0, 0), (0, 0), (width, width)))


def pair_index(first, second):
    low, high = (min(first, second), max(first, second))
    return pair_list.index((low, high))


def diffusion_tensor(parts):
    entry = {}
    for index in range(6):
        entry[pair_list[index]] = parts[index]
    ones = jnp.ones_like(parts[0])
    zeros = jnp.zeros_like(parts[0])
    basis = [[ones if row == col else zeros for col in range(3)] for row in range(3)]
    for sweep in range(SWEEPS):
        for first, second in ((0, 1), (0, 2), (1, 2)):
            third = 3 - first - second
            offdiag = entry[first, second]
            spread = entry[second, second] - entry[first, first]
            radius = jnp.sqrt(spread * spread + 4.0 * offdiag * offdiag + 1e-30)
            sign_part = jnp.where(spread >= 0.0, 1.0, -1.0)
            tangent = sign_part * 2.0 * offdiag / (jnp.abs(spread) + radius)
            cosine = 1.0 / jnp.sqrt(1.0 + tangent * tangent)
            sine = tangent * cosine
            entry[first, first] = entry[first, first] - tangent * offdiag
            entry[second, second] = entry[second, second] + tangent * offdiag
            entry[first, second] = zeros
            key_first = (min(third, first), max(third, first))
            key_second = (min(third, second), max(third, second))
            old_first = entry[key_first]
            old_second = entry[key_second]
            entry[key_first] = cosine * old_first - sine * old_second
            entry[key_second] = sine * old_first + cosine * old_second
            for row in range(3):
                left = basis[row][first]
                right = basis[row][second]
                basis[row][first] = cosine * left - sine * right
                basis[row][second] = sine * left + cosine * right
    eigen = [entry[0, 0], entry[1, 1], entry[2, 2]]
    top = jnp.maximum(jnp.maximum(eigen[0], eigen[1]), eigen[2])
    trace = eigen[0] + eigen[1] + eigen[2]
    gains = []
    for index in range(3):
        gap = top - eigen[index]
        gains.append(
            alpha_floor
            + (1.0 - alpha_floor) * gap * gap / (gap * gap + contrast * trace * trace + 1e-30)
        )
    result = []
    for first, second in pair_list:
        total = gains[0] * basis[first][0] * basis[second][0]
        total = total + gains[1] * basis[first][1] * basis[second][1]
        total = total + gains[2] * basis[first][2] * basis[second][2]
        result.append(total)
    return result


def inside_mask(shape, z_start, y_start, z_total, y_total):
    z = lax.broadcasted_iota(jnp.int32, shape, 0) + z_start
    y = lax.broadcasted_iota(jnp.int32, shape, 1) + y_start
    return (z >= 0) & (z < z_total) & (y >= 0) & (y < y_total)


def regroup(sections, halo):
    n_gz = lax.axis_size("gz")
    column = lax.all_to_all(sections, "xy", split_axis=1, concat_axis=0, tiled=True)
    z_total, y_block, _ = column.shape
    y_total = y_block * lax.axis_size("xy")
    z_block = z_total // n_gz
    padded = jnp.pad(column, ((halo, halo), (0, 0), (0, 0)))
    windows = jnp.stack(
        [lax.slice_in_dim(padded, b * z_block, b * z_block + z_block + 2 * halo, axis=0) for b in range(n_gz)]
    )
    got = lax.all_to_all(windows, "gz", split_axis=0, concat_axis=0, tiled=True)
    volume = jnp.transpose(got, (1, 2, 0, 3))
    volume = volume.reshape(volume.shape[:2] + (-1,))
    volume = extended_2(volume, (("xy", 1),), halo)
    return lax.optimization_barrier(volume), z_total, y_total, z_block, y_block


def shards(sections):
    halo = VOLUME_HALO
    volume, z_total, y_total, z_block, y_block = regroup(sections, halo)
    z0 = lax.axis_index("gz") * z_block
    y0 = lax.axis_index("xy") * y_block

    smooth = gauss_taps(sigma_noise, GRAD_REACH)
    slope = slope_taps(sigma_noise, GRAD_REACH)
    wide = gauss_taps(sigma_tensor, TENSOR_REACH)

    grads = []
    for component in range(3):
        values = volume
        for along in range(2):
            taps = slope if along == component else smooth
            values = correlate(values, taps, along)
        taps = slope if component == 2 else smooth
        values = correlate(pad_x(values, GRAD_REACH), taps, 2)
        grads.append(values)
    grad_ext = halo - GRAD_REACH
    inside = inside_mask(grads[0].shape, z0 - grad_ext, y0 - grad_ext, z_total, y_total)
    tensor = []
    for first, second in pair_list:
        values = jnp.where(inside, grads[first] * grads[second], 0.0)
        values = lax.slice_in_dim(values, grad_ext - TENSOR_REACH, values.shape[0] - grad_ext + TENSOR_REACH, axis=0)
        values = lax.slice_in_dim(values, grad_ext - TENSOR_REACH, values.shape[1] - grad_ext + TENSOR_REACH, axis=1)
        values = correlate(values, wide, 0)
        values = correlate(values, wide, 1)
        values = correlate(pad_x(values, TENSOR_REACH), wide, 2)
        tensor.append(values)
    parts = diffusion_tensor(tensor)
    stacked = jnp.stack(parts)
    stacked = extended_2(stacked, (("gz", 1), ("xy", 2)), TENSOR_HALO)

    reach = 2 * STEPS
    field = volume[halo - reach : volume.shape[0] - halo + reach, halo - reach : volume.shape[1] - halo + reach]
    for segment in range(STEPS):
        ext = reach - 2 * segment
        cut = TENSOR_HALO - (ext - 1)
        local = [
            stacked[index, cut : stacked.shape[1] - cut, cut : stacked.shape[2] - cut]
            for index in range(6)
        ]
        wide_field = pad_x(field, 1)
        slopes = [
            (wide_field[2:, 1:-1, 1:-1] - wide_field[:-2, 1:-1, 1:-1]) * 0.5,
            (wide_field[1:-1, 2:, 1:-1] - wide_field[1:-1, :-2, 1:-1]) * 0.5,
            (wide_field[1:-1, 1:-1, 2:] - wide_field[1:-1, 1:-1, :-2]) * 0.5,
        ]
        fluxes = []
        for along in range(3):
            flux = local[pair_index(along, 0)] * slopes[0]
            flux = flux + local[pair_index(along, 1)] * slopes[1]
            flux = flux + local[pair_index(along, 2)] * slopes[2]
            fluxes.append(flux)
        flux_x = pad_x(fluxes[2], 1)
        total = (fluxes[0][2:, 1:-1] - fluxes[0][:-2, 1:-1]) * 0.5
        total = total + (fluxes[1][1:-1, 2:] - fluxes[1][1:-1, :-2]) * 0.5
        total = total + (flux_x[1:-1, 1:-1, 2:] - flux_x[1:-1, 1:-1, :-2]) * 0.5
        field = field[2:-2, 2:-2] + time_step * total
        if segment < STEPS - 1:
            new_ext = ext - 2
            inside = inside_mask(field.shape, z0 - new_ext, y0 - new_ext, z_total, y_total)
            field = jnp.where(inside, field, 0.0)
    return field


def solution(mesh):
    in_specs = (P("xy", None, "gz"),)
    out_specs = P("gz", "xy", None)
    return jax.shard_map(shards, mesh=mesh, in_specs=in_specs, out_specs=out_specs, check_vma=False)
```

```python
import math

import jax
import jax.numpy as jnp
from jax import lax
from jax.sharding import PartitionSpec as P

GRAD_REACH = 3
TENSOR_REACH = 4
SWEEPS = 4
STEPS = 3


sigma_noise = 1.0
sigma_tensor = 1.5
alpha_floor = 0.05
contrast = 0.05
time_step = 0.5
pair_list = ((0, 0), (1, 1), (2, 2), (0, 1), (0, 2), (1, 2))

VOLUME_HALO = max(GRAD_REACH + TENSOR_REACH, 2 * STEPS)
TENSOR_HALO = 2 * STEPS - 1


def extended_2(block, sides, width):
    for axis, dim in sides:
        count = lax.axis_size(axis)
        forward = [(i, i + 1) for i in range(count - 1)]
        backward = [(target, source) for source, target in forward]
        low = lax.ppermute(
            lax.slice_in_dim(block, block.shape[dim] - width, None, axis=dim), axis, forward
        )
        high = lax.ppermute(lax.slice_in_dim(block, 0, width, axis=dim), axis, backward)
        block = jnp.concatenate([low, block, high], axis=dim)
    return block


def gauss_taps(sigma, reach):
    raw = [math.exp(-(t * t) / (2.0 * sigma * sigma)) for t in range(-reach, reach + 1)]
    total = sum(raw)
    return [value / total for value in raw]


def slope_taps(sigma, reach):
    base = gauss_taps(sigma, reach)
    return [t * base[t + reach] / (sigma * sigma) for t in range(-reach, reach + 1)]


def correlate(values, taps, along):
    count = values.shape[along] - len(taps) + 1
    result = taps[0] * lax.slice_in_dim(values, 0, count, axis=along)
    for index in range(1, len(taps)):
        result = result + taps[index] * lax.slice_in_dim(values, index, index + count, axis=along)
    return result


def pad_x(values, width):
    return jnp.pad(values, ((0, 0), (0, 0), (width, width)))


def pair_index(first, second):
    low, high = (min(first, second), max(first, second))
    return pair_list.index((low, high))


def diffusion_tensor(parts):
    entry = {}
    for index in range(6):
        entry[pair_list[index]] = parts[index]
    ones = jnp.ones_like(parts[0])
    zeros = jnp.zeros_like(parts[0])
    basis = [[ones if row == col else zeros for col in range(3)] for row in range(3)]
    for sweep in range(SWEEPS):
        for first, second in ((0, 1), (0, 2), (1, 2)):
            third = 3 - first - second
            offdiag = entry[first, second]
            spread = entry[second, second] - entry[first, first]
            radius = jnp.sqrt(spread * spread + 4.0 * offdiag * offdiag + 1e-30)
            sign_part = jnp.where(spread >= 0.0, 1.0, -1.0)
            tangent = sign_part * 2.0 * offdiag / (jnp.abs(spread) + radius)
            cosine = 1.0 / jnp.sqrt(1.0 + tangent * tangent)
            sine = tangent * cosine
            entry[first, first] = entry[first, first] - tangent * offdiag
            entry[second, second] = entry[second, second] + tangent * offdiag
            entry[first, second] = zeros
            key_first = (min(third, first), max(third, first))
            key_second = (min(third, second), max(third, second))
            old_first = entry[key_first]
            old_second = entry[key_second]
            entry[key_first] = cosine * old_first - sine * old_second
            entry[key_second] = sine * old_first + cosine * old_second
            for row in range(3):
                left = basis[row][first]
                right = basis[row][second]
                basis[row][first] = cosine * left - sine * right
                basis[row][second] = sine * left + cosine * right
    eigen = [entry[0, 0], entry[1, 1], entry[2, 2]]
    top = jnp.maximum(jnp.maximum(eigen[0], eigen[1]), eigen[2])
    trace = eigen[0] + eigen[1] + eigen[2]
    gains = []
    for index in range(3):
        gap = top - eigen[index]
        gains.append(
            alpha_floor
            + (1.0 - alpha_floor) * gap * gap / (gap * gap + contrast * trace * trace + 1e-30)
        )
    result = []
    for first, second in pair_list:
        total = gains[0] * basis[first][0] * basis[second][0]
        total = total + gains[1] * basis[first][1] * basis[second][1]
        total = total + gains[2] * basis[first][2] * basis[second][2]
        result.append(total)
    return result


def inside_mask(shape, z_start, y_start, z_total, y_total):
    z = lax.broadcasted_iota(jnp.int32, shape, 0) + z_start
    y = lax.broadcasted_iota(jnp.int32, shape, 1) + y_start
    return (z >= 0) & (z < z_total) & (y >= 0) & (y < y_total)


def regroup(sections, halo):
    n_gz = lax.axis_size("gz")
    column = lax.all_to_all(sections, "xy", split_axis=1, concat_axis=0, tiled=True)
    z_total, y_block, _ = column.shape
    y_total = y_block * lax.axis_size("xy")
    z_block = z_total // n_gz
    padded = jnp.pad(column, ((halo, halo), (0, 0), (0, 0)))
    windows = jnp.stack(
        [lax.slice_in_dim(padded, b * z_block, b * z_block + z_block + 2 * halo, axis=0) for b in range(n_gz)]
    )
    got = lax.all_to_all(windows, "gz", split_axis=0, concat_axis=0, tiled=True)
    volume = jnp.transpose(got, (1, 2, 0, 3))
    volume = volume.reshape(volume.shape[:2] + (-1,))
    volume = extended_2(volume, (("xy", 1),), halo)
    return lax.optimization_barrier(volume), z_total, y_total, z_block, y_block


def tensor_rim(tensor, z_block):
    width = TENSOR_HALO
    if z_block < 2 * width + 1:
        stacked = jnp.stack(diffusion_tensor(tensor))
        return extended_2(stacked, (("gz", 1), ("xy", 2)), width)
    count = lax.axis_size("gz")
    forward = [(i, i + 1) for i in range(count - 1)]
    backward = [(target, source) for source, target in forward]
    edges = [jnp.concatenate([item[:width], item[z_block - width :]], axis=0) for item in tensor]
    middle = [item[width : z_block - width] for item in tensor]
    edge_parts = jnp.stack(diffusion_tensor(edges))
    top, bottom = lax.optimization_barrier((edge_parts[:, width:], edge_parts[:, :width]))
    low = lax.ppermute(top, "gz", forward)
    high = lax.ppermute(bottom, "gz", backward)
    middle_parts = jnp.stack(diffusion_tensor(middle))
    stacked = jnp.concatenate(
        [low, edge_parts[:, :width], middle_parts, edge_parts[:, width:], high], axis=1
    )
    return extended_2(stacked, (("xy", 2),), width)


def shards(sections):
    halo = VOLUME_HALO
    volume, z_total, y_total, z_block, y_block = regroup(sections, halo)
    z0 = lax.axis_index("gz") * z_block
    y0 = lax.axis_index("xy") * y_block

    smooth = gauss_taps(sigma_noise, GRAD_REACH)
    slope = slope_taps(sigma_noise, GRAD_REACH)
    wide = gauss_taps(sigma_tensor, TENSOR_REACH)

    grads = []
    for component in range(3):
        values = volume
        for along in range(2):
            taps = slope if along == component else smooth
            values = correlate(values, taps, along)
        taps = slope if component == 2 else smooth
        values = correlate(pad_x(values, GRAD_REACH), taps, 2)
        grads.append(values)
    grad_ext = halo - GRAD_REACH
    inside = inside_mask(grads[0].shape, z0 - grad_ext, y0 - grad_ext, z_total, y_total)
    tensor = []
    for first, second in pair_list:
        values = jnp.where(inside, grads[first] * grads[second], 0.0)
        values = lax.slice_in_dim(values, grad_ext - TENSOR_REACH, values.shape[0] - grad_ext + TENSOR_REACH, axis=0)
        values = lax.slice_in_dim(values, grad_ext - TENSOR_REACH, values.shape[1] - grad_ext + TENSOR_REACH, axis=1)
        values = correlate(values, wide, 0)
        values = correlate(values, wide, 1)
        values = correlate(pad_x(values, TENSOR_REACH), wide, 2)
        tensor.append(values)
    stacked = tensor_rim(tensor, z_block)

    reach = 2 * STEPS
    field = volume[halo - reach : volume.shape[0] - halo + reach, halo - reach : volume.shape[1] - halo + reach]
    for segment in range(STEPS):
        ext = reach - 2 * segment
        cut = TENSOR_HALO - (ext - 1)
        local = [
            stacked[index, cut : stacked.shape[1] - cut, cut : stacked.shape[2] - cut]
            for index in range(6)
        ]
        wide_field = pad_x(field, 1)
        slopes = [
            (wide_field[2:, 1:-1, 1:-1] - wide_field[:-2, 1:-1, 1:-1]) * 0.5,
            (wide_field[1:-1, 2:, 1:-1] - wide_field[1:-1, :-2, 1:-1]) * 0.5,
            (wide_field[1:-1, 1:-1, 2:] - wide_field[1:-1, 1:-1, :-2]) * 0.5,
        ]
        fluxes = []
        for along in range(3):
            flux = local[pair_index(along, 0)] * slopes[0]
            flux = flux + local[pair_index(along, 1)] * slopes[1]
            flux = flux + local[pair_index(along, 2)] * slopes[2]
            fluxes.append(flux)
        flux_x = pad_x(fluxes[2], 1)
        total = (fluxes[0][2:, 1:-1] - fluxes[0][:-2, 1:-1]) * 0.5
        total = total + (fluxes[1][1:-1, 2:] - fluxes[1][1:-1, :-2]) * 0.5
        total = total + (flux_x[1:-1, 1:-1, 2:] - flux_x[1:-1, 1:-1, :-2]) * 0.5
        field = field[2:-2, 2:-2] + time_step * total
        if segment < STEPS - 1:
            new_ext = ext - 2
            inside = inside_mask(field.shape, z0 - new_ext, y0 - new_ext, z_total, y_total)
            field = jnp.where(inside, field, 0.0)
    return field


def solution(mesh):
    in_specs = (P("xy", None, "gz"),)
    out_specs = P("gz", "xy", None)
    return jax.shard_map(shards, mesh=mesh, in_specs=in_specs, out_specs=out_specs, check_vma=False)
```

```python
import math

import jax
import jax.numpy as jnp
from jax import lax
from jax.sharding import PartitionSpec as P

GRAD_REACH = 3
TENSOR_REACH = 4
SWEEPS = 4
STEPS = 3


sigma_noise = 1.0
sigma_tensor = 1.5
alpha_floor = 0.05
contrast = 0.05
time_step = 0.5
pair_list = ((0, 0), (1, 1), (2, 2), (0, 1), (0, 2), (1, 2))

VOLUME_HALO = max(GRAD_REACH + TENSOR_REACH, 2 * STEPS)
TENSOR_HALO = 2 * STEPS - 1


def extended_2(block, sides, width):
    for axis, dim in sides:
        count = lax.axis_size(axis)
        forward = [(i, i + 1) for i in range(count - 1)]
        backward = [(target, source) for source, target in forward]
        low = lax.ppermute(
            lax.slice_in_dim(block, block.shape[dim] - width, None, axis=dim), axis, forward
        )
        high = lax.ppermute(lax.slice_in_dim(block, 0, width, axis=dim), axis, backward)
        block = jnp.concatenate([low, block, high], axis=dim)
    return block


def gauss_taps(sigma, reach):
    raw = [math.exp(-(t * t) / (2.0 * sigma * sigma)) for t in range(-reach, reach + 1)]
    total = sum(raw)
    return [value / total for value in raw]


def slope_taps(sigma, reach):
    base = gauss_taps(sigma, reach)
    return [t * base[t + reach] / (sigma * sigma) for t in range(-reach, reach + 1)]


def correlate(values, taps, along):
    count = values.shape[along] - len(taps) + 1
    result = taps[0] * lax.slice_in_dim(values, 0, count, axis=along)
    for index in range(1, len(taps)):
        result = result + taps[index] * lax.slice_in_dim(values, index, index + count, axis=along)
    return result


def pad_x(values, width):
    return jnp.pad(values, ((0, 0), (0, 0), (width, width)))


def pair_index(first, second):
    low, high = (min(first, second), max(first, second))
    return pair_list.index((low, high))


def diffusion_tensor(parts):
    entry = {}
    for index in range(6):
        entry[pair_list[index]] = parts[index]
    ones = jnp.ones_like(parts[0])
    zeros = jnp.zeros_like(parts[0])
    basis = [[ones if row == col else zeros for col in range(3)] for row in range(3)]
    for sweep in range(SWEEPS):
        for first, second in ((0, 1), (0, 2), (1, 2)):
            third = 3 - first - second
            offdiag = entry[first, second]
            spread = entry[second, second] - entry[first, first]
            radius = jnp.sqrt(spread * spread + 4.0 * offdiag * offdiag + 1e-30)
            sign_part = jnp.where(spread >= 0.0, 1.0, -1.0)
            tangent = sign_part * 2.0 * offdiag / (jnp.abs(spread) + radius)
            cosine = 1.0 / jnp.sqrt(1.0 + tangent * tangent)
            sine = tangent * cosine
            entry[first, first] = entry[first, first] - tangent * offdiag
            entry[second, second] = entry[second, second] + tangent * offdiag
            entry[first, second] = zeros
            key_first = (min(third, first), max(third, first))
            key_second = (min(third, second), max(third, second))
            old_first = entry[key_first]
            old_second = entry[key_second]
            entry[key_first] = cosine * old_first - sine * old_second
            entry[key_second] = sine * old_first + cosine * old_second
            for row in range(3):
                left = basis[row][first]
                right = basis[row][second]
                basis[row][first] = cosine * left - sine * right
                basis[row][second] = sine * left + cosine * right
    eigen = [entry[0, 0], entry[1, 1], entry[2, 2]]
    top = jnp.maximum(jnp.maximum(eigen[0], eigen[1]), eigen[2])
    trace = eigen[0] + eigen[1] + eigen[2]
    gains = []
    for index in range(3):
        gap = top - eigen[index]
        gains.append(
            alpha_floor
            + (1.0 - alpha_floor) * gap * gap / (gap * gap + contrast * trace * trace + 1e-30)
        )
    result = []
    for first, second in pair_list:
        total = gains[0] * basis[first][0] * basis[second][0]
        total = total + gains[1] * basis[first][1] * basis[second][1]
        total = total + gains[2] * basis[first][2] * basis[second][2]
        result.append(total)
    return result


def inside_mask(shape, z_start, y_start, z_total, y_total):
    z = lax.broadcasted_iota(jnp.int32, shape, 0) + z_start
    y = lax.broadcasted_iota(jnp.int32, shape, 1) + y_start
    return (z >= 0) & (z < z_total) & (y >= 0) & (y < y_total)


def regroup(sections, halo):
    n_gz = lax.axis_size("gz")
    column = lax.all_to_all(sections, "xy", split_axis=1, concat_axis=0, tiled=True)
    z_total, y_block, _ = column.shape
    y_total = y_block * lax.axis_size("xy")
    z_block = z_total // n_gz
    padded = jnp.pad(column, ((halo, halo), (0, 0), (0, 0)))
    windows = jnp.stack(
        [lax.slice_in_dim(padded, b * z_block, b * z_block + z_block + 2 * halo, axis=0) for b in range(n_gz)]
    )
    got = lax.all_to_all(windows, "gz", split_axis=0, concat_axis=0, tiled=True)
    volume = jnp.transpose(got, (1, 2, 0, 3))
    volume = volume.reshape(volume.shape[:2] + (-1,))
    volume = extended_2(volume, (("xy", 1),), halo)
    return lax.optimization_barrier(volume), z_total, y_total, z_block, y_block


def surround(block, width):
    n_xy = lax.axis_size("xy")
    n_gz = lax.axis_size("gz")
    z_block, y_block = block.shape[1], block.shape[2]
    edge_z = {-1: slice(z_block - width, None), 0: slice(None), 1: slice(0, width)}
    edge_y = {-1: slice(y_block - width, None), 0: slice(None), 1: slice(0, width)}
    pieces = {}
    for dz in (-1, 0, 1):
        for dy in (-1, 0, 1):
            if dz == 0 and dy == 0:
                pieces[dz, dy] = block
                continue
            part = block[:, edge_z[dz], edge_y[dy]]
            pairs = []
            for a in range(n_xy):
                for b in range(n_gz):
                    if 0 <= a + dy < n_xy and 0 <= b + dz < n_gz:
                        pairs.append(((a + dy) * n_gz + (b + dz), a * n_gz + b))
            pieces[dz, dy] = lax.ppermute(part, ("xy", "gz"), pairs)
    rows = [jnp.concatenate([pieces[dz, dy] for dy in (-1, 0, 1)], axis=2) for dz in (-1, 0, 1)]
    return jnp.concatenate(rows, axis=1)


def shards(sections):
    halo = VOLUME_HALO
    volume, z_total, y_total, z_block, y_block = regroup(sections, halo)
    z0 = lax.axis_index("gz") * z_block
    y0 = lax.axis_index("xy") * y_block

    smooth = gauss_taps(sigma_noise, GRAD_REACH)
    slope = slope_taps(sigma_noise, GRAD_REACH)
    wide = gauss_taps(sigma_tensor, TENSOR_REACH)

    grads = []
    for component in range(3):
        values = volume
        for along in range(2):
            taps = slope if along == component else smooth
            values = correlate(values, taps, along)
        taps = slope if component == 2 else smooth
        values = correlate(pad_x(values, GRAD_REACH), taps, 2)
        grads.append(values)
    grad_ext = halo - GRAD_REACH
    inside = inside_mask(grads[0].shape, z0 - grad_ext, y0 - grad_ext, z_total, y_total)
    tensor = []
    for first, second in pair_list:
        values = jnp.where(inside, grads[first] * grads[second], 0.0)
        values = lax.slice_in_dim(values, grad_ext - TENSOR_REACH, values.shape[0] - grad_ext + TENSOR_REACH, axis=0)
        values = lax.slice_in_dim(values, grad_ext - TENSOR_REACH, values.shape[1] - grad_ext + TENSOR_REACH, axis=1)
        values = correlate(values, wide, 0)
        values = correlate(values, wide, 1)
        values = correlate(pad_x(values, TENSOR_REACH), wide, 2)
        tensor.append(values)
    parts = diffusion_tensor(tensor)
    stacked = jnp.stack(parts)
    stacked = surround(stacked, TENSOR_HALO)

    reach = 2 * STEPS
    field = volume[halo - reach : volume.shape[0] - halo + reach, halo - reach : volume.shape[1] - halo + reach]
    for segment in range(STEPS):
        ext = reach - 2 * segment
        cut = TENSOR_HALO - (ext - 1)
        local = [
            stacked[index, cut : stacked.shape[1] - cut, cut : stacked.shape[2] - cut]
            for index in range(6)
        ]
        wide_field = pad_x(field, 1)
        slopes = [
            (wide_field[2:, 1:-1, 1:-1] - wide_field[:-2, 1:-1, 1:-1]) * 0.5,
            (wide_field[1:-1, 2:, 1:-1] - wide_field[1:-1, :-2, 1:-1]) * 0.5,
            (wide_field[1:-1, 1:-1, 2:] - wide_field[1:-1, 1:-1, :-2]) * 0.5,
        ]
        fluxes = []
        for along in range(3):
            flux = local[pair_index(along, 0)] * slopes[0]
            flux = flux + local[pair_index(along, 1)] * slopes[1]
            flux = flux + local[pair_index(along, 2)] * slopes[2]
            fluxes.append(flux)
        flux_x = pad_x(fluxes[2], 1)
        total = (fluxes[0][2:, 1:-1] - fluxes[0][:-2, 1:-1]) * 0.5
        total = total + (fluxes[1][1:-1, 2:] - fluxes[1][1:-1, :-2]) * 0.5
        total = total + (flux_x[1:-1, 1:-1, 2:] - flux_x[1:-1, 1:-1, :-2]) * 0.5
        field = field[2:-2, 2:-2] + time_step * total
        if segment < STEPS - 1:
            new_ext = ext - 2
            inside = inside_mask(field.shape, z0 - new_ext, y0 - new_ext, z_total, y_total)
            field = jnp.where(inside, field, 0.0)
    return field


def solution(mesh):
    in_specs = (P("xy", None, "gz"),)
    out_specs = P("gz", "xy", None)
    return jax.shard_map(shards, mesh=mesh, in_specs=in_specs, out_specs=out_specs, check_vma=False)
```

```python
import math

import jax
import jax.numpy as jnp
from jax import lax
from jax.sharding import PartitionSpec as P

GRAD_REACH = 3
TENSOR_REACH = 4
SWEEPS = 4
STEPS = 3


sigma_noise = 1.0
sigma_tensor = 1.5
alpha_floor = 0.05
contrast = 0.05
time_step = 0.5
pair_list = ((0, 0), (1, 1), (2, 2), (0, 1), (0, 2), (1, 2))

VOLUME_HALO = max(GRAD_REACH + TENSOR_REACH, 2 * STEPS)
TENSOR_HALO = 2 * STEPS - 1


def extended_2(block, sides, width):
    for axis, dim in sides:
        count = lax.axis_size(axis)
        forward = [(i, i + 1) for i in range(count - 1)]
        backward = [(target, source) for source, target in forward]
        low = lax.ppermute(
            lax.slice_in_dim(block, block.shape[dim] - width, None, axis=dim), axis, forward
        )
        high = lax.ppermute(lax.slice_in_dim(block, 0, width, axis=dim), axis, backward)
        block = jnp.concatenate([low, block, high], axis=dim)
    return block


def gauss_taps(sigma, reach):
    raw = [math.exp(-(t * t) / (2.0 * sigma * sigma)) for t in range(-reach, reach + 1)]
    total = sum(raw)
    return [value / total for value in raw]


def slope_taps(sigma, reach):
    base = gauss_taps(sigma, reach)
    return [t * base[t + reach] / (sigma * sigma) for t in range(-reach, reach + 1)]


def correlate(values, taps, along):
    count = values.shape[along] - len(taps) + 1
    result = taps[0] * lax.slice_in_dim(values, 0, count, axis=along)
    for index in range(1, len(taps)):
        result = result + taps[index] * lax.slice_in_dim(values, index, index + count, axis=along)
    return result


def pad_x(values, width):
    return jnp.pad(values, ((0, 0), (0, 0), (width, width)))


def pair_index(first, second):
    low, high = (min(first, second), max(first, second))
    return pair_list.index((low, high))


def diffusion_tensor(parts):
    entry = {}
    for index in range(6):
        entry[pair_list[index]] = parts[index]
    ones = jnp.ones_like(parts[0])
    zeros = jnp.zeros_like(parts[0])
    basis = [[ones if row == col else zeros for col in range(3)] for row in range(3)]
    for sweep in range(SWEEPS):
        for first, second in ((0, 1), (0, 2), (1, 2)):
            third = 3 - first - second
            offdiag = entry[first, second]
            spread = entry[second, second] - entry[first, first]
            radius = jnp.sqrt(spread * spread + 4.0 * offdiag * offdiag + 1e-30)
            sign_part = jnp.where(spread >= 0.0, 1.0, -1.0)
            tangent = sign_part * 2.0 * offdiag / (jnp.abs(spread) + radius)
            cosine = 1.0 / jnp.sqrt(1.0 + tangent * tangent)
            sine = tangent * cosine
            entry[first, first] = entry[first, first] - tangent * offdiag
            entry[second, second] = entry[second, second] + tangent * offdiag
            entry[first, second] = zeros
            key_first = (min(third, first), max(third, first))
            key_second = (min(third, second), max(third, second))
            old_first = entry[key_first]
            old_second = entry[key_second]
            entry[key_first] = cosine * old_first - sine * old_second
            entry[key_second] = sine * old_first + cosine * old_second
            for row in range(3):
                left = basis[row][first]
                right = basis[row][second]
                basis[row][first] = cosine * left - sine * right
                basis[row][second] = sine * left + cosine * right
    eigen = [entry[0, 0], entry[1, 1], entry[2, 2]]
    top = jnp.maximum(jnp.maximum(eigen[0], eigen[1]), eigen[2])
    trace = eigen[0] + eigen[1] + eigen[2]
    gains = []
    for index in range(3):
        gap = top - eigen[index]
        gains.append(
            alpha_floor
            + (1.0 - alpha_floor) * gap * gap / (gap * gap + contrast * trace * trace + 1e-30)
        )
    result = []
    for first, second in pair_list:
        total = gains[0] * basis[first][0] * basis[second][0]
        total = total + gains[1] * basis[first][1] * basis[second][1]
        total = total + gains[2] * basis[first][2] * basis[second][2]
        result.append(total)
    return result


def inside_mask(shape, z_start, y_start, z_total, y_total):
    z = lax.broadcasted_iota(jnp.int32, shape, 0) + z_start
    y = lax.broadcasted_iota(jnp.int32, shape, 1) + y_start
    return (z >= 0) & (z < z_total) & (y >= 0) & (y < y_total)


def regroup(sections, halo):
    n_gz = lax.axis_size("gz")
    column = lax.all_to_all(sections, "xy", split_axis=1, concat_axis=0, tiled=True)
    z_total, y_block, _ = column.shape
    y_total = y_block * lax.axis_size("xy")
    z_block = z_total // n_gz
    padded = jnp.pad(column, ((halo, halo), (0, 0), (0, 0)))
    me = lax.axis_index("gz")
    x_block = column.shape[2]
    rows = z_block + 2 * halo
    volume = jnp.zeros((rows, y_block, x_block * n_gz), column.dtype)
    for shift in range(n_gz):
        target = (me + shift) % n_gz
        window = lax.dynamic_slice_in_dim(padded, target * z_block, rows, axis=0)
        if shift:
            pairs = [(source, (source + shift) % n_gz) for source in range(n_gz)]
            window = lax.ppermute(window, "gz", pairs)
        source = (me - shift) % n_gz
        volume = lax.dynamic_update_slice_in_dim(volume, window, source * x_block, axis=2)
    volume = extended_2(volume, (("xy", 1),), halo)
    return lax.optimization_barrier(volume), z_total, y_total, z_block, y_block


def surround(block, width):
    n_xy = lax.axis_size("xy")
    n_gz = lax.axis_size("gz")
    z_block, y_block = block.shape[1], block.shape[2]
    edge_z = {-1: slice(z_block - width, None), 0: slice(None), 1: slice(0, width)}
    edge_y = {-1: slice(y_block - width, None), 0: slice(None), 1: slice(0, width)}
    pieces = {}
    for dz in (-1, 0, 1):
        for dy in (-1, 0, 1):
            if dz == 0 and dy == 0:
                pieces[dz, dy] = block
                continue
            part = block[:, edge_z[dz], edge_y[dy]]
            pairs = []
            for a in range(n_xy):
                for b in range(n_gz):
                    if 0 <= a + dy < n_xy and 0 <= b + dz < n_gz:
                        pairs.append(((a + dy) * n_gz + (b + dz), a * n_gz + b))
            pieces[dz, dy] = lax.ppermute(part, ("xy", "gz"), pairs)
    rows = [jnp.concatenate([pieces[dz, dy] for dy in (-1, 0, 1)], axis=2) for dz in (-1, 0, 1)]
    return jnp.concatenate(rows, axis=1)


def shards(sections):
    halo = VOLUME_HALO
    volume, z_total, y_total, z_block, y_block = regroup(sections, halo)
    z0 = lax.axis_index("gz") * z_block
    y0 = lax.axis_index("xy") * y_block

    smooth = gauss_taps(sigma_noise, GRAD_REACH)
    slope = slope_taps(sigma_noise, GRAD_REACH)
    wide = gauss_taps(sigma_tensor, TENSOR_REACH)

    grads = []
    for component in range(3):
        values = volume
        for along in range(2):
            taps = slope if along == component else smooth
            values = correlate(values, taps, along)
        taps = slope if component == 2 else smooth
        values = correlate(pad_x(values, GRAD_REACH), taps, 2)
        grads.append(values)
    grad_ext = halo - GRAD_REACH
    inside = inside_mask(grads[0].shape, z0 - grad_ext, y0 - grad_ext, z_total, y_total)
    tensor = []
    for first, second in pair_list:
        values = jnp.where(inside, grads[first] * grads[second], 0.0)
        values = lax.slice_in_dim(values, grad_ext - TENSOR_REACH, values.shape[0] - grad_ext + TENSOR_REACH, axis=0)
        values = lax.slice_in_dim(values, grad_ext - TENSOR_REACH, values.shape[1] - grad_ext + TENSOR_REACH, axis=1)
        values = correlate(values, wide, 0)
        values = correlate(values, wide, 1)
        values = correlate(pad_x(values, TENSOR_REACH), wide, 2)
        tensor.append(values)
    parts = diffusion_tensor(tensor)
    stacked = jnp.stack(parts)
    stacked = surround(stacked, TENSOR_HALO)

    reach = 2 * STEPS
    field = volume[halo - reach : volume.shape[0] - halo + reach, halo - reach : volume.shape[1] - halo + reach]
    for segment in range(STEPS):
        ext = reach - 2 * segment
        cut = TENSOR_HALO - (ext - 1)
        local = [
            stacked[index, cut : stacked.shape[1] - cut, cut : stacked.shape[2] - cut]
            for index in range(6)
        ]
        wide_field = pad_x(field, 1)
        slopes = [
            (wide_field[2:, 1:-1, 1:-1] - wide_field[:-2, 1:-1, 1:-1]) * 0.5,
            (wide_field[1:-1, 2:, 1:-1] - wide_field[1:-1, :-2, 1:-1]) * 0.5,
            (wide_field[1:-1, 1:-1, 2:] - wide_field[1:-1, 1:-1, :-2]) * 0.5,
        ]
        fluxes = []
        for along in range(3):
            flux = local[pair_index(along, 0)] * slopes[0]
            flux = flux + local[pair_index(along, 1)] * slopes[1]
            flux = flux + local[pair_index(along, 2)] * slopes[2]
            fluxes.append(flux)
        flux_x = pad_x(fluxes[2], 1)
        total = (fluxes[0][2:, 1:-1] - fluxes[0][:-2, 1:-1]) * 0.5
        total = total + (fluxes[1][1:-1, 2:] - fluxes[1][1:-1, :-2]) * 0.5
        total = total + (flux_x[1:-1, 1:-1, 2:] - flux_x[1:-1, 1:-1, :-2]) * 0.5
        field = field[2:-2, 2:-2] + time_step * total
        if segment < STEPS - 1:
            new_ext = ext - 2
            inside = inside_mask(field.shape, z0 - new_ext, y0 - new_ext, z_total, y_total)
            field = jnp.where(inside, field, 0.0)
    return field


def solution(mesh):
    in_specs = (P("xy", None, "gz"),)
    out_specs = P("gz", "xy", None)
    return jax.shard_map(shards, mesh=mesh, in_specs=in_specs, out_specs=out_specs, check_vma=False)
```

```python
import math

import jax
import jax.numpy as jnp
from jax import lax
from jax.sharding import PartitionSpec as P

GRAD_REACH = 3
TENSOR_REACH = 4
SWEEPS = 4
STEPS = 3


sigma_noise = 1.0
sigma_tensor = 1.5
alpha_floor = 0.05
contrast = 0.05
time_step = 0.5
pair_list = ((0, 0), (1, 1), (2, 2), (0, 1), (0, 2), (1, 2))

VOLUME_HALO = max(GRAD_REACH + TENSOR_REACH, 2 * STEPS)
TENSOR_HALO = 2 * STEPS - 1


def extended_2(block, sides, width):
    for axis, dim in sides:
        count = lax.axis_size(axis)
        forward = [(i, i + 1) for i in range(count - 1)]
        backward = [(target, source) for source, target in forward]
        low = lax.ppermute(
            lax.slice_in_dim(block, block.shape[dim] - width, None, axis=dim), axis, forward
        )
        high = lax.ppermute(lax.slice_in_dim(block, 0, width, axis=dim), axis, backward)
        block = jnp.concatenate([low, block, high], axis=dim)
    return block


def gauss_taps(sigma, reach):
    raw = [math.exp(-(t * t) / (2.0 * sigma * sigma)) for t in range(-reach, reach + 1)]
    total = sum(raw)
    return [value / total for value in raw]


def slope_taps(sigma, reach):
    base = gauss_taps(sigma, reach)
    return [t * base[t + reach] / (sigma * sigma) for t in range(-reach, reach + 1)]


def correlate(values, taps, along):
    count = values.shape[along] - len(taps) + 1
    result = taps[0] * lax.slice_in_dim(values, 0, count, axis=along)
    for index in range(1, len(taps)):
        result = result + taps[index] * lax.slice_in_dim(values, index, index + count, axis=along)
    return result


def pad_x(values, width):
    return jnp.pad(values, ((0, 0), (0, 0), (width, width)))


def pair_index(first, second):
    low, high = (min(first, second), max(first, second))
    return pair_list.index((low, high))


def diffusion_tensor(parts):
    entry = {}
    for index in range(6):
        entry[pair_list[index]] = parts[index]
    ones = jnp.ones_like(parts[0])
    zeros = jnp.zeros_like(parts[0])
    basis = [[ones if row == col else zeros for col in range(3)] for row in range(3)]
    for sweep in range(SWEEPS):
        for first, second in ((0, 1), (0, 2), (1, 2)):
            third = 3 - first - second
            offdiag = entry[first, second]
            spread = entry[second, second] - entry[first, first]
            radius = jnp.sqrt(spread * spread + 4.0 * offdiag * offdiag + 1e-30)
            sign_part = jnp.where(spread >= 0.0, 1.0, -1.0)
            tangent = sign_part * 2.0 * offdiag / (jnp.abs(spread) + radius)
            cosine = 1.0 / jnp.sqrt(1.0 + tangent * tangent)
            sine = tangent * cosine
            entry[first, first] = entry[first, first] - tangent * offdiag
            entry[second, second] = entry[second, second] + tangent * offdiag
            entry[first, second] = zeros
            key_first = (min(third, first), max(third, first))
            key_second = (min(third, second), max(third, second))
            old_first = entry[key_first]
            old_second = entry[key_second]
            entry[key_first] = cosine * old_first - sine * old_second
            entry[key_second] = sine * old_first + cosine * old_second
            for row in range(3):
                left = basis[row][first]
                right = basis[row][second]
                basis[row][first] = cosine * left - sine * right
                basis[row][second] = sine * left + cosine * right
    eigen = [entry[0, 0], entry[1, 1], entry[2, 2]]
    top = jnp.maximum(jnp.maximum(eigen[0], eigen[1]), eigen[2])
    trace = eigen[0] + eigen[1] + eigen[2]
    gains = []
    for index in range(3):
        gap = top - eigen[index]
        gains.append(
            alpha_floor
            + (1.0 - alpha_floor) * gap * gap / (gap * gap + contrast * trace * trace + 1e-30)
        )
    result = []
    for first, second in pair_list:
        total = gains[0] * basis[first][0] * basis[second][0]
        total = total + gains[1] * basis[first][1] * basis[second][1]
        total = total + gains[2] * basis[first][2] * basis[second][2]
        result.append(total)
    return result


def inside_mask(shape, z_start, y_start, z_total, y_total):
    z = lax.broadcasted_iota(jnp.int32, shape, 0) + z_start
    y = lax.broadcasted_iota(jnp.int32, shape, 1) + y_start
    return (z >= 0) & (z < z_total) & (y >= 0) & (y < y_total)


def regroup(sections, halo):
    n_gz = lax.axis_size("gz")
    column = lax.all_to_all(sections, "xy", split_axis=1, concat_axis=0, tiled=True)
    z_total, y_block, _ = column.shape
    y_total = y_block * lax.axis_size("xy")
    z_block = z_total // n_gz
    padded = jnp.pad(column, ((halo, halo), (0, 0), (0, 0)))
    me = lax.axis_index("gz")
    x_block = column.shape[2]
    rows = z_block + 2 * halo
    pieces = []
    for shift in range(n_gz):
        target = (me + shift) % n_gz
        window = lax.dynamic_slice_in_dim(padded, target * z_block, rows, axis=0)
        if shift:
            pairs = [(source, (source + shift) % n_gz) for source in range(n_gz)]
            window = lax.ppermute(window, "gz", pairs)
        pieces.append(window)
    slots = []
    for slot in range(n_gz):
        arrived = (me - slot) % n_gz
        value = pieces[0]
        for shift in range(1, n_gz):
            value = jnp.where(arrived == shift, pieces[shift], value)
        slots.append(value)
    volume = jnp.concatenate(slots, axis=2)
    volume = extended_2(volume, (("xy", 1),), halo)
    return lax.optimization_barrier(volume), z_total, y_total, z_block, y_block


def surround(block, width):
    n_xy = lax.axis_size("xy")
    n_gz = lax.axis_size("gz")
    z_block, y_block = block.shape[1], block.shape[2]
    edge_z = {-1: slice(z_block - width, None), 0: slice(None), 1: slice(0, width)}
    edge_y = {-1: slice(y_block - width, None), 0: slice(None), 1: slice(0, width)}
    pieces = {}
    for dz in (-1, 0, 1):
        for dy in (-1, 0, 1):
            if dz == 0 and dy == 0:
                pieces[dz, dy] = block
                continue
            part = block[:, edge_z[dz], edge_y[dy]]
            pairs = []
            for a in range(n_xy):
                for b in range(n_gz):
                    if 0 <= a + dy < n_xy and 0 <= b + dz < n_gz:
                        pairs.append(((a + dy) * n_gz + (b + dz), a * n_gz + b))
            pieces[dz, dy] = lax.ppermute(part, ("xy", "gz"), pairs)
    rows = [jnp.concatenate([pieces[dz, dy] for dy in (-1, 0, 1)], axis=2) for dz in (-1, 0, 1)]
    return jnp.concatenate(rows, axis=1)


def shards(sections):
    halo = VOLUME_HALO
    volume, z_total, y_total, z_block, y_block = regroup(sections, halo)
    z0 = lax.axis_index("gz") * z_block
    y0 = lax.axis_index("xy") * y_block

    smooth = gauss_taps(sigma_noise, GRAD_REACH)
    slope = slope_taps(sigma_noise, GRAD_REACH)
    wide = gauss_taps(sigma_tensor, TENSOR_REACH)

    grads = []
    for component in range(3):
        values = volume
        for along in range(2):
            taps = slope if along == component else smooth
            values = correlate(values, taps, along)
        taps = slope if component == 2 else smooth
        values = correlate(pad_x(values, GRAD_REACH), taps, 2)
        grads.append(values)
    grad_ext = halo - GRAD_REACH
    inside = inside_mask(grads[0].shape, z0 - grad_ext, y0 - grad_ext, z_total, y_total)
    tensor = []
    for first, second in pair_list:
        values = jnp.where(inside, grads[first] * grads[second], 0.0)
        values = lax.slice_in_dim(values, grad_ext - TENSOR_REACH, values.shape[0] - grad_ext + TENSOR_REACH, axis=0)
        values = lax.slice_in_dim(values, grad_ext - TENSOR_REACH, values.shape[1] - grad_ext + TENSOR_REACH, axis=1)
        values = correlate(values, wide, 0)
        values = correlate(values, wide, 1)
        values = correlate(pad_x(values, TENSOR_REACH), wide, 2)
        tensor.append(values)
    parts = diffusion_tensor(tensor)
    stacked = jnp.stack(parts)
    stacked = surround(stacked, TENSOR_HALO)

    reach = 2 * STEPS
    field = volume[halo - reach : volume.shape[0] - halo + reach, halo - reach : volume.shape[1] - halo + reach]
    for segment in range(STEPS):
        ext = reach - 2 * segment
        cut = TENSOR_HALO - (ext - 1)
        local = [
            stacked[index, cut : stacked.shape[1] - cut, cut : stacked.shape[2] - cut]
            for index in range(6)
        ]
        wide_field = pad_x(field, 1)
        slopes = [
            (wide_field[2:, 1:-1, 1:-1] - wide_field[:-2, 1:-1, 1:-1]) * 0.5,
            (wide_field[1:-1, 2:, 1:-1] - wide_field[1:-1, :-2, 1:-1]) * 0.5,
            (wide_field[1:-1, 1:-1, 2:] - wide_field[1:-1, 1:-1, :-2]) * 0.5,
        ]
        fluxes = []
        for along in range(3):
            flux = local[pair_index(along, 0)] * slopes[0]
            flux = flux + local[pair_index(along, 1)] * slopes[1]
            flux = flux + local[pair_index(along, 2)] * slopes[2]
            fluxes.append(flux)
        flux_x = pad_x(fluxes[2], 1)
        total = (fluxes[0][2:, 1:-1] - fluxes[0][:-2, 1:-1]) * 0.5
        total = total + (fluxes[1][1:-1, 2:] - fluxes[1][1:-1, :-2]) * 0.5
        total = total + (flux_x[1:-1, 1:-1, 2:] - flux_x[1:-1, 1:-1, :-2]) * 0.5
        field = field[2:-2, 2:-2] + time_step * total
        if segment < STEPS - 1:
            new_ext = ext - 2
            inside = inside_mask(field.shape, z0 - new_ext, y0 - new_ext, z_total, y_total)
            field = jnp.where(inside, field, 0.0)
    return field


def solution(mesh):
    in_specs = (P("xy", None, "gz"),)
    out_specs = P("gz", "xy", None)
    return jax.shard_map(shards, mesh=mesh, in_specs=in_specs, out_specs=out_specs, check_vma=False)
```

```python
import math

import jax
import jax.numpy as jnp
from jax import lax
from jax.sharding import PartitionSpec as P

GRAD_REACH = 3
TENSOR_REACH = 4
SWEEPS = 4
STEPS = 3


sigma_noise = 1.0
sigma_tensor = 1.5
alpha_floor = 0.05
contrast = 0.05
time_step = 0.5
pair_list = ((0, 0), (1, 1), (2, 2), (0, 1), (0, 2), (1, 2))

VOLUME_HALO = max(GRAD_REACH + TENSOR_REACH, 2 * STEPS)
TENSOR_HALO = 2 * STEPS - 1
Y_HALO = GRAD_REACH + TENSOR_REACH + TENSOR_HALO


def extended_2(block, sides, width):
    for axis, dim in sides:
        count = lax.axis_size(axis)
        forward = [(i, i + 1) for i in range(count - 1)]
        backward = [(target, source) for source, target in forward]
        low = lax.ppermute(
            lax.slice_in_dim(block, block.shape[dim] - width, None, axis=dim), axis, forward
        )
        high = lax.ppermute(lax.slice_in_dim(block, 0, width, axis=dim), axis, backward)
        block = jnp.concatenate([low, block, high], axis=dim)
    return block


def gauss_taps(sigma, reach):
    raw = [math.exp(-(t * t) / (2.0 * sigma * sigma)) for t in range(-reach, reach + 1)]
    total = sum(raw)
    return [value / total for value in raw]


def slope_taps(sigma, reach):
    base = gauss_taps(sigma, reach)
    return [t * base[t + reach] / (sigma * sigma) for t in range(-reach, reach + 1)]


def correlate(values, taps, along):
    count = values.shape[along] - len(taps) + 1
    result = taps[0] * lax.slice_in_dim(values, 0, count, axis=along)
    for index in range(1, len(taps)):
        result = result + taps[index] * lax.slice_in_dim(values, index, index + count, axis=along)
    return result


def pad_x(values, width):
    return jnp.pad(values, ((0, 0), (0, 0), (width, width)))


def pair_index(first, second):
    low, high = (min(first, second), max(first, second))
    return pair_list.index((low, high))


def diffusion_tensor(parts):
    entry = {}
    for index in range(6):
        entry[pair_list[index]] = parts[index]
    ones = jnp.ones_like(parts[0])
    zeros = jnp.zeros_like(parts[0])
    basis = [[ones if row == col else zeros for col in range(3)] for row in range(3)]
    for sweep in range(SWEEPS):
        for first, second in ((0, 1), (0, 2), (1, 2)):
            third = 3 - first - second
            offdiag = entry[first, second]
            spread = entry[second, second] - entry[first, first]
            radius = jnp.sqrt(spread * spread + 4.0 * offdiag * offdiag + 1e-30)
            sign_part = jnp.where(spread >= 0.0, 1.0, -1.0)
            tangent = sign_part * 2.0 * offdiag / (jnp.abs(spread) + radius)
            cosine = 1.0 / jnp.sqrt(1.0 + tangent * tangent)
            sine = tangent * cosine
            entry[first, first] = entry[first, first] - tangent * offdiag
            entry[second, second] = entry[second, second] + tangent * offdiag
            entry[first, second] = zeros
            key_first = (min(third, first), max(third, first))
            key_second = (min(third, second), max(third, second))
            old_first = entry[key_first]
            old_second = entry[key_second]
            entry[key_first] = cosine * old_first - sine * old_second
            entry[key_second] = sine * old_first + cosine * old_second
            for row in range(3):
                left = basis[row][first]
                right = basis[row][second]
                basis[row][first] = cosine * left - sine * right
                basis[row][second] = sine * left + cosine * right
    eigen = [entry[0, 0], entry[1, 1], entry[2, 2]]
    top = jnp.maximum(jnp.maximum(eigen[0], eigen[1]), eigen[2])
    trace = eigen[0] + eigen[1] + eigen[2]
    gains = []
    for index in range(3):
        gap = top - eigen[index]
        gains.append(
            alpha_floor
            + (1.0 - alpha_floor) * gap * gap / (gap * gap + contrast * trace * trace + 1e-30)
        )
    result = []
    for first, second in pair_list:
        total = gains[0] * basis[first][0] * basis[second][0]
        total = total + gains[1] * basis[first][1] * basis[second][1]
        total = total + gains[2] * basis[first][2] * basis[second][2]
        result.append(total)
    return result


def inside_mask(shape, z_start, y_start, z_total, y_total):
    z = lax.broadcasted_iota(jnp.int32, shape, 0) + z_start
    y = lax.broadcasted_iota(jnp.int32, shape, 1) + y_start
    return (z >= 0) & (z < z_total) & (y >= 0) & (y < y_total)


def regroup(sections, halo):
    n_gz = lax.axis_size("gz")
    column = lax.all_to_all(sections, "xy", split_axis=1, concat_axis=0, tiled=True)
    z_total, y_block, _ = column.shape
    y_total = y_block * lax.axis_size("xy")
    z_block = z_total // n_gz
    padded = jnp.pad(column, ((halo, halo), (0, 0), (0, 0)))
    windows = jnp.stack(
        [lax.slice_in_dim(padded, b * z_block, b * z_block + z_block + 2 * halo, axis=0) for b in range(n_gz)]
    )
    got = lax.all_to_all(windows, "gz", split_axis=0, concat_axis=0, tiled=True)
    volume = jnp.transpose(got, (1, 2, 0, 3))
    volume = volume.reshape(volume.shape[:2] + (-1,))
    volume = extended_2(volume, (("xy", 1),), Y_HALO)
    return lax.optimization_barrier(volume), z_total, y_total, z_block, y_block


def surround(block, width):
    n_xy = lax.axis_size("xy")
    n_gz = lax.axis_size("gz")
    z_block, y_block = block.shape[1], block.shape[2]
    edge_z = {-1: slice(z_block - width, None), 0: slice(None), 1: slice(0, width)}
    edge_y = {-1: slice(y_block - width, None), 0: slice(None), 1: slice(0, width)}
    pieces = {}
    for dz in (-1, 0, 1):
        for dy in (-1, 0, 1):
            if dz == 0 and dy == 0:
                pieces[dz, dy] = block
                continue
            part = block[:, edge_z[dz], edge_y[dy]]
            pairs = []
            for a in range(n_xy):
                for b in range(n_gz):
                    if 0 <= a + dy < n_xy and 0 <= b + dz < n_gz:
                        pairs.append(((a + dy) * n_gz + (b + dz), a * n_gz + b))
            pieces[dz, dy] = lax.ppermute(part, ("xy", "gz"), pairs)
    rows = [jnp.concatenate([pieces[dz, dy] for dy in (-1, 0, 1)], axis=2) for dz in (-1, 0, 1)]
    return jnp.concatenate(rows, axis=1)


def shards(sections):
    halo = VOLUME_HALO
    volume, z_total, y_total, z_block, y_block = regroup(sections, halo)
    z0 = lax.axis_index("gz") * z_block
    y0 = lax.axis_index("xy") * y_block

    smooth = gauss_taps(sigma_noise, GRAD_REACH)
    slope = slope_taps(sigma_noise, GRAD_REACH)
    wide = gauss_taps(sigma_tensor, TENSOR_REACH)

    grads = []
    for component in range(3):
        values = volume
        for along in range(2):
            taps = slope if along == component else smooth
            values = correlate(values, taps, along)
        taps = slope if component == 2 else smooth
        values = correlate(pad_x(values, GRAD_REACH), taps, 2)
        grads.append(values)
    grad_ext = halo - GRAD_REACH
    grad_ext_y = Y_HALO - GRAD_REACH
    inside = inside_mask(grads[0].shape, z0 - grad_ext, y0 - grad_ext_y, z_total, y_total)
    tensor = []
    for first, second in pair_list:
        values = jnp.where(inside, grads[first] * grads[second], 0.0)
        values = lax.slice_in_dim(values, grad_ext - TENSOR_REACH, values.shape[0] - grad_ext + TENSOR_REACH, axis=0)
        values = correlate(values, wide, 0)
        values = correlate(values, wide, 1)
        values = correlate(pad_x(values, TENSOR_REACH), wide, 2)
        tensor.append(values)
    parts = diffusion_tensor(tensor)
    inside = inside_mask(parts[0].shape, z0, y0 - TENSOR_HALO, z_total, y_total)
    stacked = jnp.stack([jnp.where(inside, item, 0.0) for item in parts])
    stacked = extended_2(stacked, (("gz", 1),), TENSOR_HALO)

    reach = 2 * STEPS
    field = volume[halo - reach : volume.shape[0] - halo + reach, Y_HALO - reach : volume.shape[1] - Y_HALO + reach]
    for segment in range(STEPS):
        ext = reach - 2 * segment
        cut = TENSOR_HALO - (ext - 1)
        local = [
            stacked[index, cut : stacked.shape[1] - cut, cut : stacked.shape[2] - cut]
            for index in range(6)
        ]
        wide_field = pad_x(field, 1)
        slopes = [
            (wide_field[2:, 1:-1, 1:-1] - wide_field[:-2, 1:-1, 1:-1]) * 0.5,
            (wide_field[1:-1, 2:, 1:-1] - wide_field[1:-1, :-2, 1:-1]) * 0.5,
            (wide_field[1:-1, 1:-1, 2:] - wide_field[1:-1, 1:-1, :-2]) * 0.5,
        ]
        fluxes = []
        for along in range(3):
            flux = local[pair_index(along, 0)] * slopes[0]
            flux = flux + local[pair_index(along, 1)] * slopes[1]
            flux = flux + local[pair_index(along, 2)] * slopes[2]
            fluxes.append(flux)
        flux_x = pad_x(fluxes[2], 1)
        total = (fluxes[0][2:, 1:-1] - fluxes[0][:-2, 1:-1]) * 0.5
        total = total + (fluxes[1][1:-1, 2:] - fluxes[1][1:-1, :-2]) * 0.5
        total = total + (flux_x[1:-1, 1:-1, 2:] - flux_x[1:-1, 1:-1, :-2]) * 0.5
        field = field[2:-2, 2:-2] + time_step * total
        if segment < STEPS - 1:
            new_ext = ext - 2
            inside = inside_mask(field.shape, z0 - new_ext, y0 - new_ext, z_total, y_total)
            field = jnp.where(inside, field, 0.0)
    return field


def solution(mesh):
    in_specs = (P("xy", None, "gz"),)
    out_specs = P("gz", "xy", None)
    return jax.shard_map(shards, mesh=mesh, in_specs=in_specs, out_specs=out_specs, check_vma=False)
```

```python
import math

import jax
import jax.numpy as jnp
from jax import lax
from jax.sharding import PartitionSpec as P

GRAD_REACH = 3
TENSOR_REACH = 4
SWEEPS = 4
STEPS = 3


sigma_noise = 1.0
sigma_tensor = 1.5
alpha_floor = 0.05
contrast = 0.05
time_step = 0.5
pair_list = ((0, 0), (1, 1), (2, 2), (0, 1), (0, 2), (1, 2))

VOLUME_HALO = max(GRAD_REACH + TENSOR_REACH, 2 * STEPS)
TENSOR_HALO = 2 * STEPS - 1


def extended_2(block, sides, width):
    for axis, dim in sides:
        count = lax.axis_size(axis)
        forward = [(i, i + 1) for i in range(count - 1)]
        backward = [(target, source) for source, target in forward]
        low = lax.ppermute(
            lax.slice_in_dim(block, block.shape[dim] - width, None, axis=dim), axis, forward
        )
        high = lax.ppermute(lax.slice_in_dim(block, 0, width, axis=dim), axis, backward)
        block = jnp.concatenate([low, block, high], axis=dim)
    return block


def gauss_taps(sigma, reach):
    raw = [math.exp(-(t * t) / (2.0 * sigma * sigma)) for t in range(-reach, reach + 1)]
    total = sum(raw)
    return [value / total for value in raw]


def slope_taps(sigma, reach):
    base = gauss_taps(sigma, reach)
    return [t * base[t + reach] / (sigma * sigma) for t in range(-reach, reach + 1)]


def correlate(values, taps, along):
    count = values.shape[along] - len(taps) + 1
    result = taps[0] * lax.slice_in_dim(values, 0, count, axis=along)
    for index in range(1, len(taps)):
        result = result + taps[index] * lax.slice_in_dim(values, index, index + count, axis=along)
    return result


def pad_x(values, width):
    return jnp.pad(values, ((0, 0), (0, 0), (width, width)))


def pair_index(first, second):
    low, high = (min(first, second), max(first, second))
    return pair_list.index((low, high))


def diffusion_tensor(parts):
    entry = {}
    for index in range(6):
        entry[pair_list[index]] = parts[index]
    ones = jnp.ones_like(parts[0])
    zeros = jnp.zeros_like(parts[0])
    basis = [[ones if row == col else zeros for col in range(3)] for row in range(3)]
    for sweep in range(SWEEPS):
        for first, second in ((0, 1), (0, 2), (1, 2)):
            third = 3 - first - second
            offdiag = entry[first, second]
            spread = entry[second, second] - entry[first, first]
            radius = jnp.sqrt(spread * spread + 4.0 * offdiag * offdiag + 1e-30)
            sign_part = jnp.where(spread >= 0.0, 1.0, -1.0)
            tangent = sign_part * 2.0 * offdiag / (jnp.abs(spread) + radius)
            cosine = 1.0 / jnp.sqrt(1.0 + tangent * tangent)
            sine = tangent * cosine
            entry[first, first] = entry[first, first] - tangent * offdiag
            entry[second, second] = entry[second, second] + tangent * offdiag
            entry[first, second] = zeros
            key_first = (min(third, first), max(third, first))
            key_second = (min(third, second), max(third, second))
            old_first = entry[key_first]
            old_second = entry[key_second]
            entry[key_first] = cosine * old_first - sine * old_second
            entry[key_second] = sine * old_first + cosine * old_second
            for row in range(3):
                left = basis[row][first]
                right = basis[row][second]
                basis[row][first] = cosine * left - sine * right
                basis[row][second] = sine * left + cosine * right
    eigen = [entry[0, 0], entry[1, 1], entry[2, 2]]
    top = jnp.maximum(jnp.maximum(eigen[0], eigen[1]), eigen[2])
    trace = eigen[0] + eigen[1] + eigen[2]
    gains = []
    for index in range(3):
        gap = top - eigen[index]
        gains.append(
            alpha_floor
            + (1.0 - alpha_floor) * gap * gap / (gap * gap + contrast * trace * trace + 1e-30)
        )
    result = []
    for first, second in pair_list:
        total = gains[0] * basis[first][0] * basis[second][0]
        total = total + gains[1] * basis[first][1] * basis[second][1]
        total = total + gains[2] * basis[first][2] * basis[second][2]
        result.append(total)
    return result


def inside_mask(shape, z_start, y_start, z_total, y_total):
    z = lax.broadcasted_iota(jnp.int32, shape, 0) + z_start
    y = lax.broadcasted_iota(jnp.int32, shape, 1) + y_start
    return (z >= 0) & (z < z_total) & (y >= 0) & (y < y_total)


def regroup(sections, halo):
    n_gz = lax.axis_size("gz")
    column = lax.all_to_all(sections, "xy", split_axis=1, concat_axis=0, tiled=True)
    z_total, y_block, _ = column.shape
    y_total = y_block * lax.axis_size("xy")
    z_block = z_total // n_gz
    padded = jnp.pad(column, ((halo, halo), (0, 0), (0, 0)))
    windows = jnp.stack(
        [lax.slice_in_dim(padded, b * z_block, b * z_block + z_block + 2 * halo, axis=0) for b in range(n_gz)]
    )
    got = lax.all_to_all(windows, "gz", split_axis=0, concat_axis=0, tiled=True)
    volume = jnp.transpose(got, (1, 2, 0, 3))
    volume = volume.reshape(volume.shape[:2] + (-1,))
    volume = extended_2(volume, (("xy", 1),), halo)
    return lax.optimization_barrier(volume), z_total, y_total, z_block, y_block


def surround(block, width):

    def shifts(values, axis, dim):
        count = lax.axis_size(axis)
        forward = [(i, i + 1) for i in range(count - 1)]
        backward = [(target, source) for source, target in forward]
        size = values.shape[dim]
        low = lax.ppermute(lax.slice_in_dim(values, size - width, None, axis=dim), axis, forward)
        high = lax.ppermute(lax.slice_in_dim(values, 0, width, axis=dim), axis, backward)
        return low, high

    z_low, z_high = shifts(block, "gz", 1)
    y_low, y_high = shifts(block, "xy", 2)
    faces = jnp.concatenate([z_low, z_high], axis=1)
    corner_low, corner_high = shifts(faces, "xy", 2)
    rows = [
        jnp.concatenate([corner_low[:, :width], z_low, corner_high[:, :width]], axis=2),
        jnp.concatenate([y_low, block, y_high], axis=2),
        jnp.concatenate([corner_low[:, width:], z_high, corner_high[:, width:]], axis=2),
    ]
    return jnp.concatenate(rows, axis=1)


def shards(sections):
    halo = VOLUME_HALO
    volume, z_total, y_total, z_block, y_block = regroup(sections, halo)
    z0 = lax.axis_index("gz") * z_block
    y0 = lax.axis_index("xy") * y_block

    smooth = gauss_taps(sigma_noise, GRAD_REACH)
    slope = slope_taps(sigma_noise, GRAD_REACH)
    wide = gauss_taps(sigma_tensor, TENSOR_REACH)

    grads = []
    for component in range(3):
        values = volume
        for along in range(2):
            taps = slope if along == component else smooth
            values = correlate(values, taps, along)
        taps = slope if component == 2 else smooth
        values = correlate(pad_x(values, GRAD_REACH), taps, 2)
        grads.append(values)
    grad_ext = halo - GRAD_REACH
    inside = inside_mask(grads[0].shape, z0 - grad_ext, y0 - grad_ext, z_total, y_total)
    tensor = []
    for first, second in pair_list:
        values = jnp.where(inside, grads[first] * grads[second], 0.0)
        values = lax.slice_in_dim(values, grad_ext - TENSOR_REACH, values.shape[0] - grad_ext + TENSOR_REACH, axis=0)
        values = lax.slice_in_dim(values, grad_ext - TENSOR_REACH, values.shape[1] - grad_ext + TENSOR_REACH, axis=1)
        values = correlate(values, wide, 0)
        values = correlate(values, wide, 1)
        values = correlate(pad_x(values, TENSOR_REACH), wide, 2)
        tensor.append(values)
    parts = diffusion_tensor(tensor)
    stacked = jnp.stack(parts)
    stacked = surround(stacked, TENSOR_HALO)

    reach = 2 * STEPS
    field = volume[halo - reach : volume.shape[0] - halo + reach, halo - reach : volume.shape[1] - halo + reach]
    for segment in range(STEPS):
        ext = reach - 2 * segment
        cut = TENSOR_HALO - (ext - 1)
        local = [
            stacked[index, cut : stacked.shape[1] - cut, cut : stacked.shape[2] - cut]
            for index in range(6)
        ]
        wide_field = pad_x(field, 1)
        slopes = [
            (wide_field[2:, 1:-1, 1:-1] - wide_field[:-2, 1:-1, 1:-1]) * 0.5,
            (wide_field[1:-1, 2:, 1:-1] - wide_field[1:-1, :-2, 1:-1]) * 0.5,
            (wide_field[1:-1, 1:-1, 2:] - wide_field[1:-1, 1:-1, :-2]) * 0.5,
        ]
        fluxes = []
        for along in range(3):
            flux = local[pair_index(along, 0)] * slopes[0]
            flux = flux + local[pair_index(along, 1)] * slopes[1]
            flux = flux + local[pair_index(along, 2)] * slopes[2]
            fluxes.append(flux)
        flux_x = pad_x(fluxes[2], 1)
        total = (fluxes[0][2:, 1:-1] - fluxes[0][:-2, 1:-1]) * 0.5
        total = total + (fluxes[1][1:-1, 2:] - fluxes[1][1:-1, :-2]) * 0.5
        total = total + (flux_x[1:-1, 1:-1, 2:] - flux_x[1:-1, 1:-1, :-2]) * 0.5
        field = field[2:-2, 2:-2] + time_step * total
        if segment < STEPS - 1:
            new_ext = ext - 2
            inside = inside_mask(field.shape, z0 - new_ext, y0 - new_ext, z_total, y_total)
            field = jnp.where(inside, field, 0.0)
    return field


def solution(mesh):
    in_specs = (P("xy", None, "gz"),)
    out_specs = P("gz", "xy", None)
    return jax.shard_map(shards, mesh=mesh, in_specs=in_specs, out_specs=out_specs, check_vma=False)
```

```python
import math

import jax
import jax.numpy as jnp
from jax import lax
from jax.sharding import PartitionSpec as P

GRAD_REACH = 3
TENSOR_REACH = 4
SWEEPS = 4
STEPS = 3


sigma_noise = 1.0
sigma_tensor = 1.5
alpha_floor = 0.05
contrast = 0.05
time_step = 0.5
pair_list = ((0, 0), (1, 1), (2, 2), (0, 1), (0, 2), (1, 2))

VOLUME_HALO = max(GRAD_REACH + TENSOR_REACH, 2 * STEPS)
TENSOR_HALO = 2 * STEPS - 1


def extended_2(block, sides, width):
    for axis, dim in sides:
        count = lax.axis_size(axis)
        forward = [(i, i + 1) for i in range(count - 1)]
        backward = [(target, source) for source, target in forward]
        low = lax.ppermute(
            lax.slice_in_dim(block, block.shape[dim] - width, None, axis=dim), axis, forward
        )
        high = lax.ppermute(lax.slice_in_dim(block, 0, width, axis=dim), axis, backward)
        block = jnp.concatenate([low, block, high], axis=dim)
    return block


def gauss_taps(sigma, reach):
    raw = [math.exp(-(t * t) / (2.0 * sigma * sigma)) for t in range(-reach, reach + 1)]
    total = sum(raw)
    return [value / total for value in raw]


def slope_taps(sigma, reach):
    base = gauss_taps(sigma, reach)
    return [t * base[t + reach] / (sigma * sigma) for t in range(-reach, reach + 1)]


def correlate(values, taps, along):
    count = values.shape[along] - len(taps) + 1
    result = taps[0] * lax.slice_in_dim(values, 0, count, axis=along)
    for index in range(1, len(taps)):
        result = result + taps[index] * lax.slice_in_dim(values, index, index + count, axis=along)
    return result


def pad_x(values, width):
    return jnp.pad(values, ((0, 0), (0, 0), (width, width)))


def pair_index(first, second):
    low, high = (min(first, second), max(first, second))
    return pair_list.index((low, high))


def diffusion_tensor(parts):
    entry = {}
    for index in range(6):
        entry[pair_list[index]] = parts[index]
    ones = jnp.ones_like(parts[0])
    zeros = jnp.zeros_like(parts[0])
    basis = [[ones if row == col else zeros for col in range(3)] for row in range(3)]
    for sweep in range(SWEEPS):
        for first, second in ((0, 1), (0, 2), (1, 2)):
            third = 3 - first - second
            offdiag = entry[first, second]
            spread = entry[second, second] - entry[first, first]
            radius = jnp.sqrt(spread * spread + 4.0 * offdiag * offdiag + 1e-30)
            sign_part = jnp.where(spread >= 0.0, 1.0, -1.0)
            tangent = sign_part * 2.0 * offdiag / (jnp.abs(spread) + radius)
            cosine = 1.0 / jnp.sqrt(1.0 + tangent * tangent)
            sine = tangent * cosine
            entry[first, first] = entry[first, first] - tangent * offdiag
            entry[second, second] = entry[second, second] + tangent * offdiag
            entry[first, second] = zeros
            key_first = (min(third, first), max(third, first))
            key_second = (min(third, second), max(third, second))
            old_first = entry[key_first]
            old_second = entry[key_second]
            entry[key_first] = cosine * old_first - sine * old_second
            entry[key_second] = sine * old_first + cosine * old_second
            for row in range(3):
                left = basis[row][first]
                right = basis[row][second]
                basis[row][first] = cosine * left - sine * right
                basis[row][second] = sine * left + cosine * right
    eigen = [entry[0, 0], entry[1, 1], entry[2, 2]]
    top = jnp.maximum(jnp.maximum(eigen[0], eigen[1]), eigen[2])
    trace = eigen[0] + eigen[1] + eigen[2]
    gains = []
    for index in range(3):
        gap = top - eigen[index]
        gains.append(
            alpha_floor
            + (1.0 - alpha_floor) * gap * gap / (gap * gap + contrast * trace * trace + 1e-30)
        )
    result = []
    for first, second in pair_list:
        total = gains[0] * basis[first][0] * basis[second][0]
        total = total + gains[1] * basis[first][1] * basis[second][1]
        total = total + gains[2] * basis[first][2] * basis[second][2]
        result.append(total)
    return result


def inside_mask(shape, z_start, y_start, z_total, y_total):
    z = lax.broadcasted_iota(jnp.int32, shape, 0) + z_start
    y = lax.broadcasted_iota(jnp.int32, shape, 1) + y_start
    return (z >= 0) & (z < z_total) & (y >= 0) & (y < y_total)


def regroup(sections, halo):
    n_xy = lax.axis_size("xy")
    n_gz = lax.axis_size("gz")
    z_in, y_total, x_in = sections.shape
    y_block = y_total // n_xy
    z_total = z_in * n_xy
    z_block = z_total // n_gz
    halves = 2 if y_block % 2 == 0 and y_block // 2 >= halo else 1
    part_rows = y_block // halves
    grouped = sections.reshape(z_in, n_xy, y_block, x_in)
    parts = []
    for part in range(halves):
        piece = grouped[:, :, part * part_rows : (part + 1) * part_rows].reshape(z_in, n_xy * part_rows, x_in)
        column = lax.all_to_all(piece, "xy", split_axis=1, concat_axis=0, tiled=True)
        padded = jnp.pad(column, ((halo, halo), (0, 0), (0, 0)))
        windows = jnp.stack(
            [lax.slice_in_dim(padded, b * z_block, b * z_block + z_block + 2 * halo, axis=0) for b in range(n_gz)]
        )
        got = lax.all_to_all(windows, "gz", split_axis=0, concat_axis=0, tiled=True)
        got = jnp.transpose(got, (1, 2, 0, 3))
        parts.append(got.reshape(got.shape[:2] + (-1,)))
    forward = [(i, i + 1) for i in range(n_xy - 1)]
    backward = [(target, source) for source, target in forward]
    low = lax.ppermute(parts[-1][:, part_rows - halo :], "xy", forward)
    high = lax.ppermute(parts[0][:, :halo], "xy", backward)
    volume = jnp.concatenate([low] + parts + [high], axis=1)
    return lax.optimization_barrier(volume), z_total, y_total, z_block, y_block


def surround(block, width):

    def shifts(values, axis, dim):
        count = lax.axis_size(axis)
        forward = [(i, i + 1) for i in range(count - 1)]
        backward = [(target, source) for source, target in forward]
        size = values.shape[dim]
        low = lax.ppermute(lax.slice_in_dim(values, size - width, None, axis=dim), axis, forward)
        high = lax.ppermute(lax.slice_in_dim(values, 0, width, axis=dim), axis, backward)
        return low, high

    z_low, z_high = shifts(block, "gz", 1)
    y_low, y_high = shifts(block, "xy", 2)
    faces = jnp.concatenate([z_low, z_high], axis=1)
    corner_low, corner_high = shifts(faces, "xy", 2)
    rows = [
        jnp.concatenate([corner_low[:, :width], z_low, corner_high[:, :width]], axis=2),
        jnp.concatenate([y_low, block, y_high], axis=2),
        jnp.concatenate([corner_low[:, width:], z_high, corner_high[:, width:]], axis=2),
    ]
    return jnp.concatenate(rows, axis=1)


def shards(sections):
    halo = VOLUME_HALO
    volume, z_total, y_total, z_block, y_block = regroup(sections, halo)
    z0 = lax.axis_index("gz") * z_block
    y0 = lax.axis_index("xy") * y_block

    smooth = gauss_taps(sigma_noise, GRAD_REACH)
    slope = slope_taps(sigma_noise, GRAD_REACH)
    wide = gauss_taps(sigma_tensor, TENSOR_REACH)

    grads = []
    for component in range(3):
        values = volume
        for along in range(2):
            taps = slope if along == component else smooth
            values = correlate(values, taps, along)
        taps = slope if component == 2 else smooth
        values = correlate(pad_x(values, GRAD_REACH), taps, 2)
        grads.append(values)
    grad_ext = halo - GRAD_REACH
    inside = inside_mask(grads[0].shape, z0 - grad_ext, y0 - grad_ext, z_total, y_total)
    tensor = []
    for first, second in pair_list:
        values = jnp.where(inside, grads[first] * grads[second], 0.0)
        values = lax.slice_in_dim(values, grad_ext - TENSOR_REACH, values.shape[0] - grad_ext + TENSOR_REACH, axis=0)
        values = lax.slice_in_dim(values, grad_ext - TENSOR_REACH, values.shape[1] - grad_ext + TENSOR_REACH, axis=1)
        values = correlate(values, wide, 0)
        values = correlate(values, wide, 1)
        values = correlate(pad_x(values, TENSOR_REACH), wide, 2)
        tensor.append(values)
    parts = diffusion_tensor(tensor)
    stacked = jnp.stack(parts)
    stacked = surround(stacked, TENSOR_HALO)

    reach = 2 * STEPS
    field = volume[halo - reach : volume.shape[0] - halo + reach, halo - reach : volume.shape[1] - halo + reach]
    for segment in range(STEPS):
        ext = reach - 2 * segment
        cut = TENSOR_HALO - (ext - 1)
        local = [
            stacked[index, cut : stacked.shape[1] - cut, cut : stacked.shape[2] - cut]
            for index in range(6)
        ]
        wide_field = pad_x(field, 1)
        slopes = [
            (wide_field[2:, 1:-1, 1:-1] - wide_field[:-2, 1:-1, 1:-1]) * 0.5,
            (wide_field[1:-1, 2:, 1:-1] - wide_field[1:-1, :-2, 1:-1]) * 0.5,
            (wide_field[1:-1, 1:-1, 2:] - wide_field[1:-1, 1:-1, :-2]) * 0.5,
        ]
        fluxes = []
        for along in range(3):
            flux = local[pair_index(along, 0)] * slopes[0]
            flux = flux + local[pair_index(along, 1)] * slopes[1]
            flux = flux + local[pair_index(along, 2)] * slopes[2]
            fluxes.append(flux)
        flux_x = pad_x(fluxes[2], 1)
        total = (fluxes[0][2:, 1:-1] - fluxes[0][:-2, 1:-1]) * 0.5
        total = total + (fluxes[1][1:-1, 2:] - fluxes[1][1:-1, :-2]) * 0.5
        total = total + (flux_x[1:-1, 1:-1, 2:] - flux_x[1:-1, 1:-1, :-2]) * 0.5
        field = field[2:-2, 2:-2] + time_step * total
        if segment < STEPS - 1:
            new_ext = ext - 2
            inside = inside_mask(field.shape, z0 - new_ext, y0 - new_ext, z_total, y_total)
            field = jnp.where(inside, field, 0.0)
    return field


def solution(mesh):
    in_specs = (P("xy", None, "gz"),)
    out_specs = P("gz", "xy", None)
    return jax.shard_map(shards, mesh=mesh, in_specs=in_specs, out_specs=out_specs, check_vma=False)
```

```python
import math

import jax
import jax.numpy as jnp
from jax import lax
from jax.sharding import PartitionSpec as P

GRAD_REACH = 3
TENSOR_REACH = 4
SWEEPS = 4
STEPS = 3


sigma_noise = 1.0
sigma_tensor = 1.5
alpha_floor = 0.05
contrast = 0.05
time_step = 0.5
pair_list = ((0, 0), (1, 1), (2, 2), (0, 1), (0, 2), (1, 2))

VOLUME_HALO = max(GRAD_REACH + TENSOR_REACH, 2 * STEPS)
TENSOR_HALO = 2 * STEPS - 1


def extended_2(block, sides, width):
    for axis, dim in sides:
        count = lax.axis_size(axis)
        forward = [(i, i + 1) for i in range(count - 1)]
        backward = [(target, source) for source, target in forward]
        low = lax.ppermute(
            lax.slice_in_dim(block, block.shape[dim] - width, None, axis=dim), axis, forward
        )
        high = lax.ppermute(lax.slice_in_dim(block, 0, width, axis=dim), axis, backward)
        block = jnp.concatenate([low, block, high], axis=dim)
    return block


def gauss_taps(sigma, reach):
    raw = [math.exp(-(t * t) / (2.0 * sigma * sigma)) for t in range(-reach, reach + 1)]
    total = sum(raw)
    return [value / total for value in raw]


def slope_taps(sigma, reach):
    base = gauss_taps(sigma, reach)
    return [t * base[t + reach] / (sigma * sigma) for t in range(-reach, reach + 1)]


def correlate(values, taps, along):
    count = values.shape[along] - len(taps) + 1
    result = taps[0] * lax.slice_in_dim(values, 0, count, axis=along)
    for index in range(1, len(taps)):
        result = result + taps[index] * lax.slice_in_dim(values, index, index + count, axis=along)
    return result


def pad_x(values, width):
    return jnp.pad(values, ((0, 0), (0, 0), (width, width)))


def pair_index(first, second):
    low, high = (min(first, second), max(first, second))
    return pair_list.index((low, high))


def diffusion_tensor(parts):
    entry = {}
    for index in range(6):
        entry[pair_list[index]] = parts[index]
    ones = jnp.ones_like(parts[0])
    zeros = jnp.zeros_like(parts[0])
    basis = [[ones if row == col else zeros for col in range(3)] for row in range(3)]
    for sweep in range(SWEEPS):
        for first, second in ((0, 1), (0, 2), (1, 2)):
            third = 3 - first - second
            offdiag = entry[first, second]
            spread = entry[second, second] - entry[first, first]
            radius = jnp.sqrt(spread * spread + 4.0 * offdiag * offdiag + 1e-30)
            sign_part = jnp.where(spread >= 0.0, 1.0, -1.0)
            tangent = sign_part * 2.0 * offdiag / (jnp.abs(spread) + radius)
            cosine = 1.0 / jnp.sqrt(1.0 + tangent * tangent)
            sine = tangent * cosine
            entry[first, first] = entry[first, first] - tangent * offdiag
            entry[second, second] = entry[second, second] + tangent * offdiag
            entry[first, second] = zeros
            key_first = (min(third, first), max(third, first))
            key_second = (min(third, second), max(third, second))
            old_first = entry[key_first]
            old_second = entry[key_second]
            entry[key_first] = cosine * old_first - sine * old_second
            entry[key_second] = sine * old_first + cosine * old_second
            for row in range(3):
                left = basis[row][first]
                right = basis[row][second]
                basis[row][first] = cosine * left - sine * right
                basis[row][second] = sine * left + cosine * right
    eigen = [entry[0, 0], entry[1, 1], entry[2, 2]]
    top = jnp.maximum(jnp.maximum(eigen[0], eigen[1]), eigen[2])
    trace = eigen[0] + eigen[1] + eigen[2]
    gains = []
    for index in range(3):
        gap = top - eigen[index]
        gains.append(
            alpha_floor
            + (1.0 - alpha_floor) * gap * gap / (gap * gap + contrast * trace * trace + 1e-30)
        )
    result = []
    for first, second in pair_list:
        total = gains[0] * basis[first][0] * basis[second][0]
        total = total + gains[1] * basis[first][1] * basis[second][1]
        total = total + gains[2] * basis[first][2] * basis[second][2]
        result.append(total)
    return result


def inside_mask(shape, z_start, y_start, z_total, y_total):
    z = lax.broadcasted_iota(jnp.int32, shape, 0) + z_start
    y = lax.broadcasted_iota(jnp.int32, shape, 1) + y_start
    return (z >= 0) & (z < z_total) & (y >= 0) & (y < y_total)


def regroup(sections, halo):
    n_xy = lax.axis_size("xy")
    n_gz = lax.axis_size("gz")
    z_in, y_total, x_in = sections.shape
    y_block = y_total // n_xy
    z_total = z_in * n_xy
    z_block = z_total // n_gz
    halves = 2 if y_block % 2 == 0 and y_block // 2 >= halo else 1
    part_rows = y_block // halves
    grouped = sections.reshape(z_in, n_xy, y_block, x_in)
    parts = []
    for part in range(halves):
        piece = grouped[:, :, part * part_rows : (part + 1) * part_rows].reshape(z_in, n_xy * part_rows, x_in)
        column = lax.all_to_all(piece, "xy", split_axis=1, concat_axis=0, tiled=True)
        padded = jnp.pad(column, ((halo, halo), (0, 0), (0, 0)))
        windows = jnp.stack(
            [lax.slice_in_dim(padded, b * z_block, b * z_block + z_block + 2 * halo, axis=0) for b in range(n_gz)]
        )
        got = lax.all_to_all(windows, "gz", split_axis=0, concat_axis=0, tiled=True)
        got = jnp.transpose(got, (1, 2, 0, 3))
        parts.append(got.reshape(got.shape[:2] + (-1,)))
    forward = [(i, i + 1) for i in range(n_xy - 1)]
    backward = [(target, source) for source, target in forward]
    low = lax.ppermute(parts[-1][:, part_rows - halo :], "xy", forward)
    high = lax.ppermute(parts[0][:, :halo], "xy", backward)
    volume = jnp.concatenate([low] + parts + [high], axis=1)
    return lax.optimization_barrier(volume), z_total, y_total, z_block, y_block


def tensor_halo(tensor, width):
    z_block = tensor[0].shape[0]
    if z_block < 2 * width + 1:
        return surround(jnp.stack(diffusion_tensor(tensor)), width)
    edges = jnp.stack(
        diffusion_tensor([jnp.concatenate([item[:width], item[z_block - width :]], axis=0) for item in tensor])
    )
    top, bottom = lax.optimization_barrier((edges[:, width:], edges[:, :width]))
    z_low, z_high = z_faces(top, bottom)
    middle = jnp.stack(diffusion_tensor([item[width : z_block - width] for item in tensor]))
    block = jnp.concatenate([bottom, middle, top], axis=1)
    return assemble(block, z_low, z_high, width)


def z_faces(top, bottom):
    count = lax.axis_size("gz")
    forward = [(i, i + 1) for i in range(count - 1)]
    backward = [(target, source) for source, target in forward]
    return lax.ppermute(top, "gz", forward), lax.ppermute(bottom, "gz", backward)


def shifts(values, axis, dim, width):
    count = lax.axis_size(axis)
    forward = [(i, i + 1) for i in range(count - 1)]
    backward = [(target, source) for source, target in forward]
    size = values.shape[dim]
    low = lax.ppermute(lax.slice_in_dim(values, size - width, None, axis=dim), axis, forward)
    high = lax.ppermute(lax.slice_in_dim(values, 0, width, axis=dim), axis, backward)
    return low, high


def assemble(block, z_low, z_high, width):
    y_low, y_high = shifts(block, "xy", 2, width)
    faces = jnp.concatenate([z_low, z_high], axis=1)
    corner_low, corner_high = shifts(faces, "xy", 2, width)
    rows = [
        jnp.concatenate([corner_low[:, :width], z_low, corner_high[:, :width]], axis=2),
        jnp.concatenate([y_low, block, y_high], axis=2),
        jnp.concatenate([corner_low[:, width:], z_high, corner_high[:, width:]], axis=2),
    ]
    return jnp.concatenate(rows, axis=1)


def surround(block, width):
    z_block = block.shape[1]
    z_low, z_high = z_faces(block[:, z_block - width :], block[:, :width])
    return assemble(block, z_low, z_high, width)


def shards(sections):
    halo = VOLUME_HALO
    volume, z_total, y_total, z_block, y_block = regroup(sections, halo)
    z0 = lax.axis_index("gz") * z_block
    y0 = lax.axis_index("xy") * y_block

    smooth = gauss_taps(sigma_noise, GRAD_REACH)
    slope = slope_taps(sigma_noise, GRAD_REACH)
    wide = gauss_taps(sigma_tensor, TENSOR_REACH)

    grads = []
    for component in range(3):
        values = volume
        for along in range(2):
            taps = slope if along == component else smooth
            values = correlate(values, taps, along)
        taps = slope if component == 2 else smooth
        values = correlate(pad_x(values, GRAD_REACH), taps, 2)
        grads.append(values)
    grad_ext = halo - GRAD_REACH
    inside = inside_mask(grads[0].shape, z0 - grad_ext, y0 - grad_ext, z_total, y_total)
    tensor = []
    for first, second in pair_list:
        values = jnp.where(inside, grads[first] * grads[second], 0.0)
        values = lax.slice_in_dim(values, grad_ext - TENSOR_REACH, values.shape[0] - grad_ext + TENSOR_REACH, axis=0)
        values = lax.slice_in_dim(values, grad_ext - TENSOR_REACH, values.shape[1] - grad_ext + TENSOR_REACH, axis=1)
        values = correlate(values, wide, 0)
        values = correlate(values, wide, 1)
        values = correlate(pad_x(values, TENSOR_REACH), wide, 2)
        tensor.append(values)
    stacked = tensor_halo(lax.optimization_barrier(tensor), TENSOR_HALO)

    reach = 2 * STEPS
    field = volume[halo - reach : volume.shape[0] - halo + reach, halo - reach : volume.shape[1] - halo + reach]
    for segment in range(STEPS):
        ext = reach - 2 * segment
        cut = TENSOR_HALO - (ext - 1)
        local = [
            stacked[index, cut : stacked.shape[1] - cut, cut : stacked.shape[2] - cut]
            for index in range(6)
        ]
        wide_field = pad_x(field, 1)
        slopes = [
            (wide_field[2:, 1:-1, 1:-1] - wide_field[:-2, 1:-1, 1:-1]) * 0.5,
            (wide_field[1:-1, 2:, 1:-1] - wide_field[1:-1, :-2, 1:-1]) * 0.5,
            (wide_field[1:-1, 1:-1, 2:] - wide_field[1:-1, 1:-1, :-2]) * 0.5,
        ]
        fluxes = []
        for along in range(3):
            flux = local[pair_index(along, 0)] * slopes[0]
            flux = flux + local[pair_index(along, 1)] * slopes[1]
            flux = flux + local[pair_index(along, 2)] * slopes[2]
            fluxes.append(flux)
        flux_x = pad_x(fluxes[2], 1)
        total = (fluxes[0][2:, 1:-1] - fluxes[0][:-2, 1:-1]) * 0.5
        total = total + (fluxes[1][1:-1, 2:] - fluxes[1][1:-1, :-2]) * 0.5
        total = total + (flux_x[1:-1, 1:-1, 2:] - flux_x[1:-1, 1:-1, :-2]) * 0.5
        field = field[2:-2, 2:-2] + time_step * total
        if segment < STEPS - 1:
            new_ext = ext - 2
            inside = inside_mask(field.shape, z0 - new_ext, y0 - new_ext, z_total, y_total)
            field = jnp.where(inside, field, 0.0)
    return field


def solution(mesh):
    in_specs = (P("xy", None, "gz"),)
    out_specs = P("gz", "xy", None)
    return jax.shard_map(shards, mesh=mesh, in_specs=in_specs, out_specs=out_specs, check_vma=False)
```

```python
import math

import jax
import jax.numpy as jnp
from jax import lax
from jax.sharding import PartitionSpec as P

GRAD_REACH = 3
TENSOR_REACH = 4
SWEEPS = 4
STEPS = 3


sigma_noise = 1.0
sigma_tensor = 1.5
alpha_floor = 0.05
contrast = 0.05
time_step = 0.5
pair_list = ((0, 0), (1, 1), (2, 2), (0, 1), (0, 2), (1, 2))

VOLUME_HALO = max(GRAD_REACH + TENSOR_REACH, 2 * STEPS)
TENSOR_HALO = 2 * STEPS - 1


def extended_2(block, sides, width):
    for axis, dim in sides:
        count = lax.axis_size(axis)
        forward = [(i, i + 1) for i in range(count - 1)]
        backward = [(target, source) for source, target in forward]
        low = lax.ppermute(
            lax.slice_in_dim(block, block.shape[dim] - width, None, axis=dim), axis, forward
        )
        high = lax.ppermute(lax.slice_in_dim(block, 0, width, axis=dim), axis, backward)
        block = jnp.concatenate([low, block, high], axis=dim)
    return block


def gauss_taps(sigma, reach):
    raw = [math.exp(-(t * t) / (2.0 * sigma * sigma)) for t in range(-reach, reach + 1)]
    total = sum(raw)
    return [value / total for value in raw]


def slope_taps(sigma, reach):
    base = gauss_taps(sigma, reach)
    return [t * base[t + reach] / (sigma * sigma) for t in range(-reach, reach + 1)]


def correlate(values, taps, along):
    count = values.shape[along] - len(taps) + 1
    result = taps[0] * lax.slice_in_dim(values, 0, count, axis=along)
    for index in range(1, len(taps)):
        result = result + taps[index] * lax.slice_in_dim(values, index, index + count, axis=along)
    return result


def pad_x(values, width):
    return jnp.pad(values, ((0, 0), (0, 0), (width, width)))


def pair_index(first, second):
    low, high = (min(first, second), max(first, second))
    return pair_list.index((low, high))


def diffusion_tensor(parts):
    entry = {}
    for index in range(6):
        entry[pair_list[index]] = parts[index]
    ones = jnp.ones_like(parts[0])
    zeros = jnp.zeros_like(parts[0])
    basis = [[ones if row == col else zeros for col in range(3)] for row in range(3)]
    for sweep in range(SWEEPS):
        for first, second in ((0, 1), (0, 2), (1, 2)):
            third = 3 - first - second
            offdiag = entry[first, second]
            spread = entry[second, second] - entry[first, first]
            radius = jnp.sqrt(spread * spread + 4.0 * offdiag * offdiag + 1e-30)
            sign_part = jnp.where(spread >= 0.0, 1.0, -1.0)
            tangent = sign_part * 2.0 * offdiag / (jnp.abs(spread) + radius)
            cosine = 1.0 / jnp.sqrt(1.0 + tangent * tangent)
            sine = tangent * cosine
            entry[first, first] = entry[first, first] - tangent * offdiag
            entry[second, second] = entry[second, second] + tangent * offdiag
            entry[first, second] = zeros
            key_first = (min(third, first), max(third, first))
            key_second = (min(third, second), max(third, second))
            old_first = entry[key_first]
            old_second = entry[key_second]
            entry[key_first] = cosine * old_first - sine * old_second
            entry[key_second] = sine * old_first + cosine * old_second
            for row in range(3):
                left = basis[row][first]
                right = basis[row][second]
                basis[row][first] = cosine * left - sine * right
                basis[row][second] = sine * left + cosine * right
    eigen = [entry[0, 0], entry[1, 1], entry[2, 2]]
    top = jnp.maximum(jnp.maximum(eigen[0], eigen[1]), eigen[2])
    trace = eigen[0] + eigen[1] + eigen[2]
    gains = []
    for index in range(3):
        gap = top - eigen[index]
        gains.append(
            alpha_floor
            + (1.0 - alpha_floor) * gap * gap / (gap * gap + contrast * trace * trace + 1e-30)
        )
    result = []
    for first, second in pair_list:
        total = gains[0] * basis[first][0] * basis[second][0]
        total = total + gains[1] * basis[first][1] * basis[second][1]
        total = total + gains[2] * basis[first][2] * basis[second][2]
        result.append(total)
    return result


def inside_mask(shape, z_start, y_start, z_total, y_total):
    z = lax.broadcasted_iota(jnp.int32, shape, 0) + z_start
    y = lax.broadcasted_iota(jnp.int32, shape, 1) + y_start
    return (z >= 0) & (z < z_total) & (y >= 0) & (y < y_total)


def regroup(sections, halo):
    n_xy = lax.axis_size("xy")
    n_gz = lax.axis_size("gz")
    z_in, y_total, x_in = sections.shape
    y_block = y_total // n_xy
    z_total = z_in * n_xy
    z_block = z_total // n_gz
    halves = 2 if y_block % 2 == 0 and y_block // 2 >= halo else 1
    part_rows = y_block // halves
    grouped = sections.reshape(z_in, n_xy, y_block, x_in)
    parts = []
    for part in range(halves):
        piece = grouped[:, :, part * part_rows : (part + 1) * part_rows].reshape(z_in, n_xy * part_rows, x_in)
        column = lax.all_to_all(piece, "xy", split_axis=1, concat_axis=0, tiled=True)
        padded = jnp.pad(column, ((halo, halo), (0, 0), (0, 0)))
        windows = jnp.stack(
            [lax.slice_in_dim(padded, b * z_block, b * z_block + z_block + 2 * halo, axis=0) for b in range(n_gz)]
        )
        got = lax.all_to_all(windows, "gz", split_axis=0, concat_axis=0, tiled=True)
        got = jnp.transpose(got, (1, 2, 0, 3))
        parts.append(got.reshape(got.shape[:2] + (-1,)))
    forward = [(i, i + 1) for i in range(n_xy - 1)]
    backward = [(target, source) for source, target in forward]
    low = lax.ppermute(parts[-1][:, part_rows - halo :], "xy", forward)
    high = lax.ppermute(parts[0][:, :halo], "xy", backward)
    volume = jnp.concatenate([low] + parts + [high], axis=1)
    return lax.optimization_barrier(volume), z_total, y_total, z_block, y_block


def tensor_halo(tensor, width):
    z_block = tensor[0].shape[0]
    if z_block < 2 * width + 1:
        return surround(jnp.stack(diffusion_tensor(tensor)), width)
    edges = jnp.stack(
        diffusion_tensor([jnp.concatenate([item[:width], item[z_block - width :]], axis=0) for item in tensor])
    )
    top, bottom, edges = lax.optimization_barrier((edges[:, width:], edges[:, :width], edges))
    z_low, z_high = z_faces(top, bottom)
    side_low, side_high = shifts(edges, "xy", 2, width)
    upward = jnp.concatenate([side_low[:, width:], side_high[:, width:]], axis=2)
    downward = jnp.concatenate([side_low[:, :width], side_high[:, :width]], axis=2)
    corner_low, corner_high = z_faces(upward, downward)
    middle = jnp.stack(diffusion_tensor([item[width : z_block - width] for item in tensor]))
    block = jnp.concatenate([bottom, middle, top], axis=1)
    y_low, y_high = shifts(block, "xy", 2, width)
    rows = [
        jnp.concatenate([corner_low[:, :, :width], z_low, corner_low[:, :, width:]], axis=2),
        jnp.concatenate([y_low, block, y_high], axis=2),
        jnp.concatenate([corner_high[:, :, :width], z_high, corner_high[:, :, width:]], axis=2),
    ]
    return jnp.concatenate(rows, axis=1)


def z_faces(top, bottom):
    count = lax.axis_size("gz")
    forward = [(i, i + 1) for i in range(count - 1)]
    backward = [(target, source) for source, target in forward]
    return lax.ppermute(top, "gz", forward), lax.ppermute(bottom, "gz", backward)


def shifts(values, axis, dim, width):
    count = lax.axis_size(axis)
    forward = [(i, i + 1) for i in range(count - 1)]
    backward = [(target, source) for source, target in forward]
    size = values.shape[dim]
    low = lax.ppermute(lax.slice_in_dim(values, size - width, None, axis=dim), axis, forward)
    high = lax.ppermute(lax.slice_in_dim(values, 0, width, axis=dim), axis, backward)
    return low, high


def assemble(block, z_low, z_high, width):
    y_low, y_high = shifts(block, "xy", 2, width)
    faces = jnp.concatenate([z_low, z_high], axis=1)
    corner_low, corner_high = shifts(faces, "xy", 2, width)
    rows = [
        jnp.concatenate([corner_low[:, :width], z_low, corner_high[:, :width]], axis=2),
        jnp.concatenate([y_low, block, y_high], axis=2),
        jnp.concatenate([corner_low[:, width:], z_high, corner_high[:, width:]], axis=2),
    ]
    return jnp.concatenate(rows, axis=1)


def surround(block, width):
    z_block = block.shape[1]
    z_low, z_high = z_faces(block[:, z_block - width :], block[:, :width])
    return assemble(block, z_low, z_high, width)


def shards(sections):
    halo = VOLUME_HALO
    volume, z_total, y_total, z_block, y_block = regroup(sections, halo)
    z0 = lax.axis_index("gz") * z_block
    y0 = lax.axis_index("xy") * y_block

    smooth = gauss_taps(sigma_noise, GRAD_REACH)
    slope = slope_taps(sigma_noise, GRAD_REACH)
    wide = gauss_taps(sigma_tensor, TENSOR_REACH)

    grads = []
    for component in range(3):
        values = volume
        for along in range(2):
            taps = slope if along == component else smooth
            values = correlate(values, taps, along)
        taps = slope if component == 2 else smooth
        values = correlate(pad_x(values, GRAD_REACH), taps, 2)
        grads.append(values)
    grad_ext = halo - GRAD_REACH
    inside = inside_mask(grads[0].shape, z0 - grad_ext, y0 - grad_ext, z_total, y_total)
    tensor = []
    for first, second in pair_list:
        values = jnp.where(inside, grads[first] * grads[second], 0.0)
        values = lax.slice_in_dim(values, grad_ext - TENSOR_REACH, values.shape[0] - grad_ext + TENSOR_REACH, axis=0)
        values = lax.slice_in_dim(values, grad_ext - TENSOR_REACH, values.shape[1] - grad_ext + TENSOR_REACH, axis=1)
        values = correlate(values, wide, 0)
        values = correlate(values, wide, 1)
        values = correlate(pad_x(values, TENSOR_REACH), wide, 2)
        tensor.append(values)
    stacked = tensor_halo(lax.optimization_barrier(tensor), TENSOR_HALO)

    reach = 2 * STEPS
    field = volume[halo - reach : volume.shape[0] - halo + reach, halo - reach : volume.shape[1] - halo + reach]
    for segment in range(STEPS):
        ext = reach - 2 * segment
        cut = TENSOR_HALO - (ext - 1)
        local = [
            stacked[index, cut : stacked.shape[1] - cut, cut : stacked.shape[2] - cut]
            for index in range(6)
        ]
        wide_field = pad_x(field, 1)
        slopes = [
            (wide_field[2:, 1:-1, 1:-1] - wide_field[:-2, 1:-1, 1:-1]) * 0.5,
            (wide_field[1:-1, 2:, 1:-1] - wide_field[1:-1, :-2, 1:-1]) * 0.5,
            (wide_field[1:-1, 1:-1, 2:] - wide_field[1:-1, 1:-1, :-2]) * 0.5,
        ]
        fluxes = []
        for along in range(3):
            flux = local[pair_index(along, 0)] * slopes[0]
            flux = flux + local[pair_index(along, 1)] * slopes[1]
            flux = flux + local[pair_index(along, 2)] * slopes[2]
            fluxes.append(flux)
        flux_x = pad_x(fluxes[2], 1)
        total = (fluxes[0][2:, 1:-1] - fluxes[0][:-2, 1:-1]) * 0.5
        total = total + (fluxes[1][1:-1, 2:] - fluxes[1][1:-1, :-2]) * 0.5
        total = total + (flux_x[1:-1, 1:-1, 2:] - flux_x[1:-1, 1:-1, :-2]) * 0.5
        field = field[2:-2, 2:-2] + time_step * total
        if segment < STEPS - 1:
            new_ext = ext - 2
            inside = inside_mask(field.shape, z0 - new_ext, y0 - new_ext, z_total, y_total)
            field = jnp.where(inside, field, 0.0)
    return field


def solution(mesh):
    in_specs = (P("xy", None, "gz"),)
    out_specs = P("gz", "xy", None)
    return jax.shard_map(shards, mesh=mesh, in_specs=in_specs, out_specs=out_specs, check_vma=False)
```

```python
import math

import jax
import jax.numpy as jnp
from jax import lax
from jax.sharding import PartitionSpec as P

GRAD_REACH = 3
TENSOR_REACH = 4
SWEEPS = 4
STEPS = 3


sigma_noise = 1.0
sigma_tensor = 1.5
alpha_floor = 0.05
contrast = 0.05
time_step = 0.5
pair_list = ((0, 0), (1, 1), (2, 2), (0, 1), (0, 2), (1, 2))

VOLUME_HALO = max(GRAD_REACH + TENSOR_REACH, 2 * STEPS)
TENSOR_HALO = 2 * STEPS - 1


def extended_2(block, sides, width):
    for axis, dim in sides:
        count = lax.axis_size(axis)
        forward = [(i, i + 1) for i in range(count - 1)]
        backward = [(target, source) for source, target in forward]
        low = lax.ppermute(
            lax.slice_in_dim(block, block.shape[dim] - width, None, axis=dim), axis, forward
        )
        high = lax.ppermute(lax.slice_in_dim(block, 0, width, axis=dim), axis, backward)
        block = jnp.concatenate([low, block, high], axis=dim)
    return block


def gauss_taps(sigma, reach):
    raw = [math.exp(-(t * t) / (2.0 * sigma * sigma)) for t in range(-reach, reach + 1)]
    total = sum(raw)
    return [value / total for value in raw]


def slope_taps(sigma, reach):
    base = gauss_taps(sigma, reach)
    return [t * base[t + reach] / (sigma * sigma) for t in range(-reach, reach + 1)]


def correlate(values, taps, along):
    count = values.shape[along] - len(taps) + 1
    result = taps[0] * lax.slice_in_dim(values, 0, count, axis=along)
    for index in range(1, len(taps)):
        result = result + taps[index] * lax.slice_in_dim(values, index, index + count, axis=along)
    return result


def pad_x(values, width):
    return jnp.pad(values, ((0, 0), (0, 0), (width, width)))


def pair_index(first, second):
    low, high = (min(first, second), max(first, second))
    return pair_list.index((low, high))


def diffusion_tensor(parts):
    entry = {}
    for index in range(6):
        entry[pair_list[index]] = parts[index]
    ones = jnp.ones_like(parts[0])
    zeros = jnp.zeros_like(parts[0])
    basis = [[ones if row == col else zeros for col in range(3)] for row in range(3)]
    for sweep in range(SWEEPS):
        for first, second in ((0, 1), (0, 2), (1, 2)):
            third = 3 - first - second
            offdiag = entry[first, second]
            spread = entry[second, second] - entry[first, first]
            radius = jnp.sqrt(spread * spread + 4.0 * offdiag * offdiag + 1e-30)
            sign_part = jnp.where(spread >= 0.0, 1.0, -1.0)
            tangent = sign_part * 2.0 * offdiag / (jnp.abs(spread) + radius)
            cosine = 1.0 / jnp.sqrt(1.0 + tangent * tangent)
            sine = tangent * cosine
            entry[first, first] = entry[first, first] - tangent * offdiag
            entry[second, second] = entry[second, second] + tangent * offdiag
            entry[first, second] = zeros
            key_first = (min(third, first), max(third, first))
            key_second = (min(third, second), max(third, second))
            old_first = entry[key_first]
            old_second = entry[key_second]
            entry[key_first] = cosine * old_first - sine * old_second
            entry[key_second] = sine * old_first + cosine * old_second
            for row in range(3):
                left = basis[row][first]
                right = basis[row][second]
                basis[row][first] = cosine * left - sine * right
                basis[row][second] = sine * left + cosine * right
    eigen = [entry[0, 0], entry[1, 1], entry[2, 2]]
    top = jnp.maximum(jnp.maximum(eigen[0], eigen[1]), eigen[2])
    trace = eigen[0] + eigen[1] + eigen[2]
    gains = []
    for index in range(3):
        gap = top - eigen[index]
        gains.append(
            alpha_floor
            + (1.0 - alpha_floor) * gap * gap / (gap * gap + contrast * trace * trace + 1e-30)
        )
    result = []
    for first, second in pair_list:
        total = gains[0] * basis[first][0] * basis[second][0]
        total = total + gains[1] * basis[first][1] * basis[second][1]
        total = total + gains[2] * basis[first][2] * basis[second][2]
        result.append(total)
    return result


def inside_mask(shape, z_start, y_start, z_total, y_total):
    z = lax.broadcasted_iota(jnp.int32, shape, 0) + z_start
    y = lax.broadcasted_iota(jnp.int32, shape, 1) + y_start
    return (z >= 0) & (z < z_total) & (y >= 0) & (y < y_total)


def regroup(sections, halo):
    n_xy = lax.axis_size("xy")
    n_gz = lax.axis_size("gz")
    z_in, y_total, x_in = sections.shape
    y_block = y_total // n_xy
    z_total = z_in * n_xy
    z_block = z_total // n_gz
    halves = 2 if y_block % 2 == 0 and y_block // 2 >= halo else 1
    part_rows = y_block // halves
    whole = lax.all_to_all(sections, "xy", split_axis=1, concat_axis=0, tiled=True)
    parts = []
    for part in range(halves):
        column = whole[:, part * part_rows : (part + 1) * part_rows]
        padded = jnp.pad(column, ((halo, halo), (0, 0), (0, 0)))
        windows = jnp.stack(
            [lax.slice_in_dim(padded, b * z_block, b * z_block + z_block + 2 * halo, axis=0) for b in range(n_gz)]
        )
        got = lax.all_to_all(windows, "gz", split_axis=0, concat_axis=0, tiled=True)
        got = jnp.transpose(got, (1, 2, 0, 3))
        parts.append(got.reshape(got.shape[:2] + (-1,)))
    forward = [(i, i + 1) for i in range(n_xy - 1)]
    backward = [(target, source) for source, target in forward]
    low = lax.ppermute(parts[-1][:, part_rows - halo :], "xy", forward)
    high = lax.ppermute(parts[0][:, :halo], "xy", backward)
    volume = jnp.concatenate([low] + parts + [high], axis=1)
    return lax.optimization_barrier(volume), z_total, y_total, z_block, y_block


def tensor_halo(tensor, width):
    z_block = tensor[0].shape[0]
    if z_block < 2 * width + 1:
        return surround(jnp.stack(diffusion_tensor(tensor)), width)
    edges = jnp.stack(
        diffusion_tensor([jnp.concatenate([item[:width], item[z_block - width :]], axis=0) for item in tensor])
    )
    top, bottom = lax.optimization_barrier((edges[:, width:], edges[:, :width]))
    z_low, z_high = z_faces(top, bottom)
    middle = jnp.stack(diffusion_tensor([item[width : z_block - width] for item in tensor]))
    block = jnp.concatenate([bottom, middle, top], axis=1)
    return assemble(block, z_low, z_high, width)


def z_faces(top, bottom):
    count = lax.axis_size("gz")
    forward = [(i, i + 1) for i in range(count - 1)]
    backward = [(target, source) for source, target in forward]
    return lax.ppermute(top, "gz", forward), lax.ppermute(bottom, "gz", backward)


def shifts(values, axis, dim, width):
    count = lax.axis_size(axis)
    forward = [(i, i + 1) for i in range(count - 1)]
    backward = [(target, source) for source, target in forward]
    size = values.shape[dim]
    low = lax.ppermute(lax.slice_in_dim(values, size - width, None, axis=dim), axis, forward)
    high = lax.ppermute(lax.slice_in_dim(values, 0, width, axis=dim), axis, backward)
    return low, high


def assemble(block, z_low, z_high, width):
    y_low, y_high = shifts(block, "xy", 2, width)
    faces = jnp.concatenate([z_low, z_high], axis=1)
    corner_low, corner_high = shifts(faces, "xy", 2, width)
    rows = [
        jnp.concatenate([corner_low[:, :width], z_low, corner_high[:, :width]], axis=2),
        jnp.concatenate([y_low, block, y_high], axis=2),
        jnp.concatenate([corner_low[:, width:], z_high, corner_high[:, width:]], axis=2),
    ]
    return jnp.concatenate(rows, axis=1)


def surround(block, width):
    z_block = block.shape[1]
    z_low, z_high = z_faces(block[:, z_block - width :], block[:, :width])
    return assemble(block, z_low, z_high, width)


def shards(sections):
    halo = VOLUME_HALO
    volume, z_total, y_total, z_block, y_block = regroup(sections, halo)
    z0 = lax.axis_index("gz") * z_block
    y0 = lax.axis_index("xy") * y_block

    smooth = gauss_taps(sigma_noise, GRAD_REACH)
    slope = slope_taps(sigma_noise, GRAD_REACH)
    wide = gauss_taps(sigma_tensor, TENSOR_REACH)

    grads = []
    for component in range(3):
        values = volume
        for along in range(2):
            taps = slope if along == component else smooth
            values = correlate(values, taps, along)
        taps = slope if component == 2 else smooth
        values = correlate(pad_x(values, GRAD_REACH), taps, 2)
        grads.append(values)
    grad_ext = halo - GRAD_REACH
    inside = inside_mask(grads[0].shape, z0 - grad_ext, y0 - grad_ext, z_total, y_total)
    tensor = []
    for first, second in pair_list:
        values = jnp.where(inside, grads[first] * grads[second], 0.0)
        values = lax.slice_in_dim(values, grad_ext - TENSOR_REACH, values.shape[0] - grad_ext + TENSOR_REACH, axis=0)
        values = lax.slice_in_dim(values, grad_ext - TENSOR_REACH, values.shape[1] - grad_ext + TENSOR_REACH, axis=1)
        values = correlate(values, wide, 0)
        values = correlate(values, wide, 1)
        values = correlate(pad_x(values, TENSOR_REACH), wide, 2)
        tensor.append(values)
    stacked = tensor_halo(lax.optimization_barrier(tensor), TENSOR_HALO)

    reach = 2 * STEPS
    field = volume[halo - reach : volume.shape[0] - halo + reach, halo - reach : volume.shape[1] - halo + reach]
    for segment in range(STEPS):
        ext = reach - 2 * segment
        cut = TENSOR_HALO - (ext - 1)
        local = [
            stacked[index, cut : stacked.shape[1] - cut, cut : stacked.shape[2] - cut]
            for index in range(6)
        ]
        wide_field = pad_x(field, 1)
        slopes = [
            (wide_field[2:, 1:-1, 1:-1] - wide_field[:-2, 1:-1, 1:-1]) * 0.5,
            (wide_field[1:-1, 2:, 1:-1] - wide_field[1:-1, :-2, 1:-1]) * 0.5,
            (wide_field[1:-1, 1:-1, 2:] - wide_field[1:-1, 1:-1, :-2]) * 0.5,
        ]
        fluxes = []
        for along in range(3):
            flux = local[pair_index(along, 0)] * slopes[0]
            flux = flux + local[pair_index(along, 1)] * slopes[1]
            flux = flux + local[pair_index(along, 2)] * slopes[2]
            fluxes.append(flux)
        flux_x = pad_x(fluxes[2], 1)
        total = (fluxes[0][2:, 1:-1] - fluxes[0][:-2, 1:-1]) * 0.5
        total = total + (fluxes[1][1:-1, 2:] - fluxes[1][1:-1, :-2]) * 0.5
        total = total + (flux_x[1:-1, 1:-1, 2:] - flux_x[1:-1, 1:-1, :-2]) * 0.5
        field = field[2:-2, 2:-2] + time_step * total
        if segment < STEPS - 1:
            new_ext = ext - 2
            inside = inside_mask(field.shape, z0 - new_ext, y0 - new_ext, z_total, y_total)
            field = jnp.where(inside, field, 0.0)
    return field


def solution(mesh):
    in_specs = (P("xy", None, "gz"),)
    out_specs = P("gz", "xy", None)
    return jax.shard_map(shards, mesh=mesh, in_specs=in_specs, out_specs=out_specs, check_vma=False)
```

```python
import math

import jax
import jax.numpy as jnp
from jax import lax
from jax.sharding import PartitionSpec as P

GRAD_REACH = 3
TENSOR_REACH = 4
SWEEPS = 4
STEPS = 3


sigma_noise = 1.0
sigma_tensor = 1.5
alpha_floor = 0.05
contrast = 0.05
time_step = 0.5
pair_list = ((0, 0), (1, 1), (2, 2), (0, 1), (0, 2), (1, 2))

VOLUME_HALO = max(GRAD_REACH + TENSOR_REACH, 2 * STEPS)
TENSOR_HALO = 2 * STEPS - 1


def extended_2(block, sides, width):
    for axis, dim in sides:
        count = lax.axis_size(axis)
        forward = [(i, i + 1) for i in range(count - 1)]
        backward = [(target, source) for source, target in forward]
        low = lax.ppermute(
            lax.slice_in_dim(block, block.shape[dim] - width, None, axis=dim), axis, forward
        )
        high = lax.ppermute(lax.slice_in_dim(block, 0, width, axis=dim), axis, backward)
        block = jnp.concatenate([low, block, high], axis=dim)
    return block


def gauss_taps(sigma, reach):
    raw = [math.exp(-(t * t) / (2.0 * sigma * sigma)) for t in range(-reach, reach + 1)]
    total = sum(raw)
    return [value / total for value in raw]


def slope_taps(sigma, reach):
    base = gauss_taps(sigma, reach)
    return [t * base[t + reach] / (sigma * sigma) for t in range(-reach, reach + 1)]


def correlate(values, taps, along):
    count = values.shape[along] - len(taps) + 1
    result = taps[0] * lax.slice_in_dim(values, 0, count, axis=along)
    for index in range(1, len(taps)):
        result = result + taps[index] * lax.slice_in_dim(values, index, index + count, axis=along)
    return result


def pad_x(values, width):
    return jnp.pad(values, ((0, 0), (0, 0), (width, width)))


def pair_index(first, second):
    low, high = (min(first, second), max(first, second))
    return pair_list.index((low, high))


def diffusion_tensor(parts):
    entry = {}
    for index in range(6):
        entry[pair_list[index]] = parts[index]
    ones = jnp.ones_like(parts[0])
    zeros = jnp.zeros_like(parts[0])
    basis = [[ones if row == col else zeros for col in range(3)] for row in range(3)]
    for sweep in range(SWEEPS):
        for first, second in ((0, 1), (0, 2), (1, 2)):
            third = 3 - first - second
            offdiag = entry[first, second]
            spread = entry[second, second] - entry[first, first]
            radius = jnp.sqrt(spread * spread + 4.0 * offdiag * offdiag + 1e-30)
            sign_part = jnp.where(spread >= 0.0, 1.0, -1.0)
            tangent = sign_part * 2.0 * offdiag / (jnp.abs(spread) + radius)
            cosine = 1.0 / jnp.sqrt(1.0 + tangent * tangent)
            sine = tangent * cosine
            entry[first, first] = entry[first, first] - tangent * offdiag
            entry[second, second] = entry[second, second] + tangent * offdiag
            entry[first, second] = zeros
            key_first = (min(third, first), max(third, first))
            key_second = (min(third, second), max(third, second))
            old_first = entry[key_first]
            old_second = entry[key_second]
            entry[key_first] = cosine * old_first - sine * old_second
            entry[key_second] = sine * old_first + cosine * old_second
            for row in range(3):
                left = basis[row][first]
                right = basis[row][second]
                basis[row][first] = cosine * left - sine * right
                basis[row][second] = sine * left + cosine * right
    eigen = [entry[0, 0], entry[1, 1], entry[2, 2]]
    top = jnp.maximum(jnp.maximum(eigen[0], eigen[1]), eigen[2])
    trace = eigen[0] + eigen[1] + eigen[2]
    gains = []
    for index in range(3):
        gap = top - eigen[index]
        gains.append(
            alpha_floor
            + (1.0 - alpha_floor) * gap * gap / (gap * gap + contrast * trace * trace + 1e-30)
        )
    result = []
    for first, second in pair_list:
        total = gains[0] * basis[first][0] * basis[second][0]
        total = total + gains[1] * basis[first][1] * basis[second][1]
        total = total + gains[2] * basis[first][2] * basis[second][2]
        result.append(total)
    return result


def inside_mask(shape, z_start, y_start, z_total, y_total):
    z = lax.broadcasted_iota(jnp.int32, shape, 0) + z_start
    y = lax.broadcasted_iota(jnp.int32, shape, 1) + y_start
    return (z >= 0) & (z < z_total) & (y >= 0) & (y < y_total)


def regroup(sections, halo):
    n_xy = lax.axis_size("xy")
    n_gz = lax.axis_size("gz")
    z_in, y_total, x_in = sections.shape
    y_block = y_total // n_xy
    z_total = z_in * n_xy
    z_block = z_total // n_gz
    grouped = sections.reshape(z_in, n_xy, y_block, x_in)
    if y_block > 2 * halo:
        row_sets = [
            jnp.concatenate([grouped[:, :, :halo], grouped[:, :, y_block - halo :]], axis=2),
            grouped[:, :, halo : y_block - halo],
        ]
    else:
        row_sets = [grouped]
    parts = []
    for rows in row_sets:
        piece = rows.reshape(z_in, -1, x_in)
        column = lax.all_to_all(piece, "xy", split_axis=1, concat_axis=0, tiled=True)
        padded = jnp.pad(column, ((halo, halo), (0, 0), (0, 0)))
        windows = jnp.stack(
            [lax.slice_in_dim(padded, b * z_block, b * z_block + z_block + 2 * halo, axis=0) for b in range(n_gz)]
        )
        got = lax.all_to_all(windows, "gz", split_axis=0, concat_axis=0, tiled=True)
        got = jnp.transpose(got, (1, 2, 0, 3))
        parts.append(got.reshape(got.shape[:2] + (-1,)))
    edges = parts[0]
    forward = [(i, i + 1) for i in range(n_xy - 1)]
    backward = [(target, source) for source, target in forward]
    low = lax.ppermute(edges[:, edges.shape[1] - halo :], "xy", forward)
    high = lax.ppermute(edges[:, :halo], "xy", backward)
    if len(parts) > 1:
        middle = [edges[:, :halo], parts[1], edges[:, halo:]]
    else:
        middle = [edges]
    volume = jnp.concatenate([low] + middle + [high], axis=1)
    return lax.optimization_barrier(volume), z_total, y_total, z_block, y_block


def tensor_halo(tensor, width):
    z_block = tensor[0].shape[0]
    if z_block < 2 * width + 1:
        return surround(jnp.stack(diffusion_tensor(tensor)), width)
    edges = jnp.stack(
        diffusion_tensor([jnp.concatenate([item[:width], item[z_block - width :]], axis=0) for item in tensor])
    )
    top, bottom = lax.optimization_barrier((edges[:, width:], edges[:, :width]))
    z_low, z_high = z_faces(top, bottom)
    middle = jnp.stack(diffusion_tensor([item[width : z_block - width] for item in tensor]))
    block = jnp.concatenate([bottom, middle, top], axis=1)
    return assemble(block, z_low, z_high, width)


def z_faces(top, bottom):
    count = lax.axis_size("gz")
    forward = [(i, i + 1) for i in range(count - 1)]
    backward = [(target, source) for source, target in forward]
    return lax.ppermute(top, "gz", forward), lax.ppermute(bottom, "gz", backward)


def shifts(values, axis, dim, width):
    count = lax.axis_size(axis)
    forward = [(i, i + 1) for i in range(count - 1)]
    backward = [(target, source) for source, target in forward]
    size = values.shape[dim]
    low = lax.ppermute(lax.slice_in_dim(values, size - width, None, axis=dim), axis, forward)
    high = lax.ppermute(lax.slice_in_dim(values, 0, width, axis=dim), axis, backward)
    return low, high


def assemble(block, z_low, z_high, width):
    y_low, y_high = shifts(block, "xy", 2, width)
    faces = jnp.concatenate([z_low, z_high], axis=1)
    corner_low, corner_high = shifts(faces, "xy", 2, width)
    rows = [
        jnp.concatenate([corner_low[:, :width], z_low, corner_high[:, :width]], axis=2),
        jnp.concatenate([y_low, block, y_high], axis=2),
        jnp.concatenate([corner_low[:, width:], z_high, corner_high[:, width:]], axis=2),
    ]
    return jnp.concatenate(rows, axis=1)


def surround(block, width):
    z_block = block.shape[1]
    z_low, z_high = z_faces(block[:, z_block - width :], block[:, :width])
    return assemble(block, z_low, z_high, width)


def shards(sections):
    halo = VOLUME_HALO
    volume, z_total, y_total, z_block, y_block = regroup(sections, halo)
    z0 = lax.axis_index("gz") * z_block
    y0 = lax.axis_index("xy") * y_block

    smooth = gauss_taps(sigma_noise, GRAD_REACH)
    slope = slope_taps(sigma_noise, GRAD_REACH)
    wide = gauss_taps(sigma_tensor, TENSOR_REACH)

    grads = []
    for component in range(3):
        values = volume
        for along in range(2):
            taps = slope if along == component else smooth
            values = correlate(values, taps, along)
        taps = slope if component == 2 else smooth
        values = correlate(pad_x(values, GRAD_REACH), taps, 2)
        grads.append(values)
    grad_ext = halo - GRAD_REACH
    inside = inside_mask(grads[0].shape, z0 - grad_ext, y0 - grad_ext, z_total, y_total)
    tensor = []
    for first, second in pair_list:
        values = jnp.where(inside, grads[first] * grads[second], 0.0)
        values = lax.slice_in_dim(values, grad_ext - TENSOR_REACH, values.shape[0] - grad_ext + TENSOR_REACH, axis=0)
        values = lax.slice_in_dim(values, grad_ext - TENSOR_REACH, values.shape[1] - grad_ext + TENSOR_REACH, axis=1)
        values = correlate(values, wide, 0)
        values = correlate(values, wide, 1)
        values = correlate(pad_x(values, TENSOR_REACH), wide, 2)
        tensor.append(values)
    stacked = tensor_halo(lax.optimization_barrier(tensor), TENSOR_HALO)

    reach = 2 * STEPS
    field = volume[halo - reach : volume.shape[0] - halo + reach, halo - reach : volume.shape[1] - halo + reach]
    for segment in range(STEPS):
        ext = reach - 2 * segment
        cut = TENSOR_HALO - (ext - 1)
        local = [
            stacked[index, cut : stacked.shape[1] - cut, cut : stacked.shape[2] - cut]
            for index in range(6)
        ]
        wide_field = pad_x(field, 1)
        slopes = [
            (wide_field[2:, 1:-1, 1:-1] - wide_field[:-2, 1:-1, 1:-1]) * 0.5,
            (wide_field[1:-1, 2:, 1:-1] - wide_field[1:-1, :-2, 1:-1]) * 0.5,
            (wide_field[1:-1, 1:-1, 2:] - wide_field[1:-1, 1:-1, :-2]) * 0.5,
        ]
        fluxes = []
        for along in range(3):
            flux = local[pair_index(along, 0)] * slopes[0]
            flux = flux + local[pair_index(along, 1)] * slopes[1]
            flux = flux + local[pair_index(along, 2)] * slopes[2]
            fluxes.append(flux)
        flux_x = pad_x(fluxes[2], 1)
        total = (fluxes[0][2:, 1:-1] - fluxes[0][:-2, 1:-1]) * 0.5
        total = total + (fluxes[1][1:-1, 2:] - fluxes[1][1:-1, :-2]) * 0.5
        total = total + (flux_x[1:-1, 1:-1, 2:] - flux_x[1:-1, 1:-1, :-2]) * 0.5
        field = field[2:-2, 2:-2] + time_step * total
        if segment < STEPS - 1:
            new_ext = ext - 2
            inside = inside_mask(field.shape, z0 - new_ext, y0 - new_ext, z_total, y_total)
            field = jnp.where(inside, field, 0.0)
    return field


def solution(mesh):
    in_specs = (P("xy", None, "gz"),)
    out_specs = P("gz", "xy", None)
    return jax.shard_map(shards, mesh=mesh, in_specs=in_specs, out_specs=out_specs, check_vma=False)
```

```python
import math

import jax
import jax.numpy as jnp
from jax import lax
from jax.sharding import PartitionSpec as P

GRAD_REACH = 3
TENSOR_REACH = 4
SWEEPS = 4
STEPS = 3


sigma_noise = 1.0
sigma_tensor = 1.5
alpha_floor = 0.05
contrast = 0.05
time_step = 0.5
pair_list = ((0, 0), (1, 1), (2, 2), (0, 1), (0, 2), (1, 2))

VOLUME_HALO = max(GRAD_REACH + TENSOR_REACH, 2 * STEPS)
TENSOR_HALO = 2 * STEPS - 1


def extended_2(block, sides, width):
    for axis, dim in sides:
        count = lax.axis_size(axis)
        forward = [(i, i + 1) for i in range(count - 1)]
        backward = [(target, source) for source, target in forward]
        low = lax.ppermute(
            lax.slice_in_dim(block, block.shape[dim] - width, None, axis=dim), axis, forward
        )
        high = lax.ppermute(lax.slice_in_dim(block, 0, width, axis=dim), axis, backward)
        block = jnp.concatenate([low, block, high], axis=dim)
    return block


def gauss_taps(sigma, reach):
    raw = [math.exp(-(t * t) / (2.0 * sigma * sigma)) for t in range(-reach, reach + 1)]
    total = sum(raw)
    return [value / total for value in raw]


def slope_taps(sigma, reach):
    base = gauss_taps(sigma, reach)
    return [t * base[t + reach] / (sigma * sigma) for t in range(-reach, reach + 1)]


def correlate(values, taps, along):
    count = values.shape[along] - len(taps) + 1
    result = taps[0] * lax.slice_in_dim(values, 0, count, axis=along)
    for index in range(1, len(taps)):
        result = result + taps[index] * lax.slice_in_dim(values, index, index + count, axis=along)
    return result


def pad_x(values, width):
    return jnp.pad(values, ((0, 0), (0, 0), (width, width)))


def pair_index(first, second):
    low, high = (min(first, second), max(first, second))
    return pair_list.index((low, high))


def diffusion_tensor(parts):
    entry = {}
    for index in range(6):
        entry[pair_list[index]] = parts[index]
    ones = jnp.ones_like(parts[0])
    zeros = jnp.zeros_like(parts[0])
    basis = [[ones if row == col else zeros for col in range(3)] for row in range(3)]
    for sweep in range(SWEEPS):
        for first, second in ((0, 1), (0, 2), (1, 2)):
            third = 3 - first - second
            offdiag = entry[first, second]
            spread = entry[second, second] - entry[first, first]
            radius = jnp.sqrt(spread * spread + 4.0 * offdiag * offdiag + 1e-30)
            sign_part = jnp.where(spread >= 0.0, 1.0, -1.0)
            tangent = sign_part * 2.0 * offdiag / (jnp.abs(spread) + radius)
            cosine = 1.0 / jnp.sqrt(1.0 + tangent * tangent)
            sine = tangent * cosine
            entry[first, first] = entry[first, first] - tangent * offdiag
            entry[second, second] = entry[second, second] + tangent * offdiag
            entry[first, second] = zeros
            key_first = (min(third, first), max(third, first))
            key_second = (min(third, second), max(third, second))
            old_first = entry[key_first]
            old_second = entry[key_second]
            entry[key_first] = cosine * old_first - sine * old_second
            entry[key_second] = sine * old_first + cosine * old_second
            for row in range(3):
                left = basis[row][first]
                right = basis[row][second]
                basis[row][first] = cosine * left - sine * right
                basis[row][second] = sine * left + cosine * right
    eigen = [entry[0, 0], entry[1, 1], entry[2, 2]]
    top = jnp.maximum(jnp.maximum(eigen[0], eigen[1]), eigen[2])
    trace = eigen[0] + eigen[1] + eigen[2]
    gains = []
    for index in range(3):
        gap = top - eigen[index]
        gains.append(
            alpha_floor
            + (1.0 - alpha_floor) * gap * gap / (gap * gap + contrast * trace * trace + 1e-30)
        )
    result = []
    for first, second in pair_list:
        total = gains[0] * basis[first][0] * basis[second][0]
        total = total + gains[1] * basis[first][1] * basis[second][1]
        total = total + gains[2] * basis[first][2] * basis[second][2]
        result.append(total)
    return result


def inside_mask(shape, z_start, y_start, z_total, y_total):
    z = lax.broadcasted_iota(jnp.int32, shape, 0) + z_start
    y = lax.broadcasted_iota(jnp.int32, shape, 1) + y_start
    return (z >= 0) & (z < z_total) & (y >= 0) & (y < y_total)


def regroup(sections, halo):
    n_xy = lax.axis_size("xy")
    n_gz = lax.axis_size("gz")
    z_in, y_total, x_in = sections.shape
    y_block = y_total // n_xy
    z_total = z_in * n_xy
    z_block = z_total // n_gz
    grouped = sections.reshape(z_in, n_xy, y_block, x_in)
    if y_block > 2 * halo:
        row_sets = [
            jnp.concatenate([grouped[:, :, :halo], grouped[:, :, y_block - halo :]], axis=2),
            grouped[:, :, halo : y_block - halo],
        ]
    else:
        row_sets = [grouped]
    parts = []
    for rows in row_sets:
        piece = rows.reshape(z_in, -1, x_in)
        column = lax.all_to_all(piece, "xy", split_axis=1, concat_axis=0, tiled=True)
        padded = jnp.pad(column, ((halo, halo), (0, 0), (0, 0)))
        windows = jnp.stack(
            [lax.slice_in_dim(padded, b * z_block, b * z_block + z_block + 2 * halo, axis=0) for b in range(n_gz)]
        )
        got = lax.all_to_all(windows, "gz", split_axis=0, concat_axis=0, tiled=True)
        got = jnp.transpose(got, (1, 2, 0, 3))
        parts.append(got.reshape(got.shape[:2] + (-1,)))
    edges = parts[0]
    forward = [(i, i + 1) for i in range(n_xy - 1)]
    backward = [(target, source) for source, target in forward]
    low = lax.ppermute(edges[:, edges.shape[1] - halo :], "xy", forward)
    high = lax.ppermute(edges[:, :halo], "xy", backward)
    if len(parts) > 1:
        middle = [edges[:, :halo], parts[1], edges[:, halo:]]
    else:
        middle = [edges]
    volume = jnp.concatenate([low] + middle + [high], axis=1)
    return lax.optimization_barrier(volume), z_total, y_total, z_block, y_block


def tensor_halo(tensor, width):
    z_block = tensor[0].shape[0]
    if z_block < 2 * width + 1:
        return surround(jnp.stack(diffusion_tensor(tensor)), width)
    edges = jnp.stack(
        diffusion_tensor([jnp.concatenate([item[:width], item[z_block - width :]], axis=0) for item in tensor])
    )
    top, bottom = lax.optimization_barrier((edges[:, width:], edges[:, :width]))
    z_low, z_high = z_faces(top, bottom)
    middle = jnp.stack(diffusion_tensor([item[width : z_block - width] for item in tensor]))
    tall = jnp.concatenate([z_low, bottom, middle, top, z_high], axis=1)
    y_low, y_high = shifts(tall, "xy", 2, width)
    return jnp.concatenate([y_low, tall, y_high], axis=2)


def z_faces(top, bottom):
    count = lax.axis_size("gz")
    forward = [(i, i + 1) for i in range(count - 1)]
    backward = [(target, source) for source, target in forward]
    return lax.ppermute(top, "gz", forward), lax.ppermute(bottom, "gz", backward)


def shifts(values, axis, dim, width):
    count = lax.axis_size(axis)
    forward = [(i, i + 1) for i in range(count - 1)]
    backward = [(target, source) for source, target in forward]
    size = values.shape[dim]
    low = lax.ppermute(lax.slice_in_dim(values, size - width, None, axis=dim), axis, forward)
    high = lax.ppermute(lax.slice_in_dim(values, 0, width, axis=dim), axis, backward)
    return low, high


def assemble(block, z_low, z_high, width):
    y_low, y_high = shifts(block, "xy", 2, width)
    faces = jnp.concatenate([z_low, z_high], axis=1)
    corner_low, corner_high = shifts(faces, "xy", 2, width)
    rows = [
        jnp.concatenate([corner_low[:, :width], z_low, corner_high[:, :width]], axis=2),
        jnp.concatenate([y_low, block, y_high], axis=2),
        jnp.concatenate([corner_low[:, width:], z_high, corner_high[:, width:]], axis=2),
    ]
    return jnp.concatenate(rows, axis=1)


def surround(block, width):
    z_block = block.shape[1]
    z_low, z_high = z_faces(block[:, z_block - width :], block[:, :width])
    return assemble(block, z_low, z_high, width)


def shards(sections):
    halo = VOLUME_HALO
    volume, z_total, y_total, z_block, y_block = regroup(sections, halo)
    z0 = lax.axis_index("gz") * z_block
    y0 = lax.axis_index("xy") * y_block

    smooth = gauss_taps(sigma_noise, GRAD_REACH)
    slope = slope_taps(sigma_noise, GRAD_REACH)
    wide = gauss_taps(sigma_tensor, TENSOR_REACH)

    grads = []
    for component in range(3):
        values = volume
        for along in range(2):
            taps = slope if along == component else smooth
            values = correlate(values, taps, along)
        taps = slope if component == 2 else smooth
        values = correlate(pad_x(values, GRAD_REACH), taps, 2)
        grads.append(values)
    grad_ext = halo - GRAD_REACH
    inside = inside_mask(grads[0].shape, z0 - grad_ext, y0 - grad_ext, z_total, y_total)
    tensor = []
    for first, second in pair_list:
        values = jnp.where(inside, grads[first] * grads[second], 0.0)
        values = lax.slice_in_dim(values, grad_ext - TENSOR_REACH, values.shape[0] - grad_ext + TENSOR_REACH, axis=0)
        values = lax.slice_in_dim(values, grad_ext - TENSOR_REACH, values.shape[1] - grad_ext + TENSOR_REACH, axis=1)
        values = correlate(values, wide, 0)
        values = correlate(values, wide, 1)
        values = correlate(pad_x(values, TENSOR_REACH), wide, 2)
        tensor.append(values)
    stacked = tensor_halo(lax.optimization_barrier(tensor), TENSOR_HALO)

    reach = 2 * STEPS
    field = volume[halo - reach : volume.shape[0] - halo + reach, halo - reach : volume.shape[1] - halo + reach]
    for segment in range(STEPS):
        ext = reach - 2 * segment
        cut = TENSOR_HALO - (ext - 1)
        local = [
            stacked[index, cut : stacked.shape[1] - cut, cut : stacked.shape[2] - cut]
            for index in range(6)
        ]
        wide_field = pad_x(field, 1)
        slopes = [
            (wide_field[2:, 1:-1, 1:-1] - wide_field[:-2, 1:-1, 1:-1]) * 0.5,
            (wide_field[1:-1, 2:, 1:-1] - wide_field[1:-1, :-2, 1:-1]) * 0.5,
            (wide_field[1:-1, 1:-1, 2:] - wide_field[1:-1, 1:-1, :-2]) * 0.5,
        ]
        fluxes = []
        for along in range(3):
            flux = local[pair_index(along, 0)] * slopes[0]
            flux = flux + local[pair_index(along, 1)] * slopes[1]
            flux = flux + local[pair_index(along, 2)] * slopes[2]
            fluxes.append(flux)
        flux_x = pad_x(fluxes[2], 1)
        total = (fluxes[0][2:, 1:-1] - fluxes[0][:-2, 1:-1]) * 0.5
        total = total + (fluxes[1][1:-1, 2:] - fluxes[1][1:-1, :-2]) * 0.5
        total = total + (flux_x[1:-1, 1:-1, 2:] - flux_x[1:-1, 1:-1, :-2]) * 0.5
        field = field[2:-2, 2:-2] + time_step * total
        if segment < STEPS - 1:
            new_ext = ext - 2
            inside = inside_mask(field.shape, z0 - new_ext, y0 - new_ext, z_total, y_total)
            field = jnp.where(inside, field, 0.0)
    return field


def solution(mesh):
    in_specs = (P("xy", None, "gz"),)
    out_specs = P("gz", "xy", None)
    return jax.shard_map(shards, mesh=mesh, in_specs=in_specs, out_specs=out_specs, check_vma=False)
```

```python
import math

import jax
import jax.numpy as jnp
from jax import lax
from jax.sharding import PartitionSpec as P

GRAD_REACH = 3
TENSOR_REACH = 4
SWEEPS = 4
STEPS = 3


sigma_noise = 1.0
sigma_tensor = 1.5
alpha_floor = 0.05
contrast = 0.05
time_step = 0.5
pair_list = ((0, 0), (1, 1), (2, 2), (0, 1), (0, 2), (1, 2))

VOLUME_HALO = max(GRAD_REACH + TENSOR_REACH, 2 * STEPS)
TENSOR_HALO = 2 * STEPS - 1


def extended_2(block, sides, width):
    for axis, dim in sides:
        count = lax.axis_size(axis)
        forward = [(i, i + 1) for i in range(count - 1)]
        backward = [(target, source) for source, target in forward]
        low = lax.ppermute(
            lax.slice_in_dim(block, block.shape[dim] - width, None, axis=dim), axis, forward
        )
        high = lax.ppermute(lax.slice_in_dim(block, 0, width, axis=dim), axis, backward)
        block = jnp.concatenate([low, block, high], axis=dim)
    return block


def gauss_taps(sigma, reach):
    raw = [math.exp(-(t * t) / (2.0 * sigma * sigma)) for t in range(-reach, reach + 1)]
    total = sum(raw)
    return [value / total for value in raw]


def slope_taps(sigma, reach):
    base = gauss_taps(sigma, reach)
    return [t * base[t + reach] / (sigma * sigma) for t in range(-reach, reach + 1)]


def correlate(values, taps, along):
    count = values.shape[along] - len(taps) + 1
    result = taps[0] * lax.slice_in_dim(values, 0, count, axis=along)
    for index in range(1, len(taps)):
        result = result + taps[index] * lax.slice_in_dim(values, index, index + count, axis=along)
    return result


def pad_x(values, width):
    return jnp.pad(values, ((0, 0), (0, 0), (width, width)))


def pair_index(first, second):
    low, high = (min(first, second), max(first, second))
    return pair_list.index((low, high))


def diffusion_tensor(parts):
    entry = {}
    for index in range(6):
        entry[pair_list[index]] = parts[index]
    ones = jnp.ones_like(parts[0])
    zeros = jnp.zeros_like(parts[0])
    basis = [[ones if row == col else zeros for col in range(3)] for row in range(3)]
    for sweep in range(SWEEPS):
        for first, second in ((0, 1), (0, 2), (1, 2)):
            third = 3 - first - second
            offdiag = entry[first, second]
            spread = entry[second, second] - entry[first, first]
            radius = jnp.sqrt(spread * spread + 4.0 * offdiag * offdiag + 1e-30)
            sign_part = jnp.where(spread >= 0.0, 1.0, -1.0)
            tangent = sign_part * 2.0 * offdiag / (jnp.abs(spread) + radius)
            cosine = 1.0 / jnp.sqrt(1.0 + tangent * tangent)
            sine = tangent * cosine
            entry[first, first] = entry[first, first] - tangent * offdiag
            entry[second, second] = entry[second, second] + tangent * offdiag
            entry[first, second] = zeros
            key_first = (min(third, first), max(third, first))
            key_second = (min(third, second), max(third, second))
            old_first = entry[key_first]
            old_second = entry[key_second]
            entry[key_first] = cosine * old_first - sine * old_second
            entry[key_second] = sine * old_first + cosine * old_second
            for row in range(3):
                left = basis[row][first]
                right = basis[row][second]
                basis[row][first] = cosine * left - sine * right
                basis[row][second] = sine * left + cosine * right
    eigen = [entry[0, 0], entry[1, 1], entry[2, 2]]
    top = jnp.maximum(jnp.maximum(eigen[0], eigen[1]), eigen[2])
    trace = eigen[0] + eigen[1] + eigen[2]
    gains = []
    for index in range(3):
        gap = top - eigen[index]
        gains.append(
            alpha_floor
            + (1.0 - alpha_floor) * gap * gap / (gap * gap + contrast * trace * trace + 1e-30)
        )
    result = []
    for first, second in pair_list:
        total = gains[0] * basis[first][0] * basis[second][0]
        total = total + gains[1] * basis[first][1] * basis[second][1]
        total = total + gains[2] * basis[first][2] * basis[second][2]
        result.append(total)
    return result


def inside_mask(shape, z_start, y_start, z_total, y_total):
    z = lax.broadcasted_iota(jnp.int32, shape, 0) + z_start
    y = lax.broadcasted_iota(jnp.int32, shape, 1) + y_start
    return (z >= 0) & (z < z_total) & (y >= 0) & (y < y_total)


def regroup(sections, halo):
    n_xy = lax.axis_size("xy")
    n_gz = lax.axis_size("gz")
    z_in, y_total, x_in = sections.shape
    y_block = y_total // n_xy
    z_total = z_in * n_xy
    z_block = z_total // n_gz
    grouped = sections.reshape(z_in, n_xy, y_block, x_in)
    if y_block > 2 * halo:
        row_sets = [
            jnp.concatenate([grouped[:, :, :halo], grouped[:, :, y_block - halo :]], axis=2),
            grouped[:, :, halo : y_block - halo],
        ]
    else:
        row_sets = [grouped]
    parts = []
    for rows in row_sets:
        piece = rows.reshape(z_in, -1, x_in)
        column = lax.all_to_all(piece, "xy", split_axis=1, concat_axis=0, tiled=True)
        padded = jnp.pad(column, ((halo, halo), (0, 0), (0, 0)))
        windows = jnp.stack(
            [lax.slice_in_dim(padded, b * z_block, b * z_block + z_block + 2 * halo, axis=0) for b in range(n_gz)]
        )
        got = lax.all_to_all(windows, "gz", split_axis=0, concat_axis=0, tiled=True)
        got = jnp.transpose(got, (1, 2, 0, 3))
        parts.append(got.reshape(got.shape[:2] + (-1,)))
    edges = parts[0]
    forward = [(i, i + 1) for i in range(n_xy - 1)]
    backward = [(target, source) for source, target in forward]
    low = lax.ppermute(edges[:, edges.shape[1] - halo :], "xy", forward)
    high = lax.ppermute(edges[:, :halo], "xy", backward)
    if len(parts) > 1:
        middle = [edges[:, :halo], parts[1], edges[:, halo:]]
    else:
        middle = [edges]
    volume = jnp.concatenate([low] + middle + [high], axis=1)
    return lax.optimization_barrier(volume), z_total, y_total, z_block, y_block


def tensor_halo(tensor, width):
    z_block = tensor[0].shape[0]
    if z_block < 2 * width + 1:
        return surround(jnp.stack(diffusion_tensor(tensor)), width)
    edges = jnp.stack(
        diffusion_tensor([jnp.concatenate([item[:width], item[z_block - width :]], axis=0) for item in tensor])
    )
    top, bottom = lax.optimization_barrier((edges[:, width:], edges[:, :width]))
    z_low, z_high = z_faces(top, bottom)
    middle = jnp.stack(diffusion_tensor([item[width : z_block - width] for item in tensor]))
    block = jnp.concatenate([bottom, middle, top], axis=1)
    return assemble(block, z_low, z_high, width)


def z_faces(top, bottom):
    count = lax.axis_size("gz")
    forward = [(i, i + 1) for i in range(count - 1)]
    backward = [(target, source) for source, target in forward]
    return lax.ppermute(top, "gz", forward), lax.ppermute(bottom, "gz", backward)


def shifts(values, axis, dim, width):
    count = lax.axis_size(axis)
    forward = [(i, i + 1) for i in range(count - 1)]
    backward = [(target, source) for source, target in forward]
    size = values.shape[dim]
    low = lax.ppermute(lax.slice_in_dim(values, size - width, None, axis=dim), axis, forward)
    high = lax.ppermute(lax.slice_in_dim(values, 0, width, axis=dim), axis, backward)
    return low, high


def assemble(block, z_low, z_high, width):
    y_low, y_high = shifts(block, "xy", 2, width)
    faces = jnp.concatenate([z_low, z_high], axis=1)
    corner_low, corner_high = shifts(faces, "xy", 2, width)
    rows = [
        jnp.concatenate([corner_low[:, :width], z_low, corner_high[:, :width]], axis=2),
        jnp.concatenate([y_low, block, y_high], axis=2),
        jnp.concatenate([corner_low[:, width:], z_high, corner_high[:, width:]], axis=2),
    ]
    return jnp.concatenate(rows, axis=1)


def surround(block, width):
    z_block = block.shape[1]
    z_low, z_high = z_faces(block[:, z_block - width :], block[:, :width])
    return assemble(block, z_low, z_high, width)


def shards(sections):
    halo = VOLUME_HALO
    volume, z_total, y_total, z_block, y_block = regroup(sections, halo)
    z0 = lax.axis_index("gz") * z_block
    y0 = lax.axis_index("xy") * y_block

    smooth = gauss_taps(sigma_noise, GRAD_REACH)
    slope = slope_taps(sigma_noise, GRAD_REACH)
    wide = gauss_taps(sigma_tensor, TENSOR_REACH)

    grads = []
    for component in range(3):
        values = volume
        for along in range(2):
            taps = slope if along == component else smooth
            values = correlate(values, taps, along)
        taps = slope if component == 2 else smooth
        values = correlate(pad_x(values, GRAD_REACH), taps, 2)
        grads.append(values)
    grad_ext = halo - GRAD_REACH
    inside = inside_mask(grads[0].shape, z0 - grad_ext, y0 - grad_ext, z_total, y_total)
    products = jnp.stack(
        [jnp.where(inside, grads[first] * grads[second], 0.0) for first, second in pair_list]
    )
    for along in (1, 2):
        products = lax.slice_in_dim(
            products, grad_ext - TENSOR_REACH, products.shape[along] - grad_ext + TENSOR_REACH, axis=along
        )
    products = correlate(products, wide, 1)
    products = correlate(products, wide, 2)
    products = correlate(jnp.pad(products, ((0, 0), (0, 0), (0, 0), (TENSOR_REACH, TENSOR_REACH))), wide, 3)
    tensor = [products[index] for index in range(6)]
    stacked = tensor_halo(lax.optimization_barrier(tensor), TENSOR_HALO)

    reach = 2 * STEPS
    field = volume[halo - reach : volume.shape[0] - halo + reach, halo - reach : volume.shape[1] - halo + reach]
    for segment in range(STEPS):
        ext = reach - 2 * segment
        cut = TENSOR_HALO - (ext - 1)
        local = [
            stacked[index, cut : stacked.shape[1] - cut, cut : stacked.shape[2] - cut]
            for index in range(6)
        ]
        wide_field = pad_x(field, 1)
        slopes = [
            (wide_field[2:, 1:-1, 1:-1] - wide_field[:-2, 1:-1, 1:-1]) * 0.5,
            (wide_field[1:-1, 2:, 1:-1] - wide_field[1:-1, :-2, 1:-1]) * 0.5,
            (wide_field[1:-1, 1:-1, 2:] - wide_field[1:-1, 1:-1, :-2]) * 0.5,
        ]
        fluxes = []
        for along in range(3):
            flux = local[pair_index(along, 0)] * slopes[0]
            flux = flux + local[pair_index(along, 1)] * slopes[1]
            flux = flux + local[pair_index(along, 2)] * slopes[2]
            fluxes.append(flux)
        flux_x = pad_x(fluxes[2], 1)
        total = (fluxes[0][2:, 1:-1] - fluxes[0][:-2, 1:-1]) * 0.5
        total = total + (fluxes[1][1:-1, 2:] - fluxes[1][1:-1, :-2]) * 0.5
        total = total + (flux_x[1:-1, 1:-1, 2:] - flux_x[1:-1, 1:-1, :-2]) * 0.5
        field = field[2:-2, 2:-2] + time_step * total
        if segment < STEPS - 1:
            new_ext = ext - 2
            inside = inside_mask(field.shape, z0 - new_ext, y0 - new_ext, z_total, y_total)
            field = jnp.where(inside, field, 0.0)
    return field


def solution(mesh):
    in_specs = (P("xy", None, "gz"),)
    out_specs = P("gz", "xy", None)
    return jax.shard_map(shards, mesh=mesh, in_specs=in_specs, out_specs=out_specs, check_vma=False)
```

```python
import math

import jax
import jax.numpy as jnp
from jax import lax
from jax.sharding import PartitionSpec as P

GRAD_REACH = 3
TENSOR_REACH = 4
SWEEPS = 4
STEPS = 3


sigma_noise = 1.0
sigma_tensor = 1.5
alpha_floor = 0.05
contrast = 0.05
time_step = 0.5
pair_list = ((0, 0), (1, 1), (2, 2), (0, 1), (0, 2), (1, 2))

VOLUME_HALO = max(GRAD_REACH + TENSOR_REACH, 2 * STEPS)
TENSOR_HALO = 2 * STEPS - 1


def extended_2(block, sides, width):
    for axis, dim in sides:
        count = lax.axis_size(axis)
        forward = [(i, i + 1) for i in range(count - 1)]
        backward = [(target, source) for source, target in forward]
        low = lax.ppermute(
            lax.slice_in_dim(block, block.shape[dim] - width, None, axis=dim), axis, forward
        )
        high = lax.ppermute(lax.slice_in_dim(block, 0, width, axis=dim), axis, backward)
        block = jnp.concatenate([low, block, high], axis=dim)
    return block


def gauss_taps(sigma, reach):
    raw = [math.exp(-(t * t) / (2.0 * sigma * sigma)) for t in range(-reach, reach + 1)]
    total = sum(raw)
    return [value / total for value in raw]


def slope_taps(sigma, reach):
    base = gauss_taps(sigma, reach)
    return [t * base[t + reach] / (sigma * sigma) for t in range(-reach, reach + 1)]


def correlate(values, taps, along):
    count = values.shape[along] - len(taps) + 1
    result = taps[0] * lax.slice_in_dim(values, 0, count, axis=along)
    for index in range(1, len(taps)):
        result = result + taps[index] * lax.slice_in_dim(values, index, index + count, axis=along)
    return result


def pad_x(values, width):
    return jnp.pad(values, ((0, 0), (0, 0), (width, width)))


def pair_index(first, second):
    low, high = (min(first, second), max(first, second))
    return pair_list.index((low, high))


def diffusion_tensor(parts):
    entry = {}
    for index in range(6):
        entry[pair_list[index]] = parts[index]
    ones = jnp.ones_like(parts[0])
    zeros = jnp.zeros_like(parts[0])
    basis = [[ones if row == col else zeros for col in range(3)] for row in range(3)]
    for sweep in range(SWEEPS):
        for first, second in ((0, 1), (0, 2), (1, 2)):
            third = 3 - first - second
            offdiag = entry[first, second]
            spread = entry[second, second] - entry[first, first]
            radius = jnp.sqrt(spread * spread + 4.0 * offdiag * offdiag + 1e-30)
            sign_part = jnp.where(spread >= 0.0, 1.0, -1.0)
            tangent = sign_part * 2.0 * offdiag / (jnp.abs(spread) + radius)
            cosine = 1.0 / jnp.sqrt(1.0 + tangent * tangent)
            sine = tangent * cosine
            entry[first, first] = entry[first, first] - tangent * offdiag
            entry[second, second] = entry[second, second] + tangent * offdiag
            entry[first, second] = zeros
            key_first = (min(third, first), max(third, first))
            key_second = (min(third, second), max(third, second))
            old_first = entry[key_first]
            old_second = entry[key_second]
            entry[key_first] = cosine * old_first - sine * old_second
            entry[key_second] = sine * old_first + cosine * old_second
            for row in range(3):
                left = basis[row][first]
                right = basis[row][second]
                basis[row][first] = cosine * left - sine * right
                basis[row][second] = sine * left + cosine * right
    eigen = [entry[0, 0], entry[1, 1], entry[2, 2]]
    top = jnp.maximum(jnp.maximum(eigen[0], eigen[1]), eigen[2])
    trace = eigen[0] + eigen[1] + eigen[2]
    gains = []
    for index in range(3):
        gap = top - eigen[index]
        gains.append(
            alpha_floor
            + (1.0 - alpha_floor) * gap * gap / (gap * gap + contrast * trace * trace + 1e-30)
        )
    result = []
    for first, second in pair_list:
        total = gains[0] * basis[first][0] * basis[second][0]
        total = total + gains[1] * basis[first][1] * basis[second][1]
        total = total + gains[2] * basis[first][2] * basis[second][2]
        result.append(total)
    return result


def inside_mask(shape, z_start, y_start, z_total, y_total):
    z = lax.broadcasted_iota(jnp.int32, shape, 0) + z_start
    y = lax.broadcasted_iota(jnp.int32, shape, 1) + y_start
    return (z >= 0) & (z < z_total) & (y >= 0) & (y < y_total)


def regroup(sections, halo):
    n_xy = lax.axis_size("xy")
    n_gz = lax.axis_size("gz")
    z_in, y_total, x_in = sections.shape
    y_block = y_total // n_xy
    z_total = z_in * n_xy
    z_block = z_total // n_gz
    grouped = sections.reshape(z_in, n_xy, y_block, x_in)
    if y_block > 2 * halo:
        row_sets = [
            jnp.concatenate([grouped[:, :, :halo], grouped[:, :, y_block - halo :]], axis=2),
            grouped[:, :, halo : y_block - halo],
        ]
    else:
        row_sets = [grouped]
    parts = []
    for rows in row_sets:
        piece = rows.reshape(z_in, -1, x_in)
        column = lax.all_to_all(piece, "xy", split_axis=1, concat_axis=0, tiled=True)
        padded = jnp.pad(column, ((halo, halo), (0, 0), (0, 0)))
        windows = jnp.stack(
            [lax.slice_in_dim(padded, b * z_block, b * z_block + z_block + 2 * halo, axis=0) for b in range(n_gz)]
        )
        got = lax.all_to_all(windows, "gz", split_axis=0, concat_axis=0, tiled=True)
        got = jnp.transpose(got, (1, 2, 0, 3))
        parts.append(got.reshape(got.shape[:2] + (-1,)))
    edges = parts[0]
    forward = [(i, i + 1) for i in range(n_xy - 1)]
    backward = [(target, source) for source, target in forward]
    low = lax.ppermute(edges[:, edges.shape[1] - halo :], "xy", forward)
    high = lax.ppermute(edges[:, :halo], "xy", backward)
    if len(parts) > 1:
        middle = [edges[:, :halo], parts[1], edges[:, halo:]]
    else:
        middle = [edges]
    volume = jnp.concatenate([low] + middle + [high], axis=1)
    return lax.optimization_barrier(volume), z_total, y_total, z_block, y_block


def tensor_halo(tensor, width):
    z_block = tensor[0].shape[0]
    if z_block < 2 * width + 1:
        return surround(jnp.stack(diffusion_tensor(tensor)), width)
    edges = jnp.stack(
        diffusion_tensor([jnp.concatenate([item[:width], item[z_block - width :]], axis=0) for item in tensor])
    )
    top, bottom = lax.optimization_barrier((edges[:, width:], edges[:, :width]))
    z_low, z_high = packed_z_faces(top, bottom)
    middle = jnp.stack(diffusion_tensor([item[width : z_block - width] for item in tensor]))
    block = jnp.concatenate([bottom, middle, top], axis=1)
    return assemble(block, z_low, z_high, width)


def packed_z_faces(top, bottom):
    fields, rows = top.shape[0], top.shape[1]
    full = sorted({pair_index(0, other) for other in range(3)})
    short = [index for index in range(fields) if index not in full]
    tail = top.shape[2:]

    def pack(face, keep):
        return jnp.concatenate(
            [jnp.stack([face[index] for index in full]).reshape((-1,) + tail),
             jnp.stack([face[index, keep] for index in short]).reshape((-1,) + tail)],
            axis=0,
        )

    def unpack(got, pad):
        whole = got[: len(full) * rows].reshape((len(full), rows) + tail)
        cut = got[len(full) * rows :].reshape((len(short), rows - 1) + tail)
        cut = jnp.pad(cut, ((0, 0), pad, (0, 0), (0, 0)))
        pieces = {}
        for place, index in enumerate(full):
            pieces[index] = whole[place]
        for place, index in enumerate(short):
            pieces[index] = cut[place]
        return jnp.stack([pieces[index] for index in range(fields)])

    low, high = z_faces(pack(top, slice(1, None)), pack(bottom, slice(0, rows - 1)))
    return unpack(low, (1, 0)), unpack(high, (0, 1))


def z_faces(top, bottom):
    count = lax.axis_size("gz")
    forward = [(i, i + 1) for i in range(count - 1)]
    backward = [(target, source) for source, target in forward]
    return lax.ppermute(top, "gz", forward), lax.ppermute(bottom, "gz", backward)


def shifts(values, axis, dim, width):
    count = lax.axis_size(axis)
    forward = [(i, i + 1) for i in range(count - 1)]
    backward = [(target, source) for source, target in forward]
    size = values.shape[dim]
    low = lax.ppermute(lax.slice_in_dim(values, size - width, None, axis=dim), axis, forward)
    high = lax.ppermute(lax.slice_in_dim(values, 0, width, axis=dim), axis, backward)
    return low, high


def assemble(block, z_low, z_high, width):
    y_low, y_high = shifts(block, "xy", 2, width)
    faces = jnp.concatenate([z_low, z_high], axis=1)
    corner_low, corner_high = shifts(faces, "xy", 2, width)
    rows = [
        jnp.concatenate([corner_low[:, :width], z_low, corner_high[:, :width]], axis=2),
        jnp.concatenate([y_low, block, y_high], axis=2),
        jnp.concatenate([corner_low[:, width:], z_high, corner_high[:, width:]], axis=2),
    ]
    return jnp.concatenate(rows, axis=1)


def surround(block, width):
    z_block = block.shape[1]
    z_low, z_high = z_faces(block[:, z_block - width :], block[:, :width])
    return assemble(block, z_low, z_high, width)


def shards(sections):
    halo = VOLUME_HALO
    volume, z_total, y_total, z_block, y_block = regroup(sections, halo)
    z0 = lax.axis_index("gz") * z_block
    y0 = lax.axis_index("xy") * y_block

    smooth = gauss_taps(sigma_noise, GRAD_REACH)
    slope = slope_taps(sigma_noise, GRAD_REACH)
    wide = gauss_taps(sigma_tensor, TENSOR_REACH)

    grads = []
    for component in range(3):
        values = volume
        for along in range(2):
            taps = slope if along == component else smooth
            values = correlate(values, taps, along)
        taps = slope if component == 2 else smooth
        values = correlate(pad_x(values, GRAD_REACH), taps, 2)
        grads.append(values)
    grad_ext = halo - GRAD_REACH
    inside = inside_mask(grads[0].shape, z0 - grad_ext, y0 - grad_ext, z_total, y_total)
    tensor = []
    for first, second in pair_list:
        values = jnp.where(inside, grads[first] * grads[second], 0.0)
        values = lax.slice_in_dim(values, grad_ext - TENSOR_REACH, values.shape[0] - grad_ext + TENSOR_REACH, axis=0)
        values = lax.slice_in_dim(values, grad_ext - TENSOR_REACH, values.shape[1] - grad_ext + TENSOR_REACH, axis=1)
        values = correlate(values, wide, 0)
        values = correlate(values, wide, 1)
        values = correlate(pad_x(values, TENSOR_REACH), wide, 2)
        tensor.append(values)
    stacked = tensor_halo(lax.optimization_barrier(tensor), TENSOR_HALO)

    reach = 2 * STEPS
    field = volume[halo - reach : volume.shape[0] - halo + reach, halo - reach : volume.shape[1] - halo + reach]
    for segment in range(STEPS):
        ext = reach - 2 * segment
        cut = TENSOR_HALO - (ext - 1)
        local = [
            stacked[index, cut : stacked.shape[1] - cut, cut : stacked.shape[2] - cut]
            for index in range(6)
        ]
        wide_field = pad_x(field, 1)
        slopes = [
            (wide_field[2:, 1:-1, 1:-1] - wide_field[:-2, 1:-1, 1:-1]) * 0.5,
            (wide_field[1:-1, 2:, 1:-1] - wide_field[1:-1, :-2, 1:-1]) * 0.5,
            (wide_field[1:-1, 1:-1, 2:] - wide_field[1:-1, 1:-1, :-2]) * 0.5,
        ]
        fluxes = []
        for along in range(3):
            flux = local[pair_index(along, 0)] * slopes[0]
            flux = flux + local[pair_index(along, 1)] * slopes[1]
            flux = flux + local[pair_index(along, 2)] * slopes[2]
            fluxes.append(flux)
        flux_x = pad_x(fluxes[2], 1)
        total = (fluxes[0][2:, 1:-1] - fluxes[0][:-2, 1:-1]) * 0.5
        total = total + (fluxes[1][1:-1, 2:] - fluxes[1][1:-1, :-2]) * 0.5
        total = total + (flux_x[1:-1, 1:-1, 2:] - flux_x[1:-1, 1:-1, :-2]) * 0.5
        field = field[2:-2, 2:-2] + time_step * total
        if segment < STEPS - 1:
            new_ext = ext - 2
            inside = inside_mask(field.shape, z0 - new_ext, y0 - new_ext, z_total, y_total)
            field = jnp.where(inside, field, 0.0)
    return field


def solution(mesh):
    in_specs = (P("xy", None, "gz"),)
    out_specs = P("gz", "xy", None)
    return jax.shard_map(shards, mesh=mesh, in_specs=in_specs, out_specs=out_specs, check_vma=False)
```

```python
import math

import jax
import jax.numpy as jnp
from jax import lax
from jax.sharding import PartitionSpec as P

GRAD_REACH = 3
TENSOR_REACH = 4
SWEEPS = 4
STEPS = 3


sigma_noise = 1.0
sigma_tensor = 1.5
alpha_floor = 0.05
contrast = 0.05
time_step = 0.5
pair_list = ((0, 0), (1, 1), (2, 2), (0, 1), (0, 2), (1, 2))

VOLUME_HALO = max(GRAD_REACH + TENSOR_REACH, 2 * STEPS)
TENSOR_HALO = 2 * STEPS - 1


def extended_2(block, sides, width):
    for axis, dim in sides:
        count = lax.axis_size(axis)
        forward = [(i, i + 1) for i in range(count - 1)]
        backward = [(target, source) for source, target in forward]
        low = lax.ppermute(
            lax.slice_in_dim(block, block.shape[dim] - width, None, axis=dim), axis, forward
        )
        high = lax.ppermute(lax.slice_in_dim(block, 0, width, axis=dim), axis, backward)
        block = jnp.concatenate([low, block, high], axis=dim)
    return block


def gauss_taps(sigma, reach):
    raw = [math.exp(-(t * t) / (2.0 * sigma * sigma)) for t in range(-reach, reach + 1)]
    total = sum(raw)
    return [value / total for value in raw]


def slope_taps(sigma, reach):
    base = gauss_taps(sigma, reach)
    return [t * base[t + reach] / (sigma * sigma) for t in range(-reach, reach + 1)]


def correlate(values, taps, along):
    count = values.shape[along] - len(taps) + 1
    result = taps[0] * lax.slice_in_dim(values, 0, count, axis=along)
    for index in range(1, len(taps)):
        result = result + taps[index] * lax.slice_in_dim(values, index, index + count, axis=along)
    return result


def pad_x(values, width):
    return jnp.pad(values, ((0, 0), (0, 0), (width, width)))


def pair_index(first, second):
    low, high = (min(first, second), max(first, second))
    return pair_list.index((low, high))


def diffusion_tensor(parts):
    entry = {}
    for index in range(6):
        entry[pair_list[index]] = parts[index]
    ones = jnp.ones_like(parts[0])
    zeros = jnp.zeros_like(parts[0])
    basis = [[ones if row == col else zeros for col in range(3)] for row in range(3)]
    for sweep in range(SWEEPS):
        for first, second in ((0, 1), (0, 2), (1, 2)):
            third = 3 - first - second
            offdiag = entry[first, second]
            spread = entry[second, second] - entry[first, first]
            radius = jnp.sqrt(spread * spread + 4.0 * offdiag * offdiag + 1e-30)
            sign_part = jnp.where(spread >= 0.0, 1.0, -1.0)
            tangent = sign_part * 2.0 * offdiag / (jnp.abs(spread) + radius)
            cosine = 1.0 / jnp.sqrt(1.0 + tangent * tangent)
            sine = tangent * cosine
            entry[first, first] = entry[first, first] - tangent * offdiag
            entry[second, second] = entry[second, second] + tangent * offdiag
            entry[first, second] = zeros
            key_first = (min(third, first), max(third, first))
            key_second = (min(third, second), max(third, second))
            old_first = entry[key_first]
            old_second = entry[key_second]
            entry[key_first] = cosine * old_first - sine * old_second
            entry[key_second] = sine * old_first + cosine * old_second
            for row in range(3):
                left = basis[row][first]
                right = basis[row][second]
                basis[row][first] = cosine * left - sine * right
                basis[row][second] = sine * left + cosine * right
    eigen = [entry[0, 0], entry[1, 1], entry[2, 2]]
    top = jnp.maximum(jnp.maximum(eigen[0], eigen[1]), eigen[2])
    trace = eigen[0] + eigen[1] + eigen[2]
    gains = []
    for index in range(3):
        gap = top - eigen[index]
        gains.append(
            alpha_floor
            + (1.0 - alpha_floor) * gap * gap / (gap * gap + contrast * trace * trace + 1e-30)
        )
    result = []
    for first, second in pair_list:
        total = gains[0] * basis[first][0] * basis[second][0]
        total = total + gains[1] * basis[first][1] * basis[second][1]
        total = total + gains[2] * basis[first][2] * basis[second][2]
        result.append(total)
    return result


def inside_mask(shape, z_start, y_start, z_total, y_total):
    z = lax.broadcasted_iota(jnp.int32, shape, 0) + z_start
    y = lax.broadcasted_iota(jnp.int32, shape, 1) + y_start
    return (z >= 0) & (z < z_total) & (y >= 0) & (y < y_total)


def regroup(sections, halo):
    n_xy = lax.axis_size("xy")
    n_gz = lax.axis_size("gz")
    z_in, y_total, x_in = sections.shape
    y_block = y_total // n_xy
    z_total = z_in * n_xy
    z_block = z_total // n_gz
    grouped = sections.reshape(z_in, n_xy, y_block, x_in)
    if y_block > 2 * halo:
        row_sets = [
            jnp.concatenate([grouped[:, :, :halo], grouped[:, :, y_block - halo :]], axis=2),
            grouped[:, :, halo : y_block - halo],
        ]
    else:
        row_sets = [grouped]
    parts = []
    for rows in row_sets:
        piece = rows.reshape(z_in, -1, x_in)
        column = lax.all_to_all(piece, "xy", split_axis=1, concat_axis=0, tiled=True)
        padded = jnp.pad(column, ((halo, halo), (0, 0), (0, 0)))
        windows = jnp.stack(
            [lax.slice_in_dim(padded, b * z_block, b * z_block + z_block + 2 * halo, axis=0) for b in range(n_gz)]
        )
        got = lax.all_to_all(windows, "gz", split_axis=0, concat_axis=0, tiled=True)
        got = jnp.transpose(got, (1, 2, 0, 3))
        parts.append(got.reshape(got.shape[:2] + (-1,)))
    edges = parts[0]
    forward = [(i, i + 1) for i in range(n_xy - 1)]
    backward = [(target, source) for source, target in forward]
    low = lax.ppermute(edges[:, edges.shape[1] - halo :], "xy", forward)
    high = lax.ppermute(edges[:, :halo], "xy", backward)
    if len(parts) > 1:
        middle = [edges[:, :halo], parts[1], edges[:, halo:]]
    else:
        middle = [edges]
    volume = jnp.concatenate([low] + middle + [high], axis=1)
    return lax.optimization_barrier(volume), z_total, y_total, z_block, y_block


def tensor_halo(tensor, width):
    z_block = tensor[0].shape[0]
    if z_block < 2 * width + 1:
        return surround(jnp.stack(diffusion_tensor(tensor)), width)
    edges = jnp.stack(
        diffusion_tensor([jnp.concatenate([item[:width], item[z_block - width :]], axis=0) for item in tensor])
    )
    top, bottom = lax.optimization_barrier((edges[:, width:], edges[:, :width]))
    z_low, z_high = z_faces(top, bottom)
    middle = jnp.stack(diffusion_tensor([item[width : z_block - width] for item in tensor]))
    block = jnp.concatenate([bottom, middle, top], axis=1)
    return assemble(block, z_low, z_high, width)


def z_faces(top, bottom):
    count = lax.axis_size("gz")
    forward = [(i, i + 1) for i in range(count - 1)]
    backward = [(target, source) for source, target in forward]
    return lax.ppermute(top, "gz", forward), lax.ppermute(bottom, "gz", backward)


def shifts(values, axis, dim, width):
    count = lax.axis_size(axis)
    forward = [(i, i + 1) for i in range(count - 1)]
    backward = [(target, source) for source, target in forward]
    size = values.shape[dim]
    low = lax.ppermute(lax.slice_in_dim(values, size - width, None, axis=dim), axis, forward)
    high = lax.ppermute(lax.slice_in_dim(values, 0, width, axis=dim), axis, backward)
    return low, high


def assemble(block, z_low, z_high, width):
    y_low, y_high = shifts(block, "xy", 2, width)
    faces = jnp.concatenate([z_low, z_high], axis=1)
    corner_low, corner_high = shifts(faces, "xy", 2, width)
    return [
        [corner_low[:, :width], z_low, corner_high[:, :width]],
        [y_low, block, y_high],
        [corner_low[:, width:], z_high, corner_high[:, width:]],
    ]


def window(grid, index, cut, width):
    near = [slice(cut, None), slice(None), slice(0, width - cut)]
    return jnp.concatenate(
        [
            jnp.concatenate([grid[r][c][index, near[r], near[c]] for c in range(3)], axis=1)
            for r in range(3)
        ],
        axis=0,
    )


def surround(block, width):
    z_block = block.shape[1]
    z_low, z_high = z_faces(block[:, z_block - width :], block[:, :width])
    return assemble(block, z_low, z_high, width)


def shards(sections):
    halo = VOLUME_HALO
    volume, z_total, y_total, z_block, y_block = regroup(sections, halo)
    z0 = lax.axis_index("gz") * z_block
    y0 = lax.axis_index("xy") * y_block

    smooth = gauss_taps(sigma_noise, GRAD_REACH)
    slope = slope_taps(sigma_noise, GRAD_REACH)
    wide = gauss_taps(sigma_tensor, TENSOR_REACH)

    grads = []
    for component in range(3):
        values = volume
        for along in range(2):
            taps = slope if along == component else smooth
            values = correlate(values, taps, along)
        taps = slope if component == 2 else smooth
        values = correlate(pad_x(values, GRAD_REACH), taps, 2)
        grads.append(values)
    grad_ext = halo - GRAD_REACH
    inside = inside_mask(grads[0].shape, z0 - grad_ext, y0 - grad_ext, z_total, y_total)
    tensor = []
    for first, second in pair_list:
        values = jnp.where(inside, grads[first] * grads[second], 0.0)
        values = lax.slice_in_dim(values, grad_ext - TENSOR_REACH, values.shape[0] - grad_ext + TENSOR_REACH, axis=0)
        values = lax.slice_in_dim(values, grad_ext - TENSOR_REACH, values.shape[1] - grad_ext + TENSOR_REACH, axis=1)
        values = correlate(values, wide, 0)
        values = correlate(values, wide, 1)
        values = correlate(pad_x(values, TENSOR_REACH), wide, 2)
        tensor.append(values)
    stacked = tensor_halo(lax.optimization_barrier(tensor), TENSOR_HALO)

    reach = 2 * STEPS
    field = volume[halo - reach : volume.shape[0] - halo + reach, halo - reach : volume.shape[1] - halo + reach]
    for segment in range(STEPS):
        ext = reach - 2 * segment
        cut = TENSOR_HALO - (ext - 1)
        local = [window(stacked, index, cut, TENSOR_HALO) for index in range(6)]
        wide_field = pad_x(field, 1)
        slopes = [
            (wide_field[2:, 1:-1, 1:-1] - wide_field[:-2, 1:-1, 1:-1]) * 0.5,
            (wide_field[1:-1, 2:, 1:-1] - wide_field[1:-1, :-2, 1:-1]) * 0.5,
            (wide_field[1:-1, 1:-1, 2:] - wide_field[1:-1, 1:-1, :-2]) * 0.5,
        ]
        fluxes = []
        for along in range(3):
            flux = local[pair_index(along, 0)] * slopes[0]
            flux = flux + local[pair_index(along, 1)] * slopes[1]
            flux = flux + local[pair_index(along, 2)] * slopes[2]
            fluxes.append(flux)
        flux_x = pad_x(fluxes[2], 1)
        total = (fluxes[0][2:, 1:-1] - fluxes[0][:-2, 1:-1]) * 0.5
        total = total + (fluxes[1][1:-1, 2:] - fluxes[1][1:-1, :-2]) * 0.5
        total = total + (flux_x[1:-1, 1:-1, 2:] - flux_x[1:-1, 1:-1, :-2]) * 0.5
        field = field[2:-2, 2:-2] + time_step * total
        if segment < STEPS - 1:
            new_ext = ext - 2
            inside = inside_mask(field.shape, z0 - new_ext, y0 - new_ext, z_total, y_total)
            field = jnp.where(inside, field, 0.0)
    return field


def solution(mesh):
    in_specs = (P("xy", None, "gz"),)
    out_specs = P("gz", "xy", None)
    return jax.shard_map(shards, mesh=mesh, in_specs=in_specs, out_specs=out_specs, check_vma=False)
```

```python
import math

import jax
import jax.numpy as jnp
from jax import lax
from jax.sharding import PartitionSpec as P

GRAD_REACH = 3
TENSOR_REACH = 4
SWEEPS = 4
STEPS = 3


sigma_noise = 1.0
sigma_tensor = 1.5
alpha_floor = 0.05
contrast = 0.05
time_step = 0.5
pair_list = ((0, 0), (1, 1), (2, 2), (0, 1), (0, 2), (1, 2))

VOLUME_HALO = max(GRAD_REACH + TENSOR_REACH, 2 * STEPS)
TENSOR_HALO = 2 * STEPS - 1


def extended_2(block, sides, width):
    for axis, dim in sides:
        count = lax.axis_size(axis)
        forward = [(i, i + 1) for i in range(count - 1)]
        backward = [(target, source) for source, target in forward]
        low = lax.ppermute(
            lax.slice_in_dim(block, block.shape[dim] - width, None, axis=dim), axis, forward
        )
        high = lax.ppermute(lax.slice_in_dim(block, 0, width, axis=dim), axis, backward)
        block = jnp.concatenate([low, block, high], axis=dim)
    return block


def gauss_taps(sigma, reach):
    raw = [math.exp(-(t * t) / (2.0 * sigma * sigma)) for t in range(-reach, reach + 1)]
    total = sum(raw)
    return [value / total for value in raw]


def slope_taps(sigma, reach):
    base = gauss_taps(sigma, reach)
    return [t * base[t + reach] / (sigma * sigma) for t in range(-reach, reach + 1)]


def correlate(values, taps, along):
    count = values.shape[along] - len(taps) + 1
    result = taps[0] * lax.slice_in_dim(values, 0, count, axis=along)
    for index in range(1, len(taps)):
        result = result + taps[index] * lax.slice_in_dim(values, index, index + count, axis=along)
    return result


def pad_x(values, width):
    return jnp.pad(values, ((0, 0), (0, 0), (width, width)))


def pair_index(first, second):
    low, high = (min(first, second), max(first, second))
    return pair_list.index((low, high))


def diffusion_tensor(parts):
    entry = {}
    for index in range(6):
        entry[pair_list[index]] = parts[index]
    ones = jnp.ones_like(parts[0])
    zeros = jnp.zeros_like(parts[0])
    basis = [[ones if row == col else zeros for col in range(3)] for row in range(3)]
    for sweep in range(SWEEPS):
        for first, second in ((0, 1), (0, 2), (1, 2)):
            third = 3 - first - second
            offdiag = entry[first, second]
            spread = entry[second, second] - entry[first, first]
            radius = jnp.sqrt(spread * spread + 4.0 * offdiag * offdiag + 1e-30)
            sign_part = jnp.where(spread >= 0.0, 1.0, -1.0)
            tangent = sign_part * 2.0 * offdiag / (jnp.abs(spread) + radius)
            cosine = 1.0 / jnp.sqrt(1.0 + tangent * tangent)
            sine = tangent * cosine
            entry[first, first] = entry[first, first] - tangent * offdiag
            entry[second, second] = entry[second, second] + tangent * offdiag
            entry[first, second] = zeros
            key_first = (min(third, first), max(third, first))
            key_second = (min(third, second), max(third, second))
            old_first = entry[key_first]
            old_second = entry[key_second]
            entry[key_first] = cosine * old_first - sine * old_second
            entry[key_second] = sine * old_first + cosine * old_second
            for row in range(3):
                left = basis[row][first]
                right = basis[row][second]
                basis[row][first] = cosine * left - sine * right
                basis[row][second] = sine * left + cosine * right
    eigen = [entry[0, 0], entry[1, 1], entry[2, 2]]
    top = jnp.maximum(jnp.maximum(eigen[0], eigen[1]), eigen[2])
    trace = eigen[0] + eigen[1] + eigen[2]
    gains = []
    for index in range(3):
        gap = top - eigen[index]
        gains.append(
            alpha_floor
            + (1.0 - alpha_floor) * gap * gap / (gap * gap + contrast * trace * trace + 1e-30)
        )
    result = []
    for first, second in pair_list:
        total = gains[0] * basis[first][0] * basis[second][0]
        total = total + gains[1] * basis[first][1] * basis[second][1]
        total = total + gains[2] * basis[first][2] * basis[second][2]
        result.append(total)
    return result


def inside_mask(shape, z_start, y_start, z_total, y_total):
    z = lax.broadcasted_iota(jnp.int32, shape, 0) + z_start
    y = lax.broadcasted_iota(jnp.int32, shape, 1) + y_start
    return (z >= 0) & (z < z_total) & (y >= 0) & (y < y_total)


def regroup(sections, halo):
    n_xy = lax.axis_size("xy")
    n_gz = lax.axis_size("gz")
    z_in, y_total, x_in = sections.shape
    y_block = y_total // n_xy
    z_total = z_in * n_xy
    z_block = z_total // n_gz
    grouped = sections.reshape(z_in, n_xy, y_block, x_in)
    lead = halo + (y_block - 2 * halo) // 4
    if y_block > 2 * lead:
        row_sets = [
            jnp.concatenate([grouped[:, :, :lead], grouped[:, :, y_block - lead :]], axis=2),
            grouped[:, :, lead : y_block - lead],
        ]
    else:
        row_sets = [grouped]
    parts = []
    for rows in row_sets:
        piece = rows.reshape(z_in, -1, x_in)
        column = lax.all_to_all(piece, "xy", split_axis=1, concat_axis=0, tiled=True)
        padded = jnp.pad(column, ((halo, halo), (0, 0), (0, 0)))
        windows = jnp.stack(
            [lax.slice_in_dim(padded, b * z_block, b * z_block + z_block + 2 * halo, axis=0) for b in range(n_gz)]
        )
        got = lax.all_to_all(windows, "gz", split_axis=0, concat_axis=0, tiled=True)
        got = jnp.transpose(got, (1, 2, 0, 3))
        parts.append(got.reshape(got.shape[:2] + (-1,)))
    edges = parts[0]
    forward = [(i, i + 1) for i in range(n_xy - 1)]
    backward = [(target, source) for source, target in forward]
    low = lax.ppermute(edges[:, edges.shape[1] - halo :], "xy", forward)
    high = lax.ppermute(edges[:, :halo], "xy", backward)
    if len(parts) > 1:
        middle = [edges[:, :lead], parts[1], edges[:, lead:]]
    else:
        middle = [edges]
    volume = jnp.concatenate([low] + middle + [high], axis=1)
    return lax.optimization_barrier(volume), z_total, y_total, z_block, y_block


def tensor_halo(tensor, width):
    z_block = tensor[0].shape[0]
    if z_block < 2 * width + 1:
        return surround(jnp.stack(diffusion_tensor(tensor)), width)
    edges = jnp.stack(
        diffusion_tensor([jnp.concatenate([item[:width], item[z_block - width :]], axis=0) for item in tensor])
    )
    top, bottom = lax.optimization_barrier((edges[:, width:], edges[:, :width]))
    z_low, z_high = z_faces(top, bottom)
    middle = jnp.stack(diffusion_tensor([item[width : z_block - width] for item in tensor]))
    block = jnp.concatenate([bottom, middle, top], axis=1)
    return assemble(block, z_low, z_high, width)


def z_faces(top, bottom):
    count = lax.axis_size("gz")
    forward = [(i, i + 1) for i in range(count - 1)]
    backward = [(target, source) for source, target in forward]
    return lax.ppermute(top, "gz", forward), lax.ppermute(bottom, "gz", backward)


def shifts(values, axis, dim, width):
    count = lax.axis_size(axis)
    forward = [(i, i + 1) for i in range(count - 1)]
    backward = [(target, source) for source, target in forward]
    size = values.shape[dim]
    low = lax.ppermute(lax.slice_in_dim(values, size - width, None, axis=dim), axis, forward)
    high = lax.ppermute(lax.slice_in_dim(values, 0, width, axis=dim), axis, backward)
    return low, high


def assemble(block, z_low, z_high, width):
    y_low, y_high = shifts(block, "xy", 2, width)
    faces = jnp.concatenate([z_low, z_high], axis=1)
    corner_low, corner_high = shifts(faces, "xy", 2, width)
    rows = [
        jnp.concatenate([corner_low[:, :width], z_low, corner_high[:, :width]], axis=2),
        jnp.concatenate([y_low, block, y_high], axis=2),
        jnp.concatenate([corner_low[:, width:], z_high, corner_high[:, width:]], axis=2),
    ]
    return jnp.concatenate(rows, axis=1)


def surround(block, width):
    z_block = block.shape[1]
    z_low, z_high = z_faces(block[:, z_block - width :], block[:, :width])
    return assemble(block, z_low, z_high, width)


def shards(sections):
    halo = VOLUME_HALO
    volume, z_total, y_total, z_block, y_block = regroup(sections, halo)
    z0 = lax.axis_index("gz") * z_block
    y0 = lax.axis_index("xy") * y_block

    smooth = gauss_taps(sigma_noise, GRAD_REACH)
    slope = slope_taps(sigma_noise, GRAD_REACH)
    wide = gauss_taps(sigma_tensor, TENSOR_REACH)

    grads = []
    for component in range(3):
        values = volume
        for along in range(2):
            taps = slope if along == component else smooth
            values = correlate(values, taps, along)
        taps = slope if component == 2 else smooth
        values = correlate(pad_x(values, GRAD_REACH), taps, 2)
        grads.append(values)
    grad_ext = halo - GRAD_REACH
    inside = inside_mask(grads[0].shape, z0 - grad_ext, y0 - grad_ext, z_total, y_total)
    tensor = []
    for first, second in pair_list:
        values = jnp.where(inside, grads[first] * grads[second], 0.0)
        values = lax.slice_in_dim(values, grad_ext - TENSOR_REACH, values.shape[0] - grad_ext + TENSOR_REACH, axis=0)
        values = lax.slice_in_dim(values, grad_ext - TENSOR_REACH, values.shape[1] - grad_ext + TENSOR_REACH, axis=1)
        values = correlate(values, wide, 0)
        values = correlate(values, wide, 1)
        values = correlate(pad_x(values, TENSOR_REACH), wide, 2)
        tensor.append(values)
    stacked = tensor_halo(lax.optimization_barrier(tensor), TENSOR_HALO)

    reach = 2 * STEPS
    field = volume[halo - reach : volume.shape[0] - halo + reach, halo - reach : volume.shape[1] - halo + reach]
    for segment in range(STEPS):
        ext = reach - 2 * segment
        cut = TENSOR_HALO - (ext - 1)
        local = [
            stacked[index, cut : stacked.shape[1] - cut, cut : stacked.shape[2] - cut]
            for index in range(6)
        ]
        wide_field = pad_x(field, 1)
        slopes = [
            (wide_field[2:, 1:-1, 1:-1] - wide_field[:-2, 1:-1, 1:-1]) * 0.5,
            (wide_field[1:-1, 2:, 1:-1] - wide_field[1:-1, :-2, 1:-1]) * 0.5,
            (wide_field[1:-1, 1:-1, 2:] - wide_field[1:-1, 1:-1, :-2]) * 0.5,
        ]
        fluxes = []
        for along in range(3):
            flux = local[pair_index(along, 0)] * slopes[0]
            flux = flux + local[pair_index(along, 1)] * slopes[1]
            flux = flux + local[pair_index(along, 2)] * slopes[2]
            fluxes.append(flux)
        flux_x = pad_x(fluxes[2], 1)
        total = (fluxes[0][2:, 1:-1] - fluxes[0][:-2, 1:-1]) * 0.5
        total = total + (fluxes[1][1:-1, 2:] - fluxes[1][1:-1, :-2]) * 0.5
        total = total + (flux_x[1:-1, 1:-1, 2:] - flux_x[1:-1, 1:-1, :-2]) * 0.5
        field = field[2:-2, 2:-2] + time_step * total
        if segment < STEPS - 1:
            new_ext = ext - 2
            inside = inside_mask(field.shape, z0 - new_ext, y0 - new_ext, z_total, y_total)
            field = jnp.where(inside, field, 0.0)
    return field


def solution(mesh):
    in_specs = (P("xy", None, "gz"),)
    out_specs = P("gz", "xy", None)
    return jax.shard_map(shards, mesh=mesh, in_specs=in_specs, out_specs=out_specs, check_vma=False)
```
